256 devices in a mesh: seq: 32 (over x, z), head: 8 (over y, core).
Axes of the slice: x: 4, y: 4, z: 8, core: 2. Of those that a mesh axis runs over, the one named last changes fastest.
Arguments:
- queries: bfloat16 [16384, 8192], P('seq', 'head'), may hold values from -48 to 48
- keys: bfloat16 [16384, 1024], P('seq', 'head'), may hold values from -48 to 48
- values: bfloat16 [16384, 1024], P('seq', 'head'), may hold values from -6 to 6
- offsets: int32 [64], P('seq'), may hold values from 0 to 24064, as said below
- query_map: bfloat16 [64, 128, 64], P('head'), may hold values from -0.5 to 0.5
- key_map: bfloat16 [64, 128, 64], P('head'), may hold values from -0.5 to 0.5
- window_logit: float32 [64], P('head'), may hold values from -2 to 6
Outputs:
- attn_rows: bfloat16 [16384, 8192], P(('seq', 'head'))
The draws below stay inside these ranges and needn't reach their ends.
Inputs may be any that keep to these rules, and one draw needn't show every extreme that they name: offsets[0] = 0, and each span's offset exceeds the one before by 256 or 512.
All inputs are finite; a program needn't handle non-finite values.
Results may differ from the reference program's by a relative error of at most 0.004.
The reference program's roundings to bfloat16 on the way (of `weights_b` and `affinity_b`) count: a program that leaves them out, or rounds other values in their place, can miss the bound.
Values may be sent and summed in bfloat16 or wider, within the bound.
No kernel may reach another device: no remote copies, remote signals or barrier semaphores. Data moves between devices by JAX's collectives and lax.ppermute only.
A program may use at most 128 MiB of HBM per device.

```python
import math
import jax
import jax.numpy as jnp
from jax import lax

HEADS = 64
KV_HEADS = 8
HEAD_DIM = 128
FEAT = 64
WINDOW = 64
BLOCK = 512
SPAN = 256
TOKENS = 16384
NCHUNK = 64


def span_offsets(key):
    count = NCHUNK - 1
    base = jnp.where(jnp.arange(count) < count // 2, SPAN, 0).astype(jnp.int32)
    gaps = jax.random.permutation(jax.random.fold_in(key, 31), base)
    gaps = jnp.concatenate([jnp.zeros((1,), jnp.int32), gaps])
    return (jnp.arange(NCHUNK, dtype=jnp.int32) * SPAN + jnp.cumsum(gaps)).astype(jnp.int32)


def draw_offsets(key, part):
    return span_offsets(key)


def rotate_rows(rows, positions):
    half = HEAD_DIM // 2
    frequency = 500000.0 ** (-jnp.arange(half, dtype=jnp.float32) / half)
    angle = positions.astype(jnp.float32)[:, None] * frequency[None, :]
    cos_rows = jnp.cos(angle)[:, None, :]
    sin_rows = jnp.sin(angle)[:, None, :]
    first = rows[..., :half]
    second = rows[..., half:]
    return jnp.concatenate([first * cos_rows - second * sin_rows, second * cos_rows + first * sin_rows], axis=-1)


def query_key_pair(key):
    key_means = 1.5 * jax.random.normal(jax.random.fold_in(key, 13), (TOKENS // BLOCK, KV_HEADS, HEAD_DIM), jnp.float32)
    key_means = jnp.repeat(key_means, BLOCK, axis=0)
    positions = (span_offsets(key)[:, None] + jnp.arange(SPAN, dtype=jnp.int32)[None, :]).reshape(TOKENS)
    queries = jnp.clip(3.0 * jax.random.normal(jax.random.fold_in(key, 11), (TOKENS, HEADS, HEAD_DIM), jnp.float32), -18.0, 18.0)
    keys = 5.0 * jax.random.normal(jax.random.fold_in(key, 12), (TOKENS, KV_HEADS, HEAD_DIM), jnp.float32)
    keys = jnp.clip(keys + key_means, -30.0, 30.0)
    base_keys = keys
    return (queries, keys, rotate_rows(base_keys, positions))


def draw_queries(key, part):
    queries, keys, linked = query_key_pair(key)
    return queries.reshape(TOKENS, HEADS * HEAD_DIM).astype(jnp.bfloat16)


def draw_keys(key, part):
    queries, keys, linked = query_key_pair(key)
    return keys.reshape(TOKENS, KV_HEADS * HEAD_DIM).astype(jnp.bfloat16)


def draw_values(key, part):
    queries, keys, linked = query_key_pair(key)
    value_means = 0.3 * jax.random.normal(jax.random.fold_in(key, 22), (TOKENS // BLOCK, KV_HEADS * HEAD_DIM), jnp.float32)
    value_means = jnp.repeat(value_means, BLOCK, axis=0)
    scatter = 0.5 * jax.random.normal(jax.random.fold_in(key, 21), (TOKENS, KV_HEADS * HEAD_DIM), jnp.float32)
    related = 0.12 * linked.reshape(TOKENS, KV_HEADS * HEAD_DIM)
    return jnp.clip(related + scatter + value_means, -6.0, 6.0).astype(jnp.bfloat16)


def block_scale(stream_key, shape, pieces, low, top_value):
    def one(dim, shards_of):
        heights = jax.random.uniform(jax.random.fold_in(jax.random.fold_in(stream_key, 6), dim), (shards_of,), jnp.float32, low / len(pieces), top_value / len(pieces))
        return jnp.repeat(jnp.exp(heights), shape[dim] // shards_of).reshape((-1,) + (1,) * (len(shape) - dim - 1))

    loudness = one(*pieces[0])
    for cut in pieces[1:]:
        loudness = loudness * one(*cut)
    return loudness


def gaussian(stream_key, shape, scale, limit, cuts=(), held_as=jnp.bfloat16):
    values = scale * jax.random.normal(stream_key, shape, jnp.float32)
    if cuts:
        values = values * block_scale(stream_key, shape, cuts, -0.22, 0.18)
    return jnp.clip(values, -limit, limit).astype(held_as)


def setup_inputs(seed: int = 0) -> dict:
    key_list = jax.random.split(jax.random.key(seed), 8)
    queries = draw_queries(jax.random.fold_in(key_list[7], 71), 0)
    keys = draw_keys(jax.random.fold_in(key_list[7], 71), 0)
    values = draw_values(jax.random.fold_in(key_list[7], 71), 0)
    offsets = draw_offsets(jax.random.fold_in(key_list[7], 71), 0)
    query_map = gaussian(key_list[4], (HEADS, HEAD_DIM, FEAT), HEAD_DIM ** -0.5, 0.5, ((0, 8),))
    key_map = gaussian(key_list[5], (HEADS, HEAD_DIM, FEAT), HEAD_DIM ** -0.5, 0.5, ((0, 8),))
    window_logit = jnp.clip(-2.0 + 8.0 * jax.random.uniform(key_list[6], (HEADS,), jnp.float32) ** block_scale(key_list[6], (HEADS,), ((0, 8),), -0.2, 0.2), -2.0, 6.0)
    return {"queries": queries, "keys": keys, "values": values, "offsets": offsets, "query_map": query_map, "key_map": key_map, "window_logit": window_logit}


def angle_tables(positions, half):
    frequency = [500000.0 ** (-float(order) / half) for order in range(half)]
    coarse = jnp.asarray([4096.0 * value % (2.0 * math.pi) for value in frequency], jnp.float32)
    medium = jnp.asarray([64.0 * value % (2.0 * math.pi) for value in frequency], jnp.float32)
    finest = jnp.asarray(frequency, jnp.float32)
    upper = (positions // 4096).astype(jnp.float32)[:, None] * coarse[None, :]
    middle = (positions // 64 % 64).astype(jnp.float32)[:, None] * medium[None, :]
    lower = (positions % 64).astype(jnp.float32)[:, None] * finest[None, :]
    cos_high = jnp.cos(upper) * jnp.cos(middle) - jnp.sin(upper) * jnp.sin(middle)
    sin_high = jnp.sin(upper) * jnp.cos(middle) + jnp.cos(upper) * jnp.sin(middle)
    cosine = cos_high * jnp.cos(lower) - sin_high * jnp.sin(lower)
    sine = sin_high * jnp.cos(lower) + cos_high * jnp.sin(lower)
    return (cosine, sine)

def rotate(rows, cosine, sine):
    half = rows.shape[-1] // 2
    first = rows[..., :half]
    second = rows[..., half:]
    cos_rows = cosine[:, None, :]
    sin_rows = sine[:, None, :]
    return jnp.concatenate([first * cos_rows - second * sin_rows, second * cos_rows + first * sin_rows], axis=-1)

def two_softmax(logits):
    return jnp.concatenate([jax.nn.softmax(logits, axis=-1), jax.nn.softmax(-logits, axis=-1)], axis=-1)

def reference(queries, keys, values, offsets, query_map, key_map, window_logit):
    group = HEADS // KV_HEADS
    extent = BLOCK + WINDOW
    positions = (offsets[:, None] + jnp.arange(SPAN, dtype=jnp.int32)[None, :]).reshape(TOKENS)
    cosine, sine = angle_tables(positions, HEAD_DIM // 2)
    rot_k = rotate(keys.reshape(TOKENS, KV_HEADS, HEAD_DIM).astype(jnp.float32), cosine, sine).astype(jnp.bfloat16)
    pad_keys = jnp.concatenate([jnp.zeros((WINDOW, KV_HEADS, HEAD_DIM), jnp.bfloat16), rot_k], axis=0)
    pad_values = jnp.concatenate([jnp.zeros((WINDOW, KV_HEADS, HEAD_DIM), jnp.bfloat16), values.reshape(TOKENS, KV_HEADS, HEAD_DIM)], axis=0)
    valid = jnp.arange(TOKENS + WINDOW) >= WINDOW
    factor = jax.nn.sigmoid(window_logit)
    row_index = jnp.arange(BLOCK)[:, None]
    col_index = jnp.arange(extent)[None, :]
    window_mask = (col_index > row_index) & (col_index <= row_index + WINDOW)
    linear_mask = col_index <= row_index
    query_weights = query_map.astype(jnp.float32)
    key_weights = key_map.astype(jnp.float32)

    def block_step(carry, block):
        state, norm = carry
        start = (block * BLOCK).astype(jnp.int32)
        query_rows = lax.dynamic_slice_in_dim(queries, start, BLOCK, 0).reshape(BLOCK, HEADS, HEAD_DIM)
        block_cos = lax.dynamic_slice_in_dim(cosine, start, BLOCK, 0)
        block_sin = lax.dynamic_slice_in_dim(sine, start, BLOCK, 0)
        rot_q = rotate(query_rows.astype(jnp.float32), block_cos, block_sin).astype(jnp.bfloat16)
        key_rows = lax.dynamic_slice_in_dim(pad_keys, start, extent, 0)
        value_rows = lax.dynamic_slice_in_dim(pad_values, start, extent, 0)
        live = lax.dynamic_slice_in_dim(valid, start, extent, 0)
        key_heads = jnp.repeat(key_rows, group, axis=1).astype(jnp.float32)
        value_heads = jnp.repeat(value_rows, group, axis=1).astype(jnp.float32)
        phi_q = two_softmax(jnp.einsum('ihd,hdf->ihf', rot_q.astype(jnp.float32), query_weights)).astype(jnp.bfloat16)
        phi_k = two_softmax(jnp.einsum('jhd,hdf->jhf', key_heads, key_weights))
        phi_k = jnp.where(live[:, None, None], phi_k, 0.0).astype(jnp.bfloat16)
        phi_qf = phi_q.astype(jnp.float32)
        phi_kf = phi_k.astype(jnp.float32)
        scores = jnp.einsum('ihd,jhd->hij', rot_q.astype(jnp.float32), key_heads) / math.sqrt(HEAD_DIM)
        near_window = window_mask & live[None, :]
        peak = lax.optimization_barrier(jnp.max(jnp.where(near_window, scores, -jnp.inf), axis=-1, keepdims=True))
        weights = jnp.where(near_window, jnp.exp(scores - peak), 0.0)
        window_sum = lax.optimization_barrier(jnp.sum(weights, axis=-1))
        weights_b = lax.optimization_barrier(weights.astype(jnp.bfloat16)).astype(jnp.float32)
        affinity = jnp.einsum('ihf,jhf->hij', phi_qf, phi_kf)
        affinity = jnp.where(linear_mask & live[None, :], affinity, 0.0)
        near_sum = lax.optimization_barrier(jnp.sum(affinity, axis=-1))
        affinity_b = lax.optimization_barrier(affinity.astype(jnp.bfloat16)).astype(jnp.float32)
        window_num = jnp.einsum('hij,jhd->ihd', weights_b, value_heads)
        near_num = jnp.einsum('hij,jhd->ihd', affinity_b, value_heads)
        far_num = jnp.einsum('ihf,hfd->ihd', phi_qf, state, precision=lax.Precision.HIGHEST)
        far_sum = jnp.einsum('ihf,hf->ih', phi_qf, norm, precision=lax.Precision.HIGHEST)
        head_factor = factor[None, :, None]
        numerator = head_factor * window_num + (1.0 - head_factor) * (near_num + far_num)
        denominator = factor[None, :] * window_sum.T + (1.0 - factor[None, :]) * (near_sum.T + far_sum)
        output = (numerator / denominator[:, :, None]).astype(jnp.bfloat16).reshape(BLOCK, HEADS * HEAD_DIM)
        lag_phi = phi_kf[:BLOCK]
        new_state = state + jnp.einsum('jhf,jhd->hfd', lag_phi, value_heads[:BLOCK])
        new_norm = norm + lax.optimization_barrier(jnp.sum(lag_phi, axis=0))
        return ((new_state, new_norm), output)
    start_state = jnp.zeros((HEADS, 2 * FEAT, HEAD_DIM), jnp.float32)
    start_norm = jnp.zeros((HEADS, 2 * FEAT), jnp.float32)
    carry, outputs = lax.scan(block_step, (start_state, start_norm), jnp.arange(TOKENS // BLOCK, dtype=jnp.int32))
    return outputs.reshape(TOKENS, HEADS * HEAD_DIM)
```

```python
import math

import jax
import jax.numpy as jnp
from jax import lax
from jax.sharding import PartitionSpec as P

WINDOW = 64
BLOCK = 512
SPAN = 256


def passed_along(value, axis, steps):
    count = lax.axis_size(axis)
    first, last = (max(0, -steps), min(count, count - steps))
    return lax.ppermute(value, axis, [(source, source + steps) for source in range(first, last)])


def angle_tables(positions, half):
    frequency = [500000.0 ** (-float(order) / half) for order in range(half)]
    coarse = jnp.asarray([4096.0 * value % (2.0 * math.pi) for value in frequency], jnp.float32)
    medium = jnp.asarray([64.0 * value % (2.0 * math.pi) for value in frequency], jnp.float32)
    finest = jnp.asarray(frequency, jnp.float32)
    upper = (positions // 4096).astype(jnp.float32)[:, None] * coarse[None, :]
    middle = (positions // 64 % 64).astype(jnp.float32)[:, None] * medium[None, :]
    lower = (positions % 64).astype(jnp.float32)[:, None] * finest[None, :]
    cos_high = jnp.cos(upper) * jnp.cos(middle) - jnp.sin(upper) * jnp.sin(middle)
    sin_high = jnp.sin(upper) * jnp.cos(middle) + jnp.cos(upper) * jnp.sin(middle)
    cosine = cos_high * jnp.cos(lower) - sin_high * jnp.sin(lower)
    sine = sin_high * jnp.cos(lower) + cos_high * jnp.sin(lower)
    return (cosine, sine)


def rotate(rows, cosine, sine):
    half = rows.shape[-1] // 2
    first = rows[..., :half]
    second = rows[..., half:]
    cos_rows = cosine[:, None, :]
    sin_rows = sine[:, None, :]
    return jnp.concatenate(
        [first * cos_rows - second * sin_rows, second * cos_rows + first * sin_rows], axis=-1
    )


def two_softmax(logits):
    return jnp.concatenate(
        [jax.nn.softmax(logits, axis=-1), jax.nn.softmax(-logits, axis=-1)], axis=-1
    )


def split_parts(full_value):
    high_part = full_value.astype(jnp.bfloat16)
    rest_part = (full_value - high_part.astype(jnp.float32)).astype(jnp.bfloat16)
    return (high_part, rest_part)


def body(queries, keys, values, offsets, query_map, key_map, window_logit):
    tokens = queries.shape[0]
    heads = query_map.shape[0]
    head_dim = query_map.shape[1]
    feat = query_map.shape[2]
    kv_local = keys.shape[1] // head_dim
    group = heads // kv_local
    blocks = tokens // BLOCK
    extent = BLOCK + WINDOW
    positions = (offsets[:, None] + jnp.arange(SPAN, dtype=jnp.int32)[None, :]).reshape(tokens)
    cosine, sine = angle_tables(positions, head_dim // 2)
    rot_q = rotate(
        queries.reshape(tokens, heads, head_dim).astype(jnp.float32), cosine, sine
    ).astype(jnp.bfloat16)
    rot_k = rotate(
        keys.reshape(tokens, kv_local, head_dim).astype(jnp.float32), cosine, sine
    ).astype(jnp.bfloat16)
    value_rows = values.reshape(tokens, kv_local, head_dim)
    tail_keys, tail_values = passed_along(
        (rot_k[tokens - WINDOW :], value_rows[tokens - WINDOW :]), "seq", 1
    )
    ext_keys = jnp.concatenate([tail_keys, rot_k], axis=0)
    ext_values = jnp.concatenate([tail_values, value_rows], axis=0)
    valid = (jnp.arange(tokens + WINDOW) >= WINDOW) | (lax.axis_index("seq") > 0)
    query_logits = jnp.einsum("nhd,hdf->nhf", rot_q, query_map, preferred_element_type=jnp.float32)
    phi_query = (
        two_softmax(query_logits).astype(jnp.bfloat16).reshape(tokens, kv_local, group, 2 * feat)
    )
    grouped_map = key_map.reshape(kv_local, group, head_dim, feat)
    key_logits = jnp.einsum(
        "ngd,gkdf->ngkf", ext_keys, grouped_map, preferred_element_type=jnp.float32
    )
    phi_key = jnp.where(valid[:, None, None, None], two_softmax(key_logits), 0.0).astype(
        jnp.bfloat16
    )
    lag_phi = phi_key[:tokens].reshape(blocks, BLOCK, kv_local, group, 2 * feat)
    lag_values = ext_values[:tokens].reshape(blocks, BLOCK, kv_local, head_dim)
    block_states = jnp.einsum(
        "bjgkf,bjgd->bgkfd", lag_phi, lag_values, preferred_element_type=jnp.float32
    )
    block_norms = jnp.sum(lag_phi, axis=1, dtype=jnp.float32)
    total_state = jnp.sum(block_states, axis=0)
    total_norm = jnp.sum(block_norms, axis=0)
    before_state = jnp.concatenate(
        [jnp.zeros_like(block_states), jnp.cumsum(block_states, axis=0)[:-1]], axis=0
    )
    before_norm = jnp.concatenate(
        [jnp.zeros_like(block_norms), jnp.cumsum(block_norms, axis=0)[:-1]], axis=0
    )
    state_shape = total_state.shape
    state_size = total_state.size
    packed = jnp.concatenate([total_state.reshape(-1), total_norm.reshape(-1)])
    inclusive = packed
    exclusive = jnp.zeros_like(packed)
    count = lax.axis_size("seq")
    steps = 1
    while steps < count:
        received = passed_along(inclusive, "seq", steps)
        exclusive = exclusive + received
        if 2 * steps < count:
            inclusive = inclusive + received
        steps *= 2
    prior_state = exclusive[:state_size].reshape(state_shape)
    prior_norm = exclusive[state_size:].reshape(total_norm.shape)
    factor = jax.nn.sigmoid(window_logit).reshape(kv_local, group)
    rot_grouped = rot_q.reshape(tokens, kv_local, group, head_dim)
    row_index = jnp.arange(BLOCK)[:, None]
    col_index = jnp.arange(extent)[None, :]
    window_mask = (col_index > row_index) & (col_index <= row_index + WINDOW)
    linear_mask = col_index <= row_index
    live = valid[None, :]
    scores = jnp.einsum(
        "igkd,jgd->gkij", rot_grouped, ext_keys, preferred_element_type=jnp.float32
    ) / math.sqrt(head_dim)
    near_window = window_mask & live
    peak = jnp.max(jnp.where(near_window, scores, -jnp.inf), axis=-1, keepdims=True)
    weights = jnp.where(near_window, jnp.exp(scores - peak), 0.0)
    window_sum = jnp.sum(weights, axis=-1)
    affinity = jnp.einsum("igkf,jgkf->gkij", phi_query, phi_key, preferred_element_type=jnp.float32)
    affinity = jnp.where(linear_mask & live, affinity, 0.0)
    near_sum = jnp.sum(affinity, axis=-1)
    window_num = jnp.einsum(
        "gkij,jgd->igkd",
        weights.astype(jnp.bfloat16),
        ext_values,
        preferred_element_type=jnp.float32,
    )
    near_num = jnp.einsum(
        "gkij,jgd->igkd",
        affinity.astype(jnp.bfloat16),
        ext_values,
        preferred_element_type=jnp.float32,
    )
    state_now = prior_state + before_state[0]
    norm_now = prior_norm + before_norm[0]
    state_high, state_rest = split_parts(state_now)
    norm_high, norm_rest = split_parts(norm_now)
    far_num = jnp.einsum(
        "igkf,gkfd->igkd", phi_query, state_high, preferred_element_type=jnp.float32
    )
    far_num = far_num + jnp.einsum(
        "igkf,gkfd->igkd", phi_query, state_rest, preferred_element_type=jnp.float32
    )
    far_sum = jnp.einsum("igkf,gkf->igk", phi_query, norm_high, preferred_element_type=jnp.float32)
    far_sum = far_sum + jnp.einsum(
        "igkf,gkf->igk", phi_query, norm_rest, preferred_element_type=jnp.float32
    )
    head_factor = factor[None, :, :, None]
    numerator = head_factor * window_num + (1.0 - head_factor) * (near_num + far_num)
    denominator = factor[None] * jnp.transpose(window_sum, (2, 0, 1)) + (1.0 - factor[None]) * (
        jnp.transpose(near_sum, (2, 0, 1)) + far_sum
    )
    outputs = (numerator / denominator[..., None]).astype(jnp.bfloat16)
    result = outputs.reshape(tokens, heads * head_dim)
    return lax.all_to_all(result, "head", split_axis=0, concat_axis=1, tiled=True)


def solution(mesh):
    in_specs = (
        P("seq", "head"),
        P("seq", "head"),
        P("seq", "head"),
        P("seq"),
        P("head", None, None),
        P("head", None, None),
        P("head"),
    )
    out_specs = P(("seq", "head"), None)
    return jax.shard_map(body, mesh=mesh, in_specs=in_specs, out_specs=out_specs, check_vma=False)
```

```python
import math

import jax
import jax.numpy as jnp
from jax import lax
from jax.sharding import PartitionSpec as P

WINDOW = 64
BLOCK = 512
SPAN = 256


def passed_along(value, axis, steps):
    count = lax.axis_size(axis)
    first, last = (max(0, -steps), min(count, count - steps))
    return lax.ppermute(value, axis, [(source, source + steps) for source in range(first, last)])


def angle_tables(positions, half):
    frequency = [500000.0 ** (-float(order) / half) for order in range(half)]
    coarse = jnp.asarray([4096.0 * value % (2.0 * math.pi) for value in frequency], jnp.float32)
    medium = jnp.asarray([64.0 * value % (2.0 * math.pi) for value in frequency], jnp.float32)
    finest = jnp.asarray(frequency, jnp.float32)
    upper = (positions // 4096).astype(jnp.float32)[:, None] * coarse[None, :]
    middle = (positions // 64 % 64).astype(jnp.float32)[:, None] * medium[None, :]
    lower = (positions % 64).astype(jnp.float32)[:, None] * finest[None, :]
    cos_high = jnp.cos(upper) * jnp.cos(middle) - jnp.sin(upper) * jnp.sin(middle)
    sin_high = jnp.sin(upper) * jnp.cos(middle) + jnp.cos(upper) * jnp.sin(middle)
    cosine = cos_high * jnp.cos(lower) - sin_high * jnp.sin(lower)
    sine = sin_high * jnp.cos(lower) + cos_high * jnp.sin(lower)
    return (cosine, sine)


def rotate(rows, cosine, sine):
    half = rows.shape[-1] // 2
    first = rows[..., :half]
    second = rows[..., half:]
    cos_rows = cosine[:, None, :]
    sin_rows = sine[:, None, :]
    return jnp.concatenate(
        [first * cos_rows - second * sin_rows, second * cos_rows + first * sin_rows], axis=-1
    )


def two_softmax(logits):
    return jnp.concatenate(
        [jax.nn.softmax(logits, axis=-1), jax.nn.softmax(-logits, axis=-1)], axis=-1
    )


def split_parts(full_value):
    high_part = full_value.astype(jnp.bfloat16)
    rest_part = (full_value - high_part.astype(jnp.float32)).astype(jnp.bfloat16)
    return (high_part, rest_part)


def body(queries, keys, values, offsets, query_map, key_map, window_logit):
    tokens = queries.shape[0]
    heads = query_map.shape[0]
    head_dim = query_map.shape[1]
    feat = query_map.shape[2]
    kv_local = keys.shape[1] // head_dim
    group = heads // kv_local
    blocks = tokens // BLOCK
    extent = BLOCK + WINDOW
    positions = (offsets[:, None] + jnp.arange(SPAN, dtype=jnp.int32)[None, :]).reshape(tokens)
    cosine, sine = angle_tables(positions, head_dim // 2)
    rot_q = rotate(
        queries.reshape(tokens, heads, head_dim).astype(jnp.float32), cosine, sine
    ).astype(jnp.bfloat16)
    rot_k = rotate(
        keys.reshape(tokens, kv_local, head_dim).astype(jnp.float32), cosine, sine
    ).astype(jnp.bfloat16)
    value_rows = values.reshape(tokens, kv_local, head_dim)
    tail_keys, tail_values = passed_along(
        (rot_k[tokens - WINDOW :], value_rows[tokens - WINDOW :]), "seq", 1
    )
    ext_keys = jnp.concatenate([tail_keys, rot_k], axis=0)
    ext_values = jnp.concatenate([tail_values, value_rows], axis=0)
    valid = (jnp.arange(tokens + WINDOW) >= WINDOW) | (lax.axis_index("seq") > 0)
    query_logits = jnp.einsum("nhd,hdf->nhf", rot_q, query_map, preferred_element_type=jnp.float32)
    phi_query = (
        two_softmax(query_logits).astype(jnp.bfloat16).reshape(tokens, kv_local, group, 2 * feat)
    )
    grouped_map = key_map.reshape(kv_local, group, head_dim, feat)
    key_logits = jnp.einsum(
        "ngd,gkdf->ngkf", ext_keys, grouped_map, preferred_element_type=jnp.float32
    )
    phi_key = jnp.where(valid[:, None, None, None], two_softmax(key_logits), 0.0).astype(
        jnp.bfloat16
    )
    lag_phi = phi_key[:tokens].reshape(blocks, BLOCK, kv_local, group, 2 * feat)
    lag_values = ext_values[:tokens].reshape(blocks, BLOCK, kv_local, head_dim)
    block_states = jnp.einsum(
        "bjgkf,bjgd->bgkfd", lag_phi, lag_values, preferred_element_type=jnp.float32
    )
    block_norms = jnp.sum(lag_phi, axis=1, dtype=jnp.float32)
    total_state = jnp.sum(block_states, axis=0)
    total_norm = jnp.sum(block_norms, axis=0)
    before_state = jnp.concatenate(
        [jnp.zeros_like(block_states), jnp.cumsum(block_states, axis=0)[:-1]], axis=0
    )
    before_norm = jnp.concatenate(
        [jnp.zeros_like(block_norms), jnp.cumsum(block_norms, axis=0)[:-1]], axis=0
    )
    state_shape = total_state.shape
    state_size = total_state.size
    packed = jnp.concatenate([total_state.reshape(-1), total_norm.reshape(-1)])
    count = lax.axis_size("seq")
    shifts = []
    steps = 1
    while steps < count:
        shifts.append(steps)
        steps *= 2
    half = len(shifts) // 2 + 1
    orders = (shifts, shifts[half:] + shifts[:half])
    middle = packed.size // 2
    pieces = []
    for order, piece in zip(orders, (packed[:middle], packed[middle:])):
        inclusive = piece
        exclusive = jnp.zeros_like(piece)
        for place, shift in enumerate(order):
            received = passed_along(inclusive, "seq", shift)
            exclusive = exclusive + received
            if place + 1 < len(order):
                inclusive = inclusive + received
        pieces.append(exclusive)
    exclusive = jnp.concatenate(pieces)
    prior_state = exclusive[:state_size].reshape(state_shape)
    prior_norm = exclusive[state_size:].reshape(total_norm.shape)
    factor = jax.nn.sigmoid(window_logit).reshape(kv_local, group)
    rot_grouped = rot_q.reshape(tokens, kv_local, group, head_dim)
    row_index = jnp.arange(BLOCK)[:, None]
    col_index = jnp.arange(extent)[None, :]
    window_mask = (col_index > row_index) & (col_index <= row_index + WINDOW)
    linear_mask = col_index <= row_index
    live = valid[None, :]
    scores = jnp.einsum(
        "igkd,jgd->gkij", rot_grouped, ext_keys, preferred_element_type=jnp.float32
    ) / math.sqrt(head_dim)
    near_window = window_mask & live
    peak = jnp.max(jnp.where(near_window, scores, -jnp.inf), axis=-1, keepdims=True)
    weights = jnp.where(near_window, jnp.exp(scores - peak), 0.0)
    window_sum = jnp.sum(weights, axis=-1)
    affinity = jnp.einsum("igkf,jgkf->gkij", phi_query, phi_key, preferred_element_type=jnp.float32)
    affinity = jnp.where(linear_mask & live, affinity, 0.0)
    near_sum = jnp.sum(affinity, axis=-1)
    window_num = jnp.einsum(
        "gkij,jgd->igkd",
        weights.astype(jnp.bfloat16),
        ext_values,
        preferred_element_type=jnp.float32,
    )
    near_num = jnp.einsum(
        "gkij,jgd->igkd",
        affinity.astype(jnp.bfloat16),
        ext_values,
        preferred_element_type=jnp.float32,
    )
    state_now = prior_state + before_state[0]
    norm_now = prior_norm + before_norm[0]
    state_high, state_rest = split_parts(state_now)
    norm_high, norm_rest = split_parts(norm_now)
    far_num = jnp.einsum(
        "igkf,gkfd->igkd", phi_query, state_high, preferred_element_type=jnp.float32
    )
    far_num = far_num + jnp.einsum(
        "igkf,gkfd->igkd", phi_query, state_rest, preferred_element_type=jnp.float32
    )
    far_sum = jnp.einsum("igkf,gkf->igk", phi_query, norm_high, preferred_element_type=jnp.float32)
    far_sum = far_sum + jnp.einsum(
        "igkf,gkf->igk", phi_query, norm_rest, preferred_element_type=jnp.float32
    )
    head_factor = factor[None, :, :, None]
    numerator = head_factor * window_num + (1.0 - head_factor) * (near_num + far_num)
    denominator = factor[None] * jnp.transpose(window_sum, (2, 0, 1)) + (1.0 - factor[None]) * (
        jnp.transpose(near_sum, (2, 0, 1)) + far_sum
    )
    outputs = (numerator / denominator[..., None]).astype(jnp.bfloat16)
    result = outputs.reshape(tokens, heads * head_dim)
    return lax.all_to_all(result, "head", split_axis=0, concat_axis=1, tiled=True)


def solution(mesh):
    in_specs = (
        P("seq", "head"),
        P("seq", "head"),
        P("seq", "head"),
        P("seq"),
        P("head", None, None),
        P("head", None, None),
        P("head"),
    )
    out_specs = P(("seq", "head"), None)
    return jax.shard_map(body, mesh=mesh, in_specs=in_specs, out_specs=out_specs, check_vma=False)
```

```python
import math

import jax
import jax.numpy as jnp
from jax import lax
from jax.sharding import PartitionSpec as P

WINDOW = 64
BLOCK = 512
SPAN = 256


def passed_along(value, axis, steps):
    count = lax.axis_size(axis)
    first, last = (max(0, -steps), min(count, count - steps))
    return lax.ppermute(value, axis, [(source, source + steps) for source in range(first, last)])


def angle_tables(positions, half):
    frequency = [500000.0 ** (-float(order) / half) for order in range(half)]
    coarse = jnp.asarray([4096.0 * value % (2.0 * math.pi) for value in frequency], jnp.float32)
    medium = jnp.asarray([64.0 * value % (2.0 * math.pi) for value in frequency], jnp.float32)
    finest = jnp.asarray(frequency, jnp.float32)
    upper = (positions // 4096).astype(jnp.float32)[:, None] * coarse[None, :]
    middle = (positions // 64 % 64).astype(jnp.float32)[:, None] * medium[None, :]
    lower = (positions % 64).astype(jnp.float32)[:, None] * finest[None, :]
    cos_high = jnp.cos(upper) * jnp.cos(middle) - jnp.sin(upper) * jnp.sin(middle)
    sin_high = jnp.sin(upper) * jnp.cos(middle) + jnp.cos(upper) * jnp.sin(middle)
    cosine = cos_high * jnp.cos(lower) - sin_high * jnp.sin(lower)
    sine = sin_high * jnp.cos(lower) + cos_high * jnp.sin(lower)
    return (cosine, sine)


def rotate(rows, cosine, sine):
    half = rows.shape[-1] // 2
    first = rows[..., :half]
    second = rows[..., half:]
    cos_rows = cosine[:, None, :]
    sin_rows = sine[:, None, :]
    return jnp.concatenate(
        [first * cos_rows - second * sin_rows, second * cos_rows + first * sin_rows], axis=-1
    )


def two_softmax(logits):
    return jnp.concatenate(
        [jax.nn.softmax(logits, axis=-1), jax.nn.softmax(-logits, axis=-1)], axis=-1
    )


def split_parts(full_value):
    high_part = full_value.astype(jnp.bfloat16)
    rest_part = (full_value - high_part.astype(jnp.float32)).astype(jnp.bfloat16)
    return (high_part, rest_part)


def body(queries, keys, values, offsets, query_map, key_map, window_logit):
    tokens = queries.shape[0]
    heads = query_map.shape[0]
    head_dim = query_map.shape[1]
    feat = query_map.shape[2]
    kv_local = keys.shape[1] // head_dim
    group = heads // kv_local
    blocks = tokens // BLOCK
    extent = BLOCK + WINDOW
    positions = (offsets[:, None] + jnp.arange(SPAN, dtype=jnp.int32)[None, :]).reshape(tokens)
    cosine, sine = angle_tables(positions, head_dim // 2)
    rot_k = rotate(
        keys.reshape(tokens, kv_local, head_dim).astype(jnp.float32), cosine, sine
    ).astype(jnp.bfloat16)
    value_rows = values.reshape(tokens, kv_local, head_dim)
    tail_keys, tail_values = passed_along(
        (rot_k[tokens - WINDOW :], value_rows[tokens - WINDOW :]), "seq", 1
    )
    ext_keys = jnp.concatenate([tail_keys, rot_k], axis=0)
    ext_values = jnp.concatenate([tail_values, value_rows], axis=0)
    valid = (jnp.arange(tokens + WINDOW) >= WINDOW) | (lax.axis_index("seq") > 0)
    grouped_map = key_map.reshape(kv_local, group, head_dim, feat)
    key_logits = jnp.einsum(
        "ngd,gkdf->ngkf", ext_keys, grouped_map, preferred_element_type=jnp.float32
    )
    phi_key = jnp.where(valid[:, None, None, None], two_softmax(key_logits), 0.0).astype(
        jnp.bfloat16
    )
    lag_phi = phi_key[:tokens].reshape(blocks, BLOCK, kv_local, group, 2 * feat)
    lag_values = ext_values[:tokens].reshape(blocks, BLOCK, kv_local, head_dim)
    block_states = jnp.einsum(
        "bjgkf,bjgd->bgkfd", lag_phi, lag_values, preferred_element_type=jnp.float32
    )
    block_norms = jnp.sum(lag_phi, axis=1, dtype=jnp.float32)
    total_state = jnp.sum(block_states, axis=0)
    total_norm = jnp.sum(block_norms, axis=0)
    before_state = jnp.concatenate(
        [jnp.zeros_like(block_states), jnp.cumsum(block_states, axis=0)[:-1]], axis=0
    )
    before_norm = jnp.concatenate(
        [jnp.zeros_like(block_norms), jnp.cumsum(block_norms, axis=0)[:-1]], axis=0
    )
    state_shape = total_state.shape
    state_size = total_state.size
    packed = jnp.concatenate([total_state.reshape(-1), total_norm.reshape(-1)])
    count = lax.axis_size("seq")
    shifts = []
    steps = 1
    while steps < count:
        shifts.append(steps)
        steps *= 2
    half = len(shifts) // 2 + 1
    orders = (shifts, shifts[half:] + shifts[:half])
    middle = packed.size // 2
    pieces = []
    for order, piece in zip(orders, (packed[:middle], packed[middle:])):
        inclusive = piece
        exclusive = jnp.zeros_like(piece)
        for place, shift in enumerate(order):
            received = passed_along(inclusive, "seq", shift)
            if not pieces and place == 0:
                first_received = received
            exclusive = exclusive + received
            if place + 1 < len(order):
                inclusive = inclusive + received
        pieces.append(exclusive)
    exclusive = jnp.concatenate(pieces)
    queries, first_received = lax.optimization_barrier((queries, first_received))
    rot_q = rotate(
        queries.reshape(tokens, heads, head_dim).astype(jnp.float32), cosine, sine
    ).astype(jnp.bfloat16)
    query_logits = jnp.einsum("nhd,hdf->nhf", rot_q, query_map, preferred_element_type=jnp.float32)
    phi_query = (
        two_softmax(query_logits).astype(jnp.bfloat16).reshape(tokens, kv_local, group, 2 * feat)
    )
    prior_state = exclusive[:state_size].reshape(state_shape)
    prior_norm = exclusive[state_size:].reshape(total_norm.shape)
    factor = jax.nn.sigmoid(window_logit).reshape(kv_local, group)
    rot_grouped = rot_q.reshape(tokens, kv_local, group, head_dim)
    row_index = jnp.arange(BLOCK)[:, None]
    col_index = jnp.arange(extent)[None, :]
    window_mask = (col_index > row_index) & (col_index <= row_index + WINDOW)
    linear_mask = col_index <= row_index
    live = valid[None, :]
    scores = jnp.einsum(
        "igkd,jgd->gkij", rot_grouped, ext_keys, preferred_element_type=jnp.float32
    ) / math.sqrt(head_dim)
    near_window = window_mask & live
    peak = jnp.max(jnp.where(near_window, scores, -jnp.inf), axis=-1, keepdims=True)
    weights = jnp.where(near_window, jnp.exp(scores - peak), 0.0)
    window_sum = jnp.sum(weights, axis=-1)
    affinity = jnp.einsum("igkf,jgkf->gkij", phi_query, phi_key, preferred_element_type=jnp.float32)
    affinity = jnp.where(linear_mask & live, affinity, 0.0)
    near_sum = jnp.sum(affinity, axis=-1)
    window_num = jnp.einsum(
        "gkij,jgd->igkd",
        weights.astype(jnp.bfloat16),
        ext_values,
        preferred_element_type=jnp.float32,
    )
    near_num = jnp.einsum(
        "gkij,jgd->igkd",
        affinity.astype(jnp.bfloat16),
        ext_values,
        preferred_element_type=jnp.float32,
    )
    state_now = prior_state + before_state[0]
    norm_now = prior_norm + before_norm[0]
    state_high, state_rest = split_parts(state_now)
    norm_high, norm_rest = split_parts(norm_now)
    far_num = jnp.einsum(
        "igkf,gkfd->igkd", phi_query, state_high, preferred_element_type=jnp.float32
    )
    far_num = far_num + jnp.einsum(
        "igkf,gkfd->igkd", phi_query, state_rest, preferred_element_type=jnp.float32
    )
    far_sum = jnp.einsum("igkf,gkf->igk", phi_query, norm_high, preferred_element_type=jnp.float32)
    far_sum = far_sum + jnp.einsum(
        "igkf,gkf->igk", phi_query, norm_rest, preferred_element_type=jnp.float32
    )
    head_factor = factor[None, :, :, None]
    numerator = head_factor * window_num + (1.0 - head_factor) * (near_num + far_num)
    denominator = factor[None] * jnp.transpose(window_sum, (2, 0, 1)) + (1.0 - factor[None]) * (
        jnp.transpose(near_sum, (2, 0, 1)) + far_sum
    )
    outputs = (numerator / denominator[..., None]).astype(jnp.bfloat16)
    result = outputs.reshape(tokens, heads * head_dim)
    return lax.all_to_all(result, "head", split_axis=0, concat_axis=1, tiled=True)


def solution(mesh):
    in_specs = (
        P("seq", "head"),
        P("seq", "head"),
        P("seq", "head"),
        P("seq"),
        P("head", None, None),
        P("head", None, None),
        P("head"),
    )
    out_specs = P(("seq", "head"), None)
    return jax.shard_map(body, mesh=mesh, in_specs=in_specs, out_specs=out_specs, check_vma=False)
```

```python
import math

import jax
import jax.numpy as jnp
from jax import lax
from jax.sharding import PartitionSpec as P

WINDOW = 64
BLOCK = 512
SPAN = 256


def passed_along(value, axis, steps):
    count = lax.axis_size(axis)
    first, last = (max(0, -steps), min(count, count - steps))
    return lax.ppermute(value, axis, [(source, source + steps) for source in range(first, last)])


def angle_tables(positions, half):
    frequency = [500000.0 ** (-float(order) / half) for order in range(half)]
    coarse = jnp.asarray([4096.0 * value % (2.0 * math.pi) for value in frequency], jnp.float32)
    medium = jnp.asarray([64.0 * value % (2.0 * math.pi) for value in frequency], jnp.float32)
    finest = jnp.asarray(frequency, jnp.float32)
    upper = (positions // 4096).astype(jnp.float32)[:, None] * coarse[None, :]
    middle = (positions // 64 % 64).astype(jnp.float32)[:, None] * medium[None, :]
    lower = (positions % 64).astype(jnp.float32)[:, None] * finest[None, :]
    cos_high = jnp.cos(upper) * jnp.cos(middle) - jnp.sin(upper) * jnp.sin(middle)
    sin_high = jnp.sin(upper) * jnp.cos(middle) + jnp.cos(upper) * jnp.sin(middle)
    cosine = cos_high * jnp.cos(lower) - sin_high * jnp.sin(lower)
    sine = sin_high * jnp.cos(lower) + cos_high * jnp.sin(lower)
    return (cosine, sine)


def rotate(rows, cosine, sine):
    half = rows.shape[-1] // 2
    first = rows[..., :half]
    second = rows[..., half:]
    cos_rows = cosine[:, None, :]
    sin_rows = sine[:, None, :]
    return jnp.concatenate(
        [first * cos_rows - second * sin_rows, second * cos_rows + first * sin_rows], axis=-1
    )


def two_softmax(logits):
    return jnp.concatenate(
        [jax.nn.softmax(logits, axis=-1), jax.nn.softmax(-logits, axis=-1)], axis=-1
    )


def split_parts(full_value):
    high_part = full_value.astype(jnp.bfloat16)
    rest_part = (full_value - high_part.astype(jnp.float32)).astype(jnp.bfloat16)
    return (high_part, rest_part)


def body(queries, keys, values, offsets, query_map, key_map, window_logit):
    tokens = queries.shape[0]
    heads = query_map.shape[0]
    head_dim = query_map.shape[1]
    feat = query_map.shape[2]
    kv_local = keys.shape[1] // head_dim
    group = heads // kv_local
    blocks = tokens // BLOCK
    extent = BLOCK + WINDOW
    positions = (offsets[:, None] + jnp.arange(SPAN, dtype=jnp.int32)[None, :]).reshape(tokens)
    cosine, sine = angle_tables(positions, head_dim // 2)
    rot_k = rotate(
        keys.reshape(tokens, kv_local, head_dim).astype(jnp.float32), cosine, sine
    ).astype(jnp.bfloat16)
    value_rows = values.reshape(tokens, kv_local, head_dim)
    tail_both = passed_along(
        jnp.concatenate([rot_k[tokens - WINDOW :], value_rows[tokens - WINDOW :]], axis=-1),
        "seq",
        1,
    )
    tail_keys = tail_both[..., :head_dim]
    tail_values = tail_both[..., head_dim:]
    ext_keys = jnp.concatenate([tail_keys, rot_k], axis=0)
    ext_values = jnp.concatenate([tail_values, value_rows], axis=0)
    valid = (jnp.arange(tokens + WINDOW) >= WINDOW) | (lax.axis_index("seq") > 0)
    grouped_map = key_map.reshape(kv_local, group, head_dim, feat)
    key_logits = jnp.einsum(
        "ngd,gkdf->gkfn", ext_keys, grouped_map, preferred_element_type=jnp.float32
    )
    phi_key = jnp.where(
        valid[None, None, None, :],
        jnp.concatenate(
            [jax.nn.softmax(key_logits, axis=-2), jax.nn.softmax(-key_logits, axis=-2)], axis=-2
        ),
        0.0,
    ).astype(jnp.bfloat16)
    lag_phi = phi_key[..., :tokens]
    lag_values = ext_values[:tokens]
    block_states = jnp.einsum(
        "gkfj,jgd->gkfd", lag_phi, lag_values, preferred_element_type=jnp.float32
    )[None]
    block_norms = jnp.sum(lag_phi, axis=-1, dtype=jnp.float32)[None]
    total_state = jnp.sum(block_states, axis=0)
    total_norm = jnp.sum(block_norms, axis=0)
    before_state = jnp.concatenate(
        [jnp.zeros_like(block_states), jnp.cumsum(block_states, axis=0)[:-1]], axis=0
    )
    before_norm = jnp.concatenate(
        [jnp.zeros_like(block_norms), jnp.cumsum(block_norms, axis=0)[:-1]], axis=0
    )
    state_shape = total_state.shape
    state_size = total_state.size
    packed = jnp.concatenate([total_state.reshape(-1), total_norm.reshape(-1)])
    count = lax.axis_size("seq")
    shifts = []
    steps = 1
    while steps < count:
        shifts.append(steps)
        steps *= 2
    half = len(shifts) // 2 + 1
    orders = (shifts, shifts[half:] + shifts[:half])
    middle = packed.size // 2
    pieces = []
    for order, piece in zip(orders, (packed[:middle], packed[middle:])):
        inclusive = piece
        exclusive = jnp.zeros_like(piece)
        for place, shift in enumerate(order):
            received = passed_along(inclusive, "seq", shift)
            if not pieces and place == 0:
                first_received = received
            exclusive = exclusive + received
            if place + 1 < len(order):
                inclusive = inclusive + received
        pieces.append(exclusive)
    exclusive = jnp.concatenate(pieces)
    queries, first_received = lax.optimization_barrier((queries, first_received))
    rot_q = rotate(
        queries.reshape(tokens, heads, head_dim).astype(jnp.float32), cosine, sine
    ).astype(jnp.bfloat16)
    query_logits = jnp.einsum("nhd,hdf->nhf", rot_q, query_map, preferred_element_type=jnp.float32)
    phi_query = (
        two_softmax(query_logits).astype(jnp.bfloat16).reshape(tokens, kv_local, group, 2 * feat)
    )
    prior_state = exclusive[:state_size].reshape(state_shape)
    prior_norm = exclusive[state_size:].reshape(total_norm.shape)
    factor = jax.nn.sigmoid(window_logit).reshape(kv_local, group)
    rot_grouped = rot_q.reshape(tokens, kv_local, group, head_dim)
    row_index = jnp.arange(BLOCK)[:, None]
    col_index = jnp.arange(extent)[None, :]
    window_mask = (col_index > row_index) & (col_index <= row_index + WINDOW)
    linear_mask = col_index <= row_index
    live = valid[None, :]
    scores = jnp.einsum(
        "igkd,jgd->gkij", rot_grouped, ext_keys, preferred_element_type=jnp.float32
    ) / math.sqrt(head_dim)
    near_window = window_mask & live
    peak = jnp.max(jnp.where(near_window, scores, -jnp.inf), axis=-1, keepdims=True)
    weights = jnp.where(near_window, jnp.exp(scores - peak), 0.0)
    window_sum = jnp.sum(weights, axis=-1)
    affinity = jnp.einsum("igkf,gkfj->gkij", phi_query, phi_key, preferred_element_type=jnp.float32)
    affinity = jnp.where(linear_mask & live, affinity, 0.0)
    near_sum = jnp.sum(affinity, axis=-1)
    window_num = jnp.einsum(
        "gkij,jgd->igkd",
        weights.astype(jnp.bfloat16),
        ext_values,
        preferred_element_type=jnp.float32,
    )
    near_num = jnp.einsum(
        "gkij,jgd->igkd",
        affinity.astype(jnp.bfloat16),
        ext_values,
        preferred_element_type=jnp.float32,
    )
    state_now = prior_state + before_state[0]
    norm_now = prior_norm + before_norm[0]
    state_high, state_rest = split_parts(state_now)
    norm_high, norm_rest = split_parts(norm_now)
    far_num = jnp.einsum(
        "igkf,gkfd->igkd", phi_query, state_high, preferred_element_type=jnp.float32
    )
    far_num = far_num + jnp.einsum(
        "igkf,gkfd->igkd", phi_query, state_rest, preferred_element_type=jnp.float32
    )
    far_sum = jnp.einsum("igkf,gkf->igk", phi_query, norm_high, preferred_element_type=jnp.float32)
    far_sum = far_sum + jnp.einsum(
        "igkf,gkf->igk", phi_query, norm_rest, preferred_element_type=jnp.float32
    )
    head_factor = factor[None, :, :, None]
    numerator = head_factor * window_num + (1.0 - head_factor) * (near_num + far_num)
    denominator = factor[None] * jnp.transpose(window_sum, (2, 0, 1)) + (1.0 - factor[None]) * (
        jnp.transpose(near_sum, (2, 0, 1)) + far_sum
    )
    outputs = (numerator / denominator[..., None]).astype(jnp.bfloat16)
    result = outputs.reshape(tokens, heads * head_dim)
    return lax.all_to_all(result, "head", split_axis=0, concat_axis=1, tiled=True)


def solution(mesh):
    in_specs = (
        P("seq", "head"),
        P("seq", "head"),
        P("seq", "head"),
        P("seq"),
        P("head", None, None),
        P("head", None, None),
        P("head"),
    )
    out_specs = P(("seq", "head"), None)
    return jax.shard_map(body, mesh=mesh, in_specs=in_specs, out_specs=out_specs, check_vma=False)
```

```python
import math

import jax
import jax.numpy as jnp
from jax import lax
from jax.sharding import PartitionSpec as P

WINDOW = 64
BLOCK = 512
SPAN = 256


def passed_along(value, axis, steps):
    names = axis if isinstance(axis, tuple) else (axis,)
    count = math.prod(lax.axis_size(name) for name in names)
    first, last = (max(0, -steps), min(count, count - steps))
    return lax.ppermute(value, axis, [(source, source + steps) for source in range(first, last)])


def angle_tables(positions, half):
    frequency = [500000.0 ** (-float(order) / half) for order in range(half)]
    coarse = jnp.asarray([4096.0 * value % (2.0 * math.pi) for value in frequency], jnp.float32)
    medium = jnp.asarray([64.0 * value % (2.0 * math.pi) for value in frequency], jnp.float32)
    finest = jnp.asarray(frequency, jnp.float32)
    upper = (positions // 4096).astype(jnp.float32)[:, None] * coarse[None, :]
    middle = (positions // 64 % 64).astype(jnp.float32)[:, None] * medium[None, :]
    lower = (positions % 64).astype(jnp.float32)[:, None] * finest[None, :]
    cos_high = jnp.cos(upper) * jnp.cos(middle) - jnp.sin(upper) * jnp.sin(middle)
    sin_high = jnp.sin(upper) * jnp.cos(middle) + jnp.cos(upper) * jnp.sin(middle)
    cosine = cos_high * jnp.cos(lower) - sin_high * jnp.sin(lower)
    sine = sin_high * jnp.cos(lower) + cos_high * jnp.sin(lower)
    return (cosine, sine)


def rotate(rows, cosine, sine):
    half = rows.shape[-1] // 2
    first = rows[..., :half]
    second = rows[..., half:]
    cos_rows = cosine[:, None, :]
    sin_rows = sine[:, None, :]
    return jnp.concatenate(
        [first * cos_rows - second * sin_rows, second * cos_rows + first * sin_rows], axis=-1
    )


def two_softmax(logits):
    return jnp.concatenate(
        [jax.nn.softmax(logits, axis=-1), jax.nn.softmax(-logits, axis=-1)], axis=-1
    )


def split_parts(full_value):
    high_part = full_value.astype(jnp.bfloat16)
    rest_part = (full_value - high_part.astype(jnp.float32)).astype(jnp.bfloat16)
    return (high_part, rest_part)


def body(queries, keys, values, offsets, query_map, key_map, window_logit):
    tokens = queries.shape[0]
    heads = query_map.shape[0]
    head_dim = query_map.shape[1]
    feat = query_map.shape[2]
    kv_local = keys.shape[1] // head_dim
    group = heads // kv_local
    blocks = tokens // BLOCK
    extent = BLOCK + WINDOW
    positions = (offsets[:, None] + jnp.arange(SPAN, dtype=jnp.int32)[None, :]).reshape(tokens)
    cosine, sine = angle_tables(positions, head_dim // 2)
    rot_k = rotate(
        keys.reshape(tokens, kv_local, head_dim).astype(jnp.float32), cosine, sine
    ).astype(jnp.bfloat16)
    value_rows = values.reshape(tokens, kv_local, head_dim)
    tail_keys, tail_values = passed_along(
        (rot_k[tokens - WINDOW :], value_rows[tokens - WINDOW :]), ("sx", "sz"), 1
    )
    ext_keys = jnp.concatenate([tail_keys, rot_k], axis=0)
    ext_values = jnp.concatenate([tail_values, value_rows], axis=0)
    valid = (jnp.arange(tokens + WINDOW) >= WINDOW) | (lax.axis_index("sx") > 0) | (lax.axis_index("sz") > 0)
    grouped_map = key_map.reshape(kv_local, group, head_dim, feat)
    key_logits = jnp.einsum(
        "ngd,gkdf->ngkf", ext_keys, grouped_map, preferred_element_type=jnp.float32
    )
    phi_key = jnp.where(valid[:, None, None, None], two_softmax(key_logits), 0.0).astype(
        jnp.bfloat16
    )
    lag_phi = phi_key[:tokens].reshape(blocks, BLOCK, kv_local, group, 2 * feat)
    lag_values = ext_values[:tokens].reshape(blocks, BLOCK, kv_local, head_dim)
    block_states = jnp.einsum(
        "bjgkf,bjgd->bgkfd", lag_phi, lag_values, preferred_element_type=jnp.float32
    )
    block_norms = jnp.sum(lag_phi, axis=1, dtype=jnp.float32)
    total_state = jnp.sum(block_states, axis=0)
    total_norm = jnp.sum(block_norms, axis=0)
    before_state = jnp.concatenate(
        [jnp.zeros_like(block_states), jnp.cumsum(block_states, axis=0)[:-1]], axis=0
    )
    before_norm = jnp.concatenate(
        [jnp.zeros_like(block_norms), jnp.cumsum(block_norms, axis=0)[:-1]], axis=0
    )
    state_shape = total_state.shape
    state_size = total_state.size
    packed = jnp.concatenate([total_state.reshape(-1), total_norm.reshape(-1)])
    def exclusive_scan(value, axis):
        count = lax.axis_size(axis)
        inclusive = value
        exclusive = jnp.zeros_like(value)
        first = None
        steps = 1
        while steps < count:
            received = passed_along(inclusive, axis, steps)
            first = received if first is None else first
            exclusive = exclusive + received
            if 2 * steps < count:
                inclusive = inclusive + received
            steps *= 2
        return exclusive, first

    row_total = lax.psum(packed, "sz")
    inner, first_received = exclusive_scan(packed, "sz")
    outer, _ = exclusive_scan(row_total, "sx")
    exclusive = inner + outer
    queries, first_received = lax.optimization_barrier((queries, first_received))
    rot_q = rotate(
        queries.reshape(tokens, heads, head_dim).astype(jnp.float32), cosine, sine
    ).astype(jnp.bfloat16)
    query_logits = jnp.einsum("nhd,hdf->nhf", rot_q, query_map, preferred_element_type=jnp.float32)
    phi_query = (
        two_softmax(query_logits).astype(jnp.bfloat16).reshape(tokens, kv_local, group, 2 * feat)
    )
    prior_state = exclusive[:state_size].reshape(state_shape)
    prior_norm = exclusive[state_size:].reshape(total_norm.shape)
    factor = jax.nn.sigmoid(window_logit).reshape(kv_local, group)
    rot_grouped = rot_q.reshape(tokens, kv_local, group, head_dim)
    row_index = jnp.arange(BLOCK)[:, None]
    col_index = jnp.arange(extent)[None, :]
    window_mask = (col_index > row_index) & (col_index <= row_index + WINDOW)
    linear_mask = col_index <= row_index
    live = valid[None, :]
    scores = jnp.einsum(
        "igkd,jgd->gkij", rot_grouped, ext_keys, preferred_element_type=jnp.float32
    ) / math.sqrt(head_dim)
    near_window = window_mask & live
    peak = jnp.max(jnp.where(near_window, scores, -jnp.inf), axis=-1, keepdims=True)
    weights = jnp.where(near_window, jnp.exp(scores - peak), 0.0)
    window_sum = jnp.sum(weights, axis=-1)
    affinity = jnp.einsum("igkf,jgkf->gkij", phi_query, phi_key, preferred_element_type=jnp.float32)
    affinity = jnp.where(linear_mask & live, affinity, 0.0)
    near_sum = jnp.sum(affinity, axis=-1)
    window_num = jnp.einsum(
        "gkij,jgd->igkd",
        weights.astype(jnp.bfloat16),
        ext_values,
        preferred_element_type=jnp.float32,
    )
    near_num = jnp.einsum(
        "gkij,jgd->igkd",
        affinity.astype(jnp.bfloat16),
        ext_values,
        preferred_element_type=jnp.float32,
    )
    state_now = prior_state + before_state[0]
    norm_now = prior_norm + before_norm[0]
    state_high, state_rest = split_parts(state_now)
    norm_high, norm_rest = split_parts(norm_now)
    far_num = jnp.einsum(
        "igkf,gkfd->igkd", phi_query, state_high, preferred_element_type=jnp.float32
    )
    far_num = far_num + jnp.einsum(
        "igkf,gkfd->igkd", phi_query, state_rest, preferred_element_type=jnp.float32
    )
    far_sum = jnp.einsum("igkf,gkf->igk", phi_query, norm_high, preferred_element_type=jnp.float32)
    far_sum = far_sum + jnp.einsum(
        "igkf,gkf->igk", phi_query, norm_rest, preferred_element_type=jnp.float32
    )
    head_factor = factor[None, :, :, None]
    numerator = head_factor * window_num + (1.0 - head_factor) * (near_num + far_num)
    denominator = factor[None] * jnp.transpose(window_sum, (2, 0, 1)) + (1.0 - factor[None]) * (
        jnp.transpose(near_sum, (2, 0, 1)) + far_sum
    )
    outputs = (numerator / denominator[..., None]).astype(jnp.bfloat16)
    result = outputs.reshape(tokens, heads * head_dim)
    return lax.all_to_all(result, "head", split_axis=0, concat_axis=1, tiled=True)


def solution(mesh):
    seq_count = mesh.shape["seq"]
    inner = math.gcd(seq_count, 8)
    split_mesh = jax.sharding.Mesh(
        mesh.devices.reshape(seq_count // inner, inner, mesh.shape["head"]), ("sx", "sz", "head")
    )
    rows = ("sx", "sz")
    in_specs = (
        P(rows, "head"),
        P(rows, "head"),
        P(rows, "head"),
        P(rows),
        P("head", None, None),
        P("head", None, None),
        P("head"),
    )
    out_specs = P(("sx", "sz", "head"), None)
    return jax.shard_map(
        body, mesh=split_mesh, in_specs=in_specs, out_specs=out_specs, check_vma=False
    )
```

```python
import math

import jax
import jax.numpy as jnp
from jax import lax
from jax.sharding import PartitionSpec as P

WINDOW = 64
BLOCK = 512
SPAN = 256


def passed_along(value, axis, steps):
    count = lax.axis_size(axis)
    first, last = (max(0, -steps), min(count, count - steps))
    return lax.ppermute(value, axis, [(source, source + steps) for source in range(first, last)])


def angle_tables(positions, half):
    frequency = [500000.0 ** (-float(order) / half) for order in range(half)]
    coarse = jnp.asarray([4096.0 * value % (2.0 * math.pi) for value in frequency], jnp.float32)
    medium = jnp.asarray([64.0 * value % (2.0 * math.pi) for value in frequency], jnp.float32)
    finest = jnp.asarray(frequency, jnp.float32)
    upper = (positions // 4096).astype(jnp.float32)[:, None] * coarse[None, :]
    middle = (positions // 64 % 64).astype(jnp.float32)[:, None] * medium[None, :]
    lower = (positions % 64).astype(jnp.float32)[:, None] * finest[None, :]
    cos_high = jnp.cos(upper) * jnp.cos(middle) - jnp.sin(upper) * jnp.sin(middle)
    sin_high = jnp.sin(upper) * jnp.cos(middle) + jnp.cos(upper) * jnp.sin(middle)
    cosine = cos_high * jnp.cos(lower) - sin_high * jnp.sin(lower)
    sine = sin_high * jnp.cos(lower) + cos_high * jnp.sin(lower)
    return (cosine, sine)


def rotate(rows, cosine, sine):
    half = rows.shape[-1] // 2
    first = rows[..., :half]
    second = rows[..., half:]
    cos_rows = cosine[:, None, :]
    sin_rows = sine[:, None, :]
    return jnp.concatenate(
        [first * cos_rows - second * sin_rows, second * cos_rows + first * sin_rows], axis=-1
    )


def two_softmax(logits):
    return jnp.concatenate(
        [jax.nn.softmax(logits, axis=-1), jax.nn.softmax(-logits, axis=-1)], axis=-1
    )


def split_parts(full_value):
    high_part = full_value.astype(jnp.bfloat16)
    rest_part = (full_value - high_part.astype(jnp.float32)).astype(jnp.bfloat16)
    return (high_part, rest_part)


def body(queries, keys, values, offsets, query_map, key_map, window_logit):
    tokens = queries.shape[0]
    heads = query_map.shape[0]
    head_dim = query_map.shape[1]
    feat = query_map.shape[2]
    kv_local = keys.shape[1] // head_dim
    group = heads // kv_local
    blocks = tokens // BLOCK
    extent = BLOCK + WINDOW
    positions = (offsets[:, None] + jnp.arange(SPAN, dtype=jnp.int32)[None, :]).reshape(tokens)
    cosine, sine = angle_tables(positions, head_dim // 2)
    rot_k = rotate(
        keys.reshape(tokens, kv_local, head_dim).astype(jnp.float32), cosine, sine
    ).astype(jnp.bfloat16)
    value_rows = values.reshape(tokens, kv_local, head_dim)
    tail_both = passed_along(
        jnp.concatenate([rot_k[tokens - WINDOW :], value_rows[tokens - WINDOW :]], axis=-1),
        "seq",
        1,
    )
    tail_keys = tail_both[..., :head_dim]
    tail_values = tail_both[..., head_dim:]
    ext_keys = jnp.concatenate([tail_keys, rot_k], axis=0)
    ext_values = jnp.concatenate([tail_values, value_rows], axis=0)
    valid = (jnp.arange(tokens + WINDOW) >= WINDOW) | (lax.axis_index("seq") > 0)
    grouped_map = key_map.reshape(kv_local, group, head_dim, feat)
    key_logits = jnp.einsum(
        "ngd,gkdf->ngkf", ext_keys, grouped_map, preferred_element_type=jnp.float32
    )
    phi_key = jnp.where(valid[:, None, None, None], two_softmax(key_logits), 0.0).astype(
        jnp.bfloat16
    )
    lag_phi = phi_key[:tokens].reshape(blocks, BLOCK, kv_local, group, 2 * feat)
    lag_values = ext_values[:tokens].reshape(blocks, BLOCK, kv_local, head_dim)
    block_states = jnp.einsum(
        "bjgkf,bjgd->bgkfd", lag_phi, lag_values, preferred_element_type=jnp.float32
    )
    block_norms = jnp.sum(lag_phi, axis=1, dtype=jnp.float32)
    total_state = jnp.sum(block_states, axis=0)
    total_norm = jnp.sum(block_norms, axis=0)
    before_state = jnp.concatenate(
        [jnp.zeros_like(block_states), jnp.cumsum(block_states, axis=0)[:-1]], axis=0
    )
    before_norm = jnp.concatenate(
        [jnp.zeros_like(block_norms), jnp.cumsum(block_norms, axis=0)[:-1]], axis=0
    )
    state_shape = total_state.shape
    state_size = total_state.size
    packed = jnp.concatenate([total_state.reshape(-1), total_norm.reshape(-1)])
    count = lax.axis_size("seq")
    shifts = []
    steps = 1
    while steps < count:
        shifts.append(steps)
        steps *= 2
    half = len(shifts) // 2 + 1
    orders = (shifts, shifts[half:] + shifts[:half])
    middle = packed.size // 2
    pieces = []
    for order, piece in zip(orders, (packed[:middle], packed[middle:])):
        inclusive = piece
        exclusive = jnp.zeros_like(piece)
        for place, shift in enumerate(order):
            received = passed_along(inclusive, "seq", shift)
            if not pieces and place == 0:
                first_received = received
            exclusive = exclusive + received
            if place + 1 < len(order):
                inclusive = inclusive + received
        pieces.append(exclusive)
    exclusive = jnp.concatenate(pieces)
    queries, first_received = lax.optimization_barrier((queries, first_received))
    rot_q = rotate(
        queries.reshape(tokens, heads, head_dim).astype(jnp.float32), cosine, sine
    ).astype(jnp.bfloat16)
    query_logits = jnp.einsum("nhd,hdf->nhf", rot_q, query_map, preferred_element_type=jnp.float32)
    phi_query = (
        two_softmax(query_logits).astype(jnp.bfloat16).reshape(tokens, kv_local, group, 2 * feat)
    )
    prior_state = exclusive[:state_size].reshape(state_shape)
    prior_norm = exclusive[state_size:].reshape(total_norm.shape)
    factor = jax.nn.sigmoid(window_logit).reshape(kv_local, group)
    rot_grouped = rot_q.reshape(tokens, kv_local, group, head_dim)
    row_index = jnp.arange(BLOCK)[:, None]
    col_index = jnp.arange(extent)[None, :]
    window_mask = (col_index > row_index) & (col_index <= row_index + WINDOW)
    linear_mask = col_index <= row_index
    live = valid[None, :]
    scores = jnp.einsum(
        "igkd,jgd->gkij", rot_grouped, ext_keys, preferred_element_type=jnp.float32
    ) / math.sqrt(head_dim)
    near_window = window_mask & live
    peak = jnp.max(jnp.where(near_window, scores, -jnp.inf), axis=-1, keepdims=True)
    weights = jnp.where(near_window, jnp.exp(scores - peak), 0.0)
    window_sum = jnp.sum(weights, axis=-1)
    affinity = jnp.einsum("igkf,jgkf->gkij", phi_query, phi_key, preferred_element_type=jnp.float32)
    affinity = jnp.where(linear_mask & live, affinity, 0.0)
    near_sum = jnp.sum(affinity, axis=-1)
    window_num = jnp.einsum(
        "gkij,jgd->igkd",
        weights.astype(jnp.bfloat16),
        ext_values,
        preferred_element_type=jnp.float32,
    )
    near_num = jnp.einsum(
        "gkij,jgd->igkd",
        affinity.astype(jnp.bfloat16),
        ext_values,
        preferred_element_type=jnp.float32,
    )
    state_now = prior_state + before_state[0]
    norm_now = prior_norm + before_norm[0]
    state_high, state_rest = split_parts(state_now)
    norm_high, norm_rest = split_parts(norm_now)
    far_num = jnp.einsum(
        "igkf,gkfd->igkd", phi_query, state_high, preferred_element_type=jnp.float32
    )
    far_num = far_num + jnp.einsum(
        "igkf,gkfd->igkd", phi_query, state_rest, preferred_element_type=jnp.float32
    )
    far_sum = jnp.einsum("igkf,gkf->igk", phi_query, norm_high, preferred_element_type=jnp.float32)
    far_sum = far_sum + jnp.einsum(
        "igkf,gkf->igk", phi_query, norm_rest, preferred_element_type=jnp.float32
    )
    head_factor = factor[None, :, :, None]
    numerator = head_factor * window_num + (1.0 - head_factor) * (near_num + far_num)
    denominator = factor[None] * jnp.transpose(window_sum, (2, 0, 1)) + (1.0 - factor[None]) * (
        jnp.transpose(near_sum, (2, 0, 1)) + far_sum
    )
    outputs = (numerator / denominator[..., None]).astype(jnp.bfloat16)
    result = outputs.reshape(tokens, heads * head_dim)
    return lax.all_to_all(result, "head", split_axis=0, concat_axis=1, tiled=True)


def solution(mesh):
    in_specs = (
        P("seq", "head"),
        P("seq", "head"),
        P("seq", "head"),
        P("seq"),
        P("head", None, None),
        P("head", None, None),
        P("head"),
    )
    out_specs = P(("seq", "head"), None)
    return jax.shard_map(body, mesh=mesh, in_specs=in_specs, out_specs=out_specs, check_vma=False)
```

```python
import math

import jax
import jax.numpy as jnp
from jax import lax
from jax.sharding import PartitionSpec as P

WINDOW = 64
BLOCK = 512
SPAN = 256


def passed_along(value, axis, steps):
    count = lax.axis_size(axis)
    first, last = (max(0, -steps), min(count, count - steps))
    return lax.ppermute(value, axis, [(source, source + steps) for source in range(first, last)])


def angle_tables(positions, half):
    frequency = [500000.0 ** (-float(order) / half) for order in range(half)]
    coarse = jnp.asarray([4096.0 * value % (2.0 * math.pi) for value in frequency], jnp.float32)
    medium = jnp.asarray([64.0 * value % (2.0 * math.pi) for value in frequency], jnp.float32)
    finest = jnp.asarray(frequency, jnp.float32)
    upper = (positions // 4096).astype(jnp.float32)[:, None] * coarse[None, :]
    middle = (positions // 64 % 64).astype(jnp.float32)[:, None] * medium[None, :]
    lower = (positions % 64).astype(jnp.float32)[:, None] * finest[None, :]
    cos_high = jnp.cos(upper) * jnp.cos(middle) - jnp.sin(upper) * jnp.sin(middle)
    sin_high = jnp.sin(upper) * jnp.cos(middle) + jnp.cos(upper) * jnp.sin(middle)
    cosine = cos_high * jnp.cos(lower) - sin_high * jnp.sin(lower)
    sine = sin_high * jnp.cos(lower) + cos_high * jnp.sin(lower)
    return (cosine, sine)


def rotate(rows, cosine, sine):
    half = rows.shape[-1] // 2
    first = rows[..., :half]
    second = rows[..., half:]
    cos_rows = cosine[:, None, :]
    sin_rows = sine[:, None, :]
    return jnp.concatenate(
        [first * cos_rows - second * sin_rows, second * cos_rows + first * sin_rows], axis=-1
    )


def two_softmax(logits):
    return jnp.concatenate(
        [jax.nn.softmax(logits, axis=-1), jax.nn.softmax(-logits, axis=-1)], axis=-1
    )


def split_parts(full_value):
    high_part = full_value.astype(jnp.bfloat16)
    rest_part = (full_value - high_part.astype(jnp.float32)).astype(jnp.bfloat16)
    return (high_part, rest_part)


def body(queries, keys, values, offsets, query_map, key_map, window_logit):
    tokens = queries.shape[0]
    heads = query_map.shape[0]
    head_dim = query_map.shape[1]
    feat = query_map.shape[2]
    kv_local = keys.shape[1] // head_dim
    group = heads // kv_local
    blocks = tokens // BLOCK
    extent = BLOCK + WINDOW
    positions = (offsets[:, None] + jnp.arange(SPAN, dtype=jnp.int32)[None, :]).reshape(tokens)
    cosine, sine = angle_tables(positions, head_dim // 2)
    rot_k = rotate(
        keys.reshape(tokens, kv_local, head_dim).astype(jnp.float32), cosine, sine
    ).astype(jnp.bfloat16)
    value_rows = values.reshape(tokens, kv_local, head_dim)
    tail_keys, tail_values = passed_along(
        (rot_k[tokens - WINDOW :], value_rows[tokens - WINDOW :]), "seq", 1
    )
    ext_keys = jnp.concatenate([tail_keys, rot_k], axis=0)
    ext_values = jnp.concatenate([tail_values, value_rows], axis=0)
    valid = (jnp.arange(tokens + WINDOW) >= WINDOW) | (lax.axis_index("seq") > 0)
    grouped_map = key_map.reshape(kv_local, group, head_dim, feat)
    key_logits = jnp.einsum(
        "ngd,gkdf->ngkf", ext_keys, grouped_map, preferred_element_type=jnp.float32
    )
    phi_key = jnp.where(valid[:, None, None, None], two_softmax(key_logits), 0.0).astype(
        jnp.bfloat16
    )
    lag_phi = phi_key[:tokens].reshape(blocks, BLOCK, kv_local, group, 2 * feat)
    lag_values = ext_values[:tokens].reshape(blocks, BLOCK, kv_local, head_dim)
    block_states = jnp.einsum(
        "bjgkf,bjgd->bgkfd", lag_phi, lag_values, preferred_element_type=jnp.float32
    )
    block_norms = jnp.sum(lag_phi, axis=1, dtype=jnp.float32)
    total_state = jnp.sum(block_states, axis=0)
    total_norm = jnp.sum(block_norms, axis=0)
    before_state = jnp.concatenate(
        [jnp.zeros_like(block_states), jnp.cumsum(block_states, axis=0)[:-1]], axis=0
    )
    before_norm = jnp.concatenate(
        [jnp.zeros_like(block_norms), jnp.cumsum(block_norms, axis=0)[:-1]], axis=0
    )
    half_heads = group // 2
    head_parts = (slice(0, half_heads), slice(half_heads, group))
    state_part_size = total_state[:, head_parts[0]].size
    halves = [
        jnp.concatenate(
            [total_state[:, part].reshape(-1), total_norm[:, part].reshape(-1)]
        )
        for part in head_parts
    ]
    count = lax.axis_size("seq")
    shifts = []
    steps = 1
    while steps < count:
        shifts.append(steps)
        steps *= 2
    half = len(shifts) // 2 + 1
    orders = (shifts, shifts[half:] + shifts[:half])
    pieces = []
    for order, piece in zip(orders, halves):
        inclusive = piece
        exclusive = jnp.zeros_like(piece)
        for place, shift in enumerate(order):
            received = passed_along(inclusive, "seq", shift)
            if not pieces and place == 0:
                first_received = received
            if pieces and place + 1 == len(order):
                held = received
            else:
                exclusive = exclusive + received
            if place + 1 < len(order):
                inclusive = inclusive + received
        pieces.append(exclusive)
    queries, first_received = lax.optimization_barrier((queries, first_received))
    rot_q = rotate(
        queries.reshape(tokens, heads, head_dim).astype(jnp.float32), cosine, sine
    ).astype(jnp.bfloat16)
    query_logits = jnp.einsum("nhd,hdf->nhf", rot_q, query_map, preferred_element_type=jnp.float32)
    phi_query = (
        two_softmax(query_logits).astype(jnp.bfloat16).reshape(tokens, kv_local, group, 2 * feat)
    )
    factor = jax.nn.sigmoid(window_logit).reshape(kv_local, group)
    rot_grouped = rot_q.reshape(tokens, kv_local, group, head_dim)
    row_index = jnp.arange(BLOCK)[:, None]
    col_index = jnp.arange(extent)[None, :]
    window_mask = (col_index > row_index) & (col_index <= row_index + WINDOW)
    linear_mask = col_index <= row_index
    live = valid[None, :]
    scores = jnp.einsum(
        "igkd,jgd->gkij", rot_grouped, ext_keys, preferred_element_type=jnp.float32
    ) / math.sqrt(head_dim)
    near_window = window_mask & live
    peak = jnp.max(jnp.where(near_window, scores, -jnp.inf), axis=-1, keepdims=True)
    weights = jnp.where(near_window, jnp.exp(scores - peak), 0.0)
    window_sum = jnp.sum(weights, axis=-1)
    affinity = jnp.einsum("igkf,jgkf->gkij", phi_query, phi_key, preferred_element_type=jnp.float32)
    affinity = jnp.where(linear_mask & live, affinity, 0.0)
    near_sum = jnp.sum(affinity, axis=-1)
    window_num = jnp.einsum(
        "gkij,jgd->igkd",
        weights.astype(jnp.bfloat16),
        ext_values,
        preferred_element_type=jnp.float32,
    )
    near_num = jnp.einsum(
        "gkij,jgd->igkd",
        affinity.astype(jnp.bfloat16),
        ext_values,
        preferred_element_type=jnp.float32,
    )
    head_factor = factor[None, :, :, None]
    window_sum_rows = jnp.transpose(window_sum, (2, 0, 1))
    near_sum_rows = jnp.transpose(near_sum, (2, 0, 1))
    sent = []
    for part, exclusive in zip(head_parts, pieces):
        if sent:
            sent[0], held = lax.optimization_barrier((sent[0], held))
            exclusive = exclusive + held
        prior_state = exclusive[:state_part_size].reshape(total_state[:, part].shape)
        prior_norm = exclusive[state_part_size:].reshape(total_norm[:, part].shape)
        state_now = prior_state + before_state[0][:, part]
        norm_now = prior_norm + before_norm[0][:, part]
        state_high, state_rest = split_parts(state_now)
        norm_high, norm_rest = split_parts(norm_now)
        phi_part = phi_query[:, :, part]
        far_num = jnp.einsum(
            "igkf,gkfd->igkd", phi_part, state_high, preferred_element_type=jnp.float32
        )
        far_num = far_num + jnp.einsum(
            "igkf,gkfd->igkd", phi_part, state_rest, preferred_element_type=jnp.float32
        )
        far_sum = jnp.einsum("igkf,gkf->igk", phi_part, norm_high, preferred_element_type=jnp.float32)
        far_sum = far_sum + jnp.einsum(
            "igkf,gkf->igk", phi_part, norm_rest, preferred_element_type=jnp.float32
        )
        part_factor = head_factor[:, :, part]
        numerator = part_factor * window_num[:, :, part] + (1.0 - part_factor) * (
            near_num[:, :, part] + far_num
        )
        denominator = factor[None][:, :, part] * window_sum_rows[:, :, part] + (
            1.0 - factor[None][:, :, part]
        ) * (near_sum_rows[:, :, part] + far_sum)
        outputs = (numerator / denominator[..., None]).astype(jnp.bfloat16)
        result = outputs.reshape(tokens, -1)
        moved = lax.all_to_all(result, "head", split_axis=0, concat_axis=1, tiled=True)
        sent.append(moved.reshape(moved.shape[0], lax.axis_size("head"), -1))
    joined = jnp.concatenate(sent, axis=-1)
    return joined.reshape(joined.shape[0], -1)


def solution(mesh):
    in_specs = (
        P("seq", "head"),
        P("seq", "head"),
        P("seq", "head"),
        P("seq"),
        P("head", None, None),
        P("head", None, None),
        P("head"),
    )
    out_specs = P(("seq", "head"), None)
    return jax.shard_map(body, mesh=mesh, in_specs=in_specs, out_specs=out_specs, check_vma=False)
```

```python
import math

import jax
import jax.numpy as jnp
from jax import lax
from jax.experimental import pallas as pl
from jax.sharding import PartitionSpec as P

WINDOW = 64
BLOCK = 512
SPAN = 256


def passed_along(value, axis, steps):
    count = lax.axis_size(axis)
    first, last = (max(0, -steps), min(count, count - steps))
    return lax.ppermute(value, axis, [(source, source + steps) for source in range(first, last)])


def angle_tables(positions, half):
    frequency = [500000.0 ** (-float(order) / half) for order in range(half)]
    coarse = jnp.asarray([4096.0 * value % (2.0 * math.pi) for value in frequency], jnp.float32)
    medium = jnp.asarray([64.0 * value % (2.0 * math.pi) for value in frequency], jnp.float32)
    finest = jnp.asarray(frequency, jnp.float32)
    upper = (positions // 4096).astype(jnp.float32)[:, None] * coarse[None, :]
    middle = (positions // 64 % 64).astype(jnp.float32)[:, None] * medium[None, :]
    lower = (positions % 64).astype(jnp.float32)[:, None] * finest[None, :]
    cos_high = jnp.cos(upper) * jnp.cos(middle) - jnp.sin(upper) * jnp.sin(middle)
    sin_high = jnp.sin(upper) * jnp.cos(middle) + jnp.cos(upper) * jnp.sin(middle)
    cosine = cos_high * jnp.cos(lower) - sin_high * jnp.sin(lower)
    sine = sin_high * jnp.cos(lower) + cos_high * jnp.sin(lower)
    return (cosine, sine)


def rotate(rows, cosine, sine):
    half = rows.shape[-1] // 2
    first = rows[..., :half]
    second = rows[..., half:]
    cos_rows = cosine[:, None, :]
    sin_rows = sine[:, None, :]
    return jnp.concatenate(
        [first * cos_rows - second * sin_rows, second * cos_rows + first * sin_rows], axis=-1
    )


def two_softmax(logits):
    return jnp.concatenate(
        [jax.nn.softmax(logits, axis=-1), jax.nn.softmax(-logits, axis=-1)], axis=-1
    )


def split_parts(full_value):
    high_part = full_value.astype(jnp.bfloat16)
    rest_part = (full_value - high_part.astype(jnp.float32)).astype(jnp.bfloat16)
    return (high_part, rest_part)


def key_features(ext_keys2, key_map, ext_values2, mask, lag):
    rows, dim = ext_keys2.shape
    heads, _, feat = key_map.shape

    def kernel(k_ref, m_ref, v_ref, mask_ref, phi_ref, st_ref, nm_ref):
        logits = jnp.dot(k_ref[...], m_ref[0], preferred_element_type=jnp.float32)
        live = mask_ref[...] > 0.0
        values = v_ref[0:lag, :]
        for place, sign in enumerate((1.0, -1.0)):
            shifted = sign * logits
            expo = jnp.exp(shifted - jnp.max(shifted, axis=-1, keepdims=True))
            soft = expo / jnp.sum(expo, axis=-1, keepdims=True)
            phi = jnp.where(live, soft, 0.0).astype(jnp.bfloat16)
            cols = slice(place * feat, (place + 1) * feat)
            phi_ref[0, :, cols] = phi
            lagged = phi[0:lag, :]
            st_ref[0, cols, :] = lax.dot_general(
                lagged, values, (((0,), (0,)), ((), ())), preferred_element_type=jnp.float32
            )
            nm_ref[0, :, cols] = jnp.sum(lagged.astype(jnp.float32), axis=0, keepdims=True)

    return pl.pallas_call(
        kernel,
        grid=(heads,),
        in_specs=[
            pl.BlockSpec((rows, dim), lambda h: (0, 0)),
            pl.BlockSpec((1, dim, feat), lambda h: (h, 0, 0)),
            pl.BlockSpec((rows, dim), lambda h: (0, 0)),
            pl.BlockSpec((rows, 1), lambda h: (0, 0)),
        ],
        out_specs=[
            pl.BlockSpec((1, rows, 2 * feat), lambda h: (h, 0, 0)),
            pl.BlockSpec((1, 2 * feat, dim), lambda h: (h, 0, 0)),
            pl.BlockSpec((1, 1, 2 * feat), lambda h: (h, 0, 0)),
        ],
        out_shape=[
            jax.ShapeDtypeStruct((heads, rows, 2 * feat), jnp.bfloat16),
            jax.ShapeDtypeStruct((heads, 2 * feat, dim), jnp.float32),
            jax.ShapeDtypeStruct((heads, 1, 2 * feat), jnp.float32),
        ],
    )(ext_keys2, key_map, ext_values2, mask)


def body(queries, keys, values, offsets, query_map, key_map, window_logit):
    tokens = queries.shape[0]
    heads = query_map.shape[0]
    head_dim = query_map.shape[1]
    feat = query_map.shape[2]
    kv_local = keys.shape[1] // head_dim
    group = heads // kv_local
    blocks = tokens // BLOCK
    extent = BLOCK + WINDOW
    positions = (offsets[:, None] + jnp.arange(SPAN, dtype=jnp.int32)[None, :]).reshape(tokens)
    cosine, sine = angle_tables(positions, head_dim // 2)
    rot_k = rotate(
        keys.reshape(tokens, kv_local, head_dim).astype(jnp.float32), cosine, sine
    ).astype(jnp.bfloat16)
    value_rows = values.reshape(tokens, kv_local, head_dim)
    tail_keys, tail_values = passed_along(
        (rot_k[tokens - WINDOW :], value_rows[tokens - WINDOW :]), "seq", 1
    )
    ext_keys = jnp.concatenate([tail_keys, rot_k], axis=0)
    ext_values = jnp.concatenate([tail_values, value_rows], axis=0)
    valid = (jnp.arange(tokens + WINDOW) >= WINDOW) | (lax.axis_index("seq") > 0)
    ext_rows = tokens + WINDOW
    phi_heads, state_heads, norm_heads = key_features(
        ext_keys.reshape(ext_rows, head_dim),
        key_map,
        ext_values.reshape(ext_rows, head_dim),
        valid.astype(jnp.float32)[:, None],
        tokens,
    )
    phi_key = phi_heads.reshape(kv_local, group, ext_rows, 2 * feat)
    block_states = state_heads.reshape(1, kv_local, group, 2 * feat, head_dim)
    block_norms = norm_heads.reshape(1, kv_local, group, 2 * feat)
    total_state = jnp.sum(block_states, axis=0)
    total_norm = jnp.sum(block_norms, axis=0)
    before_state = jnp.concatenate(
        [jnp.zeros_like(block_states), jnp.cumsum(block_states, axis=0)[:-1]], axis=0
    )
    before_norm = jnp.concatenate(
        [jnp.zeros_like(block_norms), jnp.cumsum(block_norms, axis=0)[:-1]], axis=0
    )
    state_shape = total_state.shape
    state_size = total_state.size
    packed = jnp.concatenate([total_state.reshape(-1), total_norm.reshape(-1)])
    count = lax.axis_size("seq")
    shifts = []
    steps = 1
    while steps < count:
        shifts.append(steps)
        steps *= 2
    half = len(shifts) // 2 + 1
    orders = (shifts, shifts[half:] + shifts[:half])
    middle = packed.size // 2
    pieces = []
    for order, piece in zip(orders, (packed[:middle], packed[middle:])):
        inclusive = piece
        exclusive = jnp.zeros_like(piece)
        for place, shift in enumerate(order):
            received = passed_along(inclusive, "seq", shift)
            if not pieces and place == 0:
                first_received = received
            exclusive = exclusive + received
            if place + 1 < len(order):
                inclusive = inclusive + received
        pieces.append(exclusive)
    exclusive = jnp.concatenate(pieces)
    queries, first_received = lax.optimization_barrier((queries, first_received))
    rot_q = rotate(
        queries.reshape(tokens, heads, head_dim).astype(jnp.float32), cosine, sine
    ).astype(jnp.bfloat16)
    query_logits = jnp.einsum("nhd,hdf->nhf", rot_q, query_map, preferred_element_type=jnp.float32)
    phi_query = (
        two_softmax(query_logits).astype(jnp.bfloat16).reshape(tokens, kv_local, group, 2 * feat)
    )
    prior_state = exclusive[:state_size].reshape(state_shape)
    prior_norm = exclusive[state_size:].reshape(total_norm.shape)
    factor = jax.nn.sigmoid(window_logit).reshape(kv_local, group)
    rot_grouped = rot_q.reshape(tokens, kv_local, group, head_dim)
    row_index = jnp.arange(BLOCK)[:, None]
    col_index = jnp.arange(extent)[None, :]
    window_mask = (col_index > row_index) & (col_index <= row_index + WINDOW)
    linear_mask = col_index <= row_index
    live = valid[None, :]
    scores = jnp.einsum(
        "igkd,jgd->gkij", rot_grouped, ext_keys, preferred_element_type=jnp.float32
    ) / math.sqrt(head_dim)
    near_window = window_mask & live
    peak = jnp.max(jnp.where(near_window, scores, -jnp.inf), axis=-1, keepdims=True)
    weights = jnp.where(near_window, jnp.exp(scores - peak), 0.0)
    window_sum = jnp.sum(weights, axis=-1)
    affinity = jnp.einsum("igkf,gkjf->gkij", phi_query, phi_key, preferred_element_type=jnp.float32)
    affinity = jnp.where(linear_mask & live, affinity, 0.0)
    near_sum = jnp.sum(affinity, axis=-1)
    window_num = jnp.einsum(
        "gkij,jgd->igkd",
        weights.astype(jnp.bfloat16),
        ext_values,
        preferred_element_type=jnp.float32,
    )
    near_num = jnp.einsum(
        "gkij,jgd->igkd",
        affinity.astype(jnp.bfloat16),
        ext_values,
        preferred_element_type=jnp.float32,
    )
    state_now = prior_state + before_state[0]
    norm_now = prior_norm + before_norm[0]
    state_high, state_rest = split_parts(state_now)
    norm_high, norm_rest = split_parts(norm_now)
    far_num = jnp.einsum(
        "igkf,gkfd->igkd", phi_query, state_high, preferred_element_type=jnp.float32
    )
    far_num = far_num + jnp.einsum(
        "igkf,gkfd->igkd", phi_query, state_rest, preferred_element_type=jnp.float32
    )
    far_sum = jnp.einsum("igkf,gkf->igk", phi_query, norm_high, preferred_element_type=jnp.float32)
    far_sum = far_sum + jnp.einsum(
        "igkf,gkf->igk", phi_query, norm_rest, preferred_element_type=jnp.float32
    )
    head_factor = factor[None, :, :, None]
    numerator = head_factor * window_num + (1.0 - head_factor) * (near_num + far_num)
    denominator = factor[None] * jnp.transpose(window_sum, (2, 0, 1)) + (1.0 - factor[None]) * (
        jnp.transpose(near_sum, (2, 0, 1)) + far_sum
    )
    outputs = (numerator / denominator[..., None]).astype(jnp.bfloat16)
    result = outputs.reshape(tokens, heads * head_dim)
    return lax.all_to_all(result, "head", split_axis=0, concat_axis=1, tiled=True)


def solution(mesh):
    in_specs = (
        P("seq", "head"),
        P("seq", "head"),
        P("seq", "head"),
        P("seq"),
        P("head", None, None),
        P("head", None, None),
        P("head"),
    )
    out_specs = P(("seq", "head"), None)
    return jax.shard_map(body, mesh=mesh, in_specs=in_specs, out_specs=out_specs, check_vma=False)
```

```python
import math

import jax
import jax.numpy as jnp
from jax import lax
from jax.experimental import pallas as pl
from jax.sharding import PartitionSpec as P

WINDOW = 64
BLOCK = 512
SPAN = 256


def passed_along(value, axis, steps):
    count = lax.axis_size(axis)
    first, last = (max(0, -steps), min(count, count - steps))
    return lax.ppermute(value, axis, [(source, source + steps) for source in range(first, last)])


def angle_tables(positions, half):
    frequency = [500000.0 ** (-float(order) / half) for order in range(half)]
    coarse = jnp.asarray([4096.0 * value % (2.0 * math.pi) for value in frequency], jnp.float32)
    medium = jnp.asarray([64.0 * value % (2.0 * math.pi) for value in frequency], jnp.float32)
    finest = jnp.asarray(frequency, jnp.float32)
    upper = (positions // 4096).astype(jnp.float32)[:, None] * coarse[None, :]
    middle = (positions // 64 % 64).astype(jnp.float32)[:, None] * medium[None, :]
    lower = (positions % 64).astype(jnp.float32)[:, None] * finest[None, :]
    cos_high = jnp.cos(upper) * jnp.cos(middle) - jnp.sin(upper) * jnp.sin(middle)
    sin_high = jnp.sin(upper) * jnp.cos(middle) + jnp.cos(upper) * jnp.sin(middle)
    cosine = cos_high * jnp.cos(lower) - sin_high * jnp.sin(lower)
    sine = sin_high * jnp.cos(lower) + cos_high * jnp.sin(lower)
    return (cosine, sine)


def rotate(rows, cosine, sine):
    half = rows.shape[-1] // 2
    first = rows[..., :half]
    second = rows[..., half:]
    cos_rows = cosine[:, None, :]
    sin_rows = sine[:, None, :]
    return jnp.concatenate(
        [first * cos_rows - second * sin_rows, second * cos_rows + first * sin_rows], axis=-1
    )


def two_softmax(logits):
    return jnp.concatenate(
        [jax.nn.softmax(logits, axis=-1), jax.nn.softmax(-logits, axis=-1)], axis=-1
    )


def split_parts(full_value):
    high_part = full_value.astype(jnp.bfloat16)
    rest_part = (full_value - high_part.astype(jnp.float32)).astype(jnp.bfloat16)
    return (high_part, rest_part)


def key_features(ext_keys2, key_map, ext_values2, mask, lag):
    rows, dim = ext_keys2.shape
    heads, _, feat = key_map.shape

    def kernel(k_ref, m_ref, v_ref, mask_ref, phi_ref, st_ref, nm_ref):
        keys = k_ref[...]
        live = mask_ref[...] > 0.0
        values = v_ref[0:lag, :]
        for head in range(heads):
            logits = jnp.dot(keys, m_ref[head], preferred_element_type=jnp.float32)
            for place, sign in enumerate((1.0, -1.0)):
                shifted = sign * logits
                expo = jnp.exp(shifted - jnp.max(shifted, axis=-1, keepdims=True))
                soft = expo / jnp.sum(expo, axis=-1, keepdims=True)
                phi = jnp.where(live, soft, 0.0).astype(jnp.bfloat16)
                cols = slice(place * feat, (place + 1) * feat)
                phi_ref[head, :, cols] = phi
                lagged = phi[0:lag, :]
                st_ref[head, cols, :] = lax.dot_general(
                    lagged, values, (((0,), (0,)), ((), ())), preferred_element_type=jnp.float32
                )
                nm_ref[head, :, cols] = jnp.sum(lagged.astype(jnp.float32), axis=0, keepdims=True)

    return pl.pallas_call(
        kernel,
        grid=(1,),
        in_specs=[
            pl.BlockSpec((rows, dim), lambda h: (0, 0)),
            pl.BlockSpec((heads, dim, feat), lambda h: (0, 0, 0)),
            pl.BlockSpec((rows, dim), lambda h: (0, 0)),
            pl.BlockSpec((rows, 1), lambda h: (0, 0)),
        ],
        out_specs=[
            pl.BlockSpec((heads, rows, 2 * feat), lambda h: (0, 0, 0)),
            pl.BlockSpec((heads, 2 * feat, dim), lambda h: (0, 0, 0)),
            pl.BlockSpec((heads, 1, 2 * feat), lambda h: (0, 0, 0)),
        ],
        out_shape=[
            jax.ShapeDtypeStruct((heads, rows, 2 * feat), jnp.bfloat16),
            jax.ShapeDtypeStruct((heads, 2 * feat, dim), jnp.float32),
            jax.ShapeDtypeStruct((heads, 1, 2 * feat), jnp.float32),
        ],
    )(ext_keys2, key_map, ext_values2, mask)


def body(queries, keys, values, offsets, query_map, key_map, window_logit):
    tokens = queries.shape[0]
    heads = query_map.shape[0]
    head_dim = query_map.shape[1]
    feat = query_map.shape[2]
    kv_local = keys.shape[1] // head_dim
    group = heads // kv_local
    blocks = tokens // BLOCK
    extent = BLOCK + WINDOW
    positions = (offsets[:, None] + jnp.arange(SPAN, dtype=jnp.int32)[None, :]).reshape(tokens)
    cosine, sine = angle_tables(positions, head_dim // 2)
    rot_k = rotate(
        keys.reshape(tokens, kv_local, head_dim).astype(jnp.float32), cosine, sine
    ).astype(jnp.bfloat16)
    value_rows = values.reshape(tokens, kv_local, head_dim)
    tail_keys, tail_values = passed_along(
        (rot_k[tokens - WINDOW :], value_rows[tokens - WINDOW :]), "seq", 1
    )
    ext_keys = jnp.concatenate([tail_keys, rot_k], axis=0)
    ext_values = jnp.concatenate([tail_values, value_rows], axis=0)
    valid = (jnp.arange(tokens + WINDOW) >= WINDOW) | (lax.axis_index("seq") > 0)
    ext_rows = tokens + WINDOW
    phi_heads, state_heads, norm_heads = key_features(
        ext_keys.reshape(ext_rows, head_dim),
        key_map,
        ext_values.reshape(ext_rows, head_dim),
        valid.astype(jnp.float32)[:, None],
        tokens,
    )
    phi_key = phi_heads.reshape(kv_local, group, ext_rows, 2 * feat)
    block_states = state_heads.reshape(1, kv_local, group, 2 * feat, head_dim)
    block_norms = norm_heads.reshape(1, kv_local, group, 2 * feat)
    total_state = jnp.sum(block_states, axis=0)
    total_norm = jnp.sum(block_norms, axis=0)
    before_state = jnp.concatenate(
        [jnp.zeros_like(block_states), jnp.cumsum(block_states, axis=0)[:-1]], axis=0
    )
    before_norm = jnp.concatenate(
        [jnp.zeros_like(block_norms), jnp.cumsum(block_norms, axis=0)[:-1]], axis=0
    )
    state_shape = total_state.shape
    state_size = total_state.size
    packed = jnp.concatenate([total_state.reshape(-1), total_norm.reshape(-1)])
    count = lax.axis_size("seq")
    shifts = []
    steps = 1
    while steps < count:
        shifts.append(steps)
        steps *= 2
    half = len(shifts) // 2 + 1
    orders = (shifts, shifts[half:] + shifts[:half])
    middle = packed.size // 2
    pieces = []
    for order, piece in zip(orders, (packed[:middle], packed[middle:])):
        inclusive = piece
        exclusive = jnp.zeros_like(piece)
        for place, shift in enumerate(order):
            received = passed_along(inclusive, "seq", shift)
            if not pieces and place == 0:
                first_received = received
            exclusive = exclusive + received
            if place + 1 < len(order):
                inclusive = inclusive + received
        pieces.append(exclusive)
    exclusive = jnp.concatenate(pieces)
    queries, first_received = lax.optimization_barrier((queries, first_received))
    rot_q = rotate(
        queries.reshape(tokens, heads, head_dim).astype(jnp.float32), cosine, sine
    ).astype(jnp.bfloat16)
    query_logits = jnp.einsum("nhd,hdf->nhf", rot_q, query_map, preferred_element_type=jnp.float32)
    phi_query = (
        two_softmax(query_logits).astype(jnp.bfloat16).reshape(tokens, kv_local, group, 2 * feat)
    )
    prior_state = exclusive[:state_size].reshape(state_shape)
    prior_norm = exclusive[state_size:].reshape(total_norm.shape)
    factor = jax.nn.sigmoid(window_logit).reshape(kv_local, group)
    rot_grouped = rot_q.reshape(tokens, kv_local, group, head_dim)
    row_index = jnp.arange(BLOCK)[:, None]
    col_index = jnp.arange(extent)[None, :]
    window_mask = (col_index > row_index) & (col_index <= row_index + WINDOW)
    linear_mask = col_index <= row_index
    live = valid[None, :]
    scores = jnp.einsum(
        "igkd,jgd->gkij", rot_grouped, ext_keys, preferred_element_type=jnp.float32
    ) / math.sqrt(head_dim)
    near_window = window_mask & live
    peak = jnp.max(jnp.where(near_window, scores, -jnp.inf), axis=-1, keepdims=True)
    weights = jnp.where(near_window, jnp.exp(scores - peak), 0.0)
    window_sum = jnp.sum(weights, axis=-1)
    affinity = jnp.einsum("igkf,gkjf->gkij", phi_query, phi_key, preferred_element_type=jnp.float32)
    affinity = jnp.where(linear_mask & live, affinity, 0.0)
    near_sum = jnp.sum(affinity, axis=-1)
    window_num = jnp.einsum(
        "gkij,jgd->igkd",
        weights.astype(jnp.bfloat16),
        ext_values,
        preferred_element_type=jnp.float32,
    )
    near_num = jnp.einsum(
        "gkij,jgd->igkd",
        affinity.astype(jnp.bfloat16),
        ext_values,
        preferred_element_type=jnp.float32,
    )
    state_now = prior_state + before_state[0]
    norm_now = prior_norm + before_norm[0]
    state_high, state_rest = split_parts(state_now)
    norm_high, norm_rest = split_parts(norm_now)
    far_num = jnp.einsum(
        "igkf,gkfd->igkd", phi_query, state_high, preferred_element_type=jnp.float32
    )
    far_num = far_num + jnp.einsum(
        "igkf,gkfd->igkd", phi_query, state_rest, preferred_element_type=jnp.float32
    )
    far_sum = jnp.einsum("igkf,gkf->igk", phi_query, norm_high, preferred_element_type=jnp.float32)
    far_sum = far_sum + jnp.einsum(
        "igkf,gkf->igk", phi_query, norm_rest, preferred_element_type=jnp.float32
    )
    head_factor = factor[None, :, :, None]
    numerator = head_factor * window_num + (1.0 - head_factor) * (near_num + far_num)
    denominator = factor[None] * jnp.transpose(window_sum, (2, 0, 1)) + (1.0 - factor[None]) * (
        jnp.transpose(near_sum, (2, 0, 1)) + far_sum
    )
    outputs = (numerator / denominator[..., None]).astype(jnp.bfloat16)
    result = outputs.reshape(tokens, heads * head_dim)
    return lax.all_to_all(result, "head", split_axis=0, concat_axis=1, tiled=True)


def solution(mesh):
    in_specs = (
        P("seq", "head"),
        P("seq", "head"),
        P("seq", "head"),
        P("seq"),
        P("head", None, None),
        P("head", None, None),
        P("head"),
    )
    out_specs = P(("seq", "head"), None)
    return jax.shard_map(body, mesh=mesh, in_specs=in_specs, out_specs=out_specs, check_vma=False)
```

```python
import math

import jax
import jax.numpy as jnp
from jax import lax
from jax.experimental import pallas as pl
from jax.sharding import PartitionSpec as P

WINDOW = 64
BLOCK = 512
SPAN = 256


def passed_along(value, axis, steps):
    count = lax.axis_size(axis)
    first, last = (max(0, -steps), min(count, count - steps))
    return lax.ppermute(value, axis, [(source, source + steps) for source in range(first, last)])


def angle_tables(positions, half):
    frequency = [500000.0 ** (-float(order) / half) for order in range(half)]
    coarse = jnp.asarray([4096.0 * value % (2.0 * math.pi) for value in frequency], jnp.float32)
    medium = jnp.asarray([64.0 * value % (2.0 * math.pi) for value in frequency], jnp.float32)
    finest = jnp.asarray(frequency, jnp.float32)
    upper = (positions // 4096).astype(jnp.float32)[:, None] * coarse[None, :]
    middle = (positions // 64 % 64).astype(jnp.float32)[:, None] * medium[None, :]
    lower = (positions % 64).astype(jnp.float32)[:, None] * finest[None, :]
    cos_high = jnp.cos(upper) * jnp.cos(middle) - jnp.sin(upper) * jnp.sin(middle)
    sin_high = jnp.sin(upper) * jnp.cos(middle) + jnp.cos(upper) * jnp.sin(middle)
    cosine = cos_high * jnp.cos(lower) - sin_high * jnp.sin(lower)
    sine = sin_high * jnp.cos(lower) + cos_high * jnp.sin(lower)
    return (cosine, sine)


def rotate(rows, cosine, sine):
    half = rows.shape[-1] // 2
    first = rows[..., :half]
    second = rows[..., half:]
    cos_rows = cosine[:, None, :]
    sin_rows = sine[:, None, :]
    return jnp.concatenate(
        [first * cos_rows - second * sin_rows, second * cos_rows + first * sin_rows], axis=-1
    )


def two_softmax(logits):
    return jnp.concatenate(
        [jax.nn.softmax(logits, axis=-1), jax.nn.softmax(-logits, axis=-1)], axis=-1
    )


def split_parts(full_value):
    high_part = full_value.astype(jnp.bfloat16)
    rest_part = (full_value - high_part.astype(jnp.float32)).astype(jnp.bfloat16)
    return (high_part, rest_part)


def key_features(ext_keys2, key_map_t, ext_values2, mask, lag):
    rows, dim = ext_keys2.shape
    heads, feat, _ = key_map_t.shape

    def kernel(k_ref, m_ref, v_ref, mask_ref, phi_ref, st_ref, nm_ref):
        keys = k_ref[...]
        live = mask_ref[...] > 0.0
        values = v_ref[0:lag, :]
        for head in range(heads):
            logits = lax.dot_general(
                m_ref[head], keys, (((1,), (1,)), ((), ())), preferred_element_type=jnp.float32
            )
            for place, sign in enumerate((1.0, -1.0)):
                shifted = sign * logits
                expo = jnp.exp(shifted - jnp.max(shifted, axis=0, keepdims=True))
                soft = expo / jnp.sum(expo, axis=0, keepdims=True)
                phi = jnp.where(live, soft, 0.0).astype(jnp.bfloat16)
                band = slice(place * feat, (place + 1) * feat)
                phi_ref[head, band, :] = phi
                lagged = phi[:, 0:lag]
                st_ref[head, band, :] = jnp.dot(lagged, values, preferred_element_type=jnp.float32)
                nm_ref[head, band, :] = jnp.sum(lagged.astype(jnp.float32), axis=1, keepdims=True)

    return pl.pallas_call(
        kernel,
        grid=(1,),
        in_specs=[
            pl.BlockSpec((rows, dim), lambda h: (0, 0)),
            pl.BlockSpec((heads, feat, dim), lambda h: (0, 0, 0)),
            pl.BlockSpec((rows, dim), lambda h: (0, 0)),
            pl.BlockSpec((1, rows), lambda h: (0, 0)),
        ],
        out_specs=[
            pl.BlockSpec((heads, 2 * feat, rows), lambda h: (0, 0, 0)),
            pl.BlockSpec((heads, 2 * feat, dim), lambda h: (0, 0, 0)),
            pl.BlockSpec((heads, 2 * feat, 1), lambda h: (0, 0, 0)),
        ],
        out_shape=[
            jax.ShapeDtypeStruct((heads, 2 * feat, rows), jnp.bfloat16),
            jax.ShapeDtypeStruct((heads, 2 * feat, dim), jnp.float32),
            jax.ShapeDtypeStruct((heads, 2 * feat, 1), jnp.float32),
        ],
    )(ext_keys2, key_map_t, ext_values2, mask)

def body(queries, keys, values, offsets, query_map, key_map, window_logit):
    tokens = queries.shape[0]
    heads = query_map.shape[0]
    head_dim = query_map.shape[1]
    feat = query_map.shape[2]
    kv_local = keys.shape[1] // head_dim
    group = heads // kv_local
    blocks = tokens // BLOCK
    extent = BLOCK + WINDOW
    positions = (offsets[:, None] + jnp.arange(SPAN, dtype=jnp.int32)[None, :]).reshape(tokens)
    cosine, sine = angle_tables(positions, head_dim // 2)
    rot_k = rotate(
        keys.reshape(tokens, kv_local, head_dim).astype(jnp.float32), cosine, sine
    ).astype(jnp.bfloat16)
    value_rows = values.reshape(tokens, kv_local, head_dim)
    tail_keys, tail_values = passed_along(
        (rot_k[tokens - WINDOW :], value_rows[tokens - WINDOW :]), "seq", 1
    )
    ext_keys = jnp.concatenate([tail_keys, rot_k], axis=0)
    ext_values = jnp.concatenate([tail_values, value_rows], axis=0)
    valid = (jnp.arange(tokens + WINDOW) >= WINDOW) | (lax.axis_index("seq") > 0)
    ext_rows = tokens + WINDOW
    phi_heads, state_heads, norm_heads = key_features(
        ext_keys.reshape(ext_rows, head_dim),
        jnp.transpose(key_map, (0, 2, 1)),
        ext_values.reshape(ext_rows, head_dim),
        valid.astype(jnp.float32)[None, :],
        tokens,
    )
    phi_key = phi_heads.reshape(kv_local, group, 2 * feat, ext_rows)
    block_states = state_heads.reshape(1, kv_local, group, 2 * feat, head_dim)
    block_norms = norm_heads.reshape(1, kv_local, group, 2 * feat)
    total_state = jnp.sum(block_states, axis=0)
    total_norm = jnp.sum(block_norms, axis=0)
    before_state = jnp.concatenate(
        [jnp.zeros_like(block_states), jnp.cumsum(block_states, axis=0)[:-1]], axis=0
    )
    before_norm = jnp.concatenate(
        [jnp.zeros_like(block_norms), jnp.cumsum(block_norms, axis=0)[:-1]], axis=0
    )
    state_shape = total_state.shape
    state_size = total_state.size
    packed = jnp.concatenate([total_state.reshape(-1), total_norm.reshape(-1)])
    count = lax.axis_size("seq")
    shifts = []
    steps = 1
    while steps < count:
        shifts.append(steps)
        steps *= 2
    half = len(shifts) // 2 + 1
    orders = (shifts, shifts[half:] + shifts[:half])
    middle = packed.size // 2
    pieces = []
    for order, piece in zip(orders, (packed[:middle], packed[middle:])):
        inclusive = piece
        exclusive = jnp.zeros_like(piece)
        for place, shift in enumerate(order):
            received = passed_along(inclusive, "seq", shift)
            if not pieces and place == 0:
                first_received = received
            exclusive = exclusive + received
            if place + 1 < len(order):
                inclusive = inclusive + received
        pieces.append(exclusive)
    exclusive = jnp.concatenate(pieces)
    queries, first_received = lax.optimization_barrier((queries, first_received))
    rot_q = rotate(
        queries.reshape(tokens, heads, head_dim).astype(jnp.float32), cosine, sine
    ).astype(jnp.bfloat16)
    query_logits = jnp.einsum("nhd,hdf->nhf", rot_q, query_map, preferred_element_type=jnp.float32)
    phi_query = (
        two_softmax(query_logits).astype(jnp.bfloat16).reshape(tokens, kv_local, group, 2 * feat)
    )
    prior_state = exclusive[:state_size].reshape(state_shape)
    prior_norm = exclusive[state_size:].reshape(total_norm.shape)
    factor = jax.nn.sigmoid(window_logit).reshape(kv_local, group)
    rot_grouped = rot_q.reshape(tokens, kv_local, group, head_dim)
    row_index = jnp.arange(BLOCK)[:, None]
    col_index = jnp.arange(extent)[None, :]
    window_mask = (col_index > row_index) & (col_index <= row_index + WINDOW)
    linear_mask = col_index <= row_index
    live = valid[None, :]
    scores = jnp.einsum(
        "igkd,jgd->gkij", rot_grouped, ext_keys, preferred_element_type=jnp.float32
    ) / math.sqrt(head_dim)
    near_window = window_mask & live
    peak = jnp.max(jnp.where(near_window, scores, -jnp.inf), axis=-1, keepdims=True)
    weights = jnp.where(near_window, jnp.exp(scores - peak), 0.0)
    window_sum = jnp.sum(weights, axis=-1)
    affinity = jnp.einsum("igkf,gkfj->gkij", phi_query, phi_key, preferred_element_type=jnp.float32)
    affinity = jnp.where(linear_mask & live, affinity, 0.0)
    near_sum = jnp.sum(affinity, axis=-1)
    window_num = jnp.einsum(
        "gkij,jgd->igkd",
        weights.astype(jnp.bfloat16),
        ext_values,
        preferred_element_type=jnp.float32,
    )
    near_num = jnp.einsum(
        "gkij,jgd->igkd",
        affinity.astype(jnp.bfloat16),
        ext_values,
        preferred_element_type=jnp.float32,
    )
    state_now = prior_state + before_state[0]
    norm_now = prior_norm + before_norm[0]
    state_high, state_rest = split_parts(state_now)
    norm_high, norm_rest = split_parts(norm_now)
    far_num = jnp.einsum(
        "igkf,gkfd->igkd", phi_query, state_high, preferred_element_type=jnp.float32
    )
    far_num = far_num + jnp.einsum(
        "igkf,gkfd->igkd", phi_query, state_rest, preferred_element_type=jnp.float32
    )
    far_sum = jnp.einsum("igkf,gkf->igk", phi_query, norm_high, preferred_element_type=jnp.float32)
    far_sum = far_sum + jnp.einsum(
        "igkf,gkf->igk", phi_query, norm_rest, preferred_element_type=jnp.float32
    )
    head_factor = factor[None, :, :, None]
    numerator = head_factor * window_num + (1.0 - head_factor) * (near_num + far_num)
    denominator = factor[None] * jnp.transpose(window_sum, (2, 0, 1)) + (1.0 - factor[None]) * (
        jnp.transpose(near_sum, (2, 0, 1)) + far_sum
    )
    outputs = (numerator / denominator[..., None]).astype(jnp.bfloat16)
    result = outputs.reshape(tokens, heads * head_dim)
    return lax.all_to_all(result, "head", split_axis=0, concat_axis=1, tiled=True)


def solution(mesh):
    in_specs = (
        P("seq", "head"),
        P("seq", "head"),
        P("seq", "head"),
        P("seq"),
        P("head", None, None),
        P("head", None, None),
        P("head"),
    )
    out_specs = P(("seq", "head"), None)
    return jax.shard_map(body, mesh=mesh, in_specs=in_specs, out_specs=out_specs, check_vma=False)
```

```python
import math

import jax
import jax.numpy as jnp
from jax import lax
from jax.experimental import pallas as pl
from jax.sharding import PartitionSpec as P

WINDOW = 64
BLOCK = 512
SPAN = 256


def passed_along(value, axis, steps):
    count = lax.axis_size(axis)
    first, last = (max(0, -steps), min(count, count - steps))
    return lax.ppermute(value, axis, [(source, source + steps) for source in range(first, last)])


def angle_tables(positions, half):
    frequency = [500000.0 ** (-float(order) / half) for order in range(half)]
    coarse = jnp.asarray([4096.0 * value % (2.0 * math.pi) for value in frequency], jnp.float32)
    medium = jnp.asarray([64.0 * value % (2.0 * math.pi) for value in frequency], jnp.float32)
    finest = jnp.asarray(frequency, jnp.float32)
    upper = (positions // 4096).astype(jnp.float32)[:, None] * coarse[None, :]
    middle = (positions // 64 % 64).astype(jnp.float32)[:, None] * medium[None, :]
    lower = (positions % 64).astype(jnp.float32)[:, None] * finest[None, :]
    cos_high = jnp.cos(upper) * jnp.cos(middle) - jnp.sin(upper) * jnp.sin(middle)
    sin_high = jnp.sin(upper) * jnp.cos(middle) + jnp.cos(upper) * jnp.sin(middle)
    cosine = cos_high * jnp.cos(lower) - sin_high * jnp.sin(lower)
    sine = sin_high * jnp.cos(lower) + cos_high * jnp.sin(lower)
    return (cosine, sine)


def span_tables(offsets, half):
    frequency = [500000.0 ** (-float(order) / half) for order in range(half)]
    coarse = jnp.asarray([4096.0 * value % (2.0 * math.pi) for value in frequency], jnp.float32)
    medium = jnp.asarray([64.0 * value % (2.0 * math.pi) for value in frequency], jnp.float32)
    finest = jnp.asarray(frequency, jnp.float32)
    quarters = SPAN // 64
    upper = (offsets // 4096).astype(jnp.float32)[:, None] * coarse[None, :]
    middle_index = (offsets[:, None] // 64 + jnp.arange(quarters, dtype=jnp.int32)[None, :]) % 64
    middle = middle_index.astype(jnp.float32)[:, :, None] * medium[None, None, :]
    lower = jnp.arange(64, dtype=jnp.float32)[:, None] * finest[None, :]
    cos_upper = jnp.cos(upper)[:, None, :]
    sin_upper = jnp.sin(upper)[:, None, :]
    cos_high = cos_upper * jnp.cos(middle) - sin_upper * jnp.sin(middle)
    sin_high = sin_upper * jnp.cos(middle) + cos_upper * jnp.sin(middle)
    cos_high = cos_high[:, :, None, :]
    sin_high = sin_high[:, :, None, :]
    cos_lower = jnp.cos(lower)[None, None]
    sin_lower = jnp.sin(lower)[None, None]
    cosine = cos_high * cos_lower - sin_high * sin_lower
    sine = sin_high * cos_lower + cos_high * sin_lower
    return (cosine.reshape(-1, half), sine.reshape(-1, half))


def rotate(rows, cosine, sine):
    half = rows.shape[-1] // 2
    first = rows[..., :half]
    second = rows[..., half:]
    cos_rows = cosine[:, None, :]
    sin_rows = sine[:, None, :]
    return jnp.concatenate(
        [first * cos_rows - second * sin_rows, second * cos_rows + first * sin_rows], axis=-1
    )


def two_softmax(logits):
    return jnp.concatenate(
        [jax.nn.softmax(logits, axis=-1), jax.nn.softmax(-logits, axis=-1)], axis=-1
    )


def split_parts(full_value):
    high_part = full_value.astype(jnp.bfloat16)
    rest_part = (full_value - high_part.astype(jnp.float32)).astype(jnp.bfloat16)
    return (high_part, rest_part)


def key_features(ext_keys2, key_map_t, ext_values2, mask, lag):
    rows, dim = ext_keys2.shape
    heads, feat, _ = key_map_t.shape

    def kernel(k_ref, m_ref, v_ref, mask_ref, phi_ref, st_ref, nm_ref):
        keys = k_ref[...]
        live = mask_ref[...] > 0.0
        values = v_ref[0:lag, :]
        for head in range(heads):
            logits = lax.dot_general(
                m_ref[head], keys, (((1,), (1,)), ((), ())), preferred_element_type=jnp.float32
            )
            for place, sign in enumerate((1.0, -1.0)):
                shifted = sign * logits
                expo = jnp.exp(shifted - jnp.max(shifted, axis=0, keepdims=True))
                soft = expo / jnp.sum(expo, axis=0, keepdims=True)
                phi = jnp.where(live, soft, 0.0).astype(jnp.bfloat16)
                band = slice(place * feat, (place + 1) * feat)
                phi_ref[head, band, :] = phi
                lagged = phi[:, 0:lag]
                st_ref[head, band, :] = jnp.dot(lagged, values, preferred_element_type=jnp.float32)
                nm_ref[head, band, :] = jnp.sum(lagged.astype(jnp.float32), axis=1, keepdims=True)

    return pl.pallas_call(
        kernel,
        grid=(1,),
        in_specs=[
            pl.BlockSpec((rows, dim), lambda h: (0, 0)),
            pl.BlockSpec((heads, feat, dim), lambda h: (0, 0, 0)),
            pl.BlockSpec((rows, dim), lambda h: (0, 0)),
            pl.BlockSpec((1, rows), lambda h: (0, 0)),
        ],
        out_specs=[
            pl.BlockSpec((heads, 2 * feat, rows), lambda h: (0, 0, 0)),
            pl.BlockSpec((heads, 2 * feat, dim), lambda h: (0, 0, 0)),
            pl.BlockSpec((heads, 2 * feat, 1), lambda h: (0, 0, 0)),
        ],
        out_shape=[
            jax.ShapeDtypeStruct((heads, 2 * feat, rows), jnp.bfloat16),
            jax.ShapeDtypeStruct((heads, 2 * feat, dim), jnp.float32),
            jax.ShapeDtypeStruct((heads, 2 * feat, 1), jnp.float32),
        ],
    )(ext_keys2, key_map_t, ext_values2, mask)

def body(queries, keys, values, offsets, query_map, key_map, window_logit):
    tokens = queries.shape[0]
    heads = query_map.shape[0]
    head_dim = query_map.shape[1]
    feat = query_map.shape[2]
    kv_local = keys.shape[1] // head_dim
    group = heads // kv_local
    blocks = tokens // BLOCK
    extent = BLOCK + WINDOW
    cosine, sine = span_tables(offsets, head_dim // 2)
    rot_k = rotate(
        keys.reshape(tokens, kv_local, head_dim).astype(jnp.float32), cosine, sine
    ).astype(jnp.bfloat16)
    value_rows = values.reshape(tokens, kv_local, head_dim)
    tail_keys, tail_values = passed_along(
        (rot_k[tokens - WINDOW :], value_rows[tokens - WINDOW :]), "seq", 1
    )
    ext_keys = jnp.concatenate([tail_keys, rot_k], axis=0)
    ext_values = jnp.concatenate([tail_values, value_rows], axis=0)
    valid = (jnp.arange(tokens + WINDOW) >= WINDOW) | (lax.axis_index("seq") > 0)
    ext_rows = tokens + WINDOW
    phi_heads, state_heads, norm_heads = key_features(
        ext_keys.reshape(ext_rows, head_dim),
        jnp.transpose(key_map, (0, 2, 1)),
        ext_values.reshape(ext_rows, head_dim),
        valid.astype(jnp.float32)[None, :],
        tokens,
    )
    phi_key = phi_heads.reshape(kv_local, group, 2 * feat, ext_rows)
    block_states = state_heads.reshape(1, kv_local, group, 2 * feat, head_dim)
    block_norms = norm_heads.reshape(1, kv_local, group, 2 * feat)
    total_state = jnp.sum(block_states, axis=0)
    total_norm = jnp.sum(block_norms, axis=0)
    before_state = jnp.concatenate(
        [jnp.zeros_like(block_states), jnp.cumsum(block_states, axis=0)[:-1]], axis=0
    )
    before_norm = jnp.concatenate(
        [jnp.zeros_like(block_norms), jnp.cumsum(block_norms, axis=0)[:-1]], axis=0
    )
    state_shape = total_state.shape
    state_size = total_state.size
    packed = jnp.concatenate([total_state.reshape(-1), total_norm.reshape(-1)])
    count = lax.axis_size("seq")
    shifts = []
    steps = 1
    while steps < count:
        shifts.append(steps)
        steps *= 2
    half = len(shifts) // 2 + 1
    orders = (shifts, shifts[half:] + shifts[:half])
    middle = packed.size // 2
    pieces = []
    for order, piece in zip(orders, (packed[:middle], packed[middle:])):
        inclusive = piece
        exclusive = jnp.zeros_like(piece)
        for place, shift in enumerate(order):
            received = passed_along(inclusive, "seq", shift)
            if not pieces and place == 0:
                first_received = received
            exclusive = exclusive + received
            if place + 1 < len(order):
                inclusive = inclusive + received
        pieces.append(exclusive)
    exclusive = jnp.concatenate(pieces)
    queries, first_received = lax.optimization_barrier((queries, first_received))
    rot_q = rotate(
        queries.reshape(tokens, heads, head_dim).astype(jnp.float32), cosine, sine
    ).astype(jnp.bfloat16)
    query_logits = jnp.einsum("nhd,hdf->nhf", rot_q, query_map, preferred_element_type=jnp.float32)
    phi_query = (
        two_softmax(query_logits).astype(jnp.bfloat16).reshape(tokens, kv_local, group, 2 * feat)
    )
    prior_state = exclusive[:state_size].reshape(state_shape)
    prior_norm = exclusive[state_size:].reshape(total_norm.shape)
    factor = jax.nn.sigmoid(window_logit).reshape(kv_local, group)
    rot_grouped = rot_q.reshape(tokens, kv_local, group, head_dim)
    row_index = jnp.arange(BLOCK)[:, None]
    col_index = jnp.arange(extent)[None, :]
    window_mask = (col_index > row_index) & (col_index <= row_index + WINDOW)
    linear_mask = col_index <= row_index
    live = valid[None, :]
    scores = jnp.einsum(
        "igkd,jgd->gkij", rot_grouped, ext_keys, preferred_element_type=jnp.float32
    ) / math.sqrt(head_dim)
    near_window = window_mask & live
    peak = jnp.max(jnp.where(near_window, scores, -jnp.inf), axis=-1, keepdims=True)
    weights = jnp.where(near_window, jnp.exp(scores - peak), 0.0)
    window_sum = jnp.sum(weights, axis=-1)
    affinity = jnp.einsum("igkf,gkfj->gkij", phi_query, phi_key, preferred_element_type=jnp.float32)
    affinity = jnp.where(linear_mask & live, affinity, 0.0)
    near_sum = jnp.sum(affinity, axis=-1)
    window_num = jnp.einsum(
        "gkij,jgd->igkd",
        weights.astype(jnp.bfloat16),
        ext_values,
        preferred_element_type=jnp.float32,
    )
    near_num = jnp.einsum(
        "gkij,jgd->igkd",
        affinity.astype(jnp.bfloat16),
        ext_values,
        preferred_element_type=jnp.float32,
    )
    state_now = prior_state + before_state[0]
    norm_now = prior_norm + before_norm[0]
    state_high, state_rest = split_parts(state_now)
    norm_high, norm_rest = split_parts(norm_now)
    far_num = jnp.einsum(
        "igkf,gkfd->igkd", phi_query, state_high, preferred_element_type=jnp.float32
    )
    far_num = far_num + jnp.einsum(
        "igkf,gkfd->igkd", phi_query, state_rest, preferred_element_type=jnp.float32
    )
    far_sum = jnp.einsum("igkf,gkf->igk", phi_query, norm_high, preferred_element_type=jnp.float32)
    far_sum = far_sum + jnp.einsum(
        "igkf,gkf->igk", phi_query, norm_rest, preferred_element_type=jnp.float32
    )
    head_factor = factor[None, :, :, None]
    numerator = head_factor * window_num + (1.0 - head_factor) * (near_num + far_num)
    denominator = factor[None] * jnp.transpose(window_sum, (2, 0, 1)) + (1.0 - factor[None]) * (
        jnp.transpose(near_sum, (2, 0, 1)) + far_sum
    )
    outputs = (numerator / denominator[..., None]).astype(jnp.bfloat16)
    result = outputs.reshape(tokens, heads * head_dim)
    return lax.all_to_all(result, "head", split_axis=0, concat_axis=1, tiled=True)


def solution(mesh):
    in_specs = (
        P("seq", "head"),
        P("seq", "head"),
        P("seq", "head"),
        P("seq"),
        P("head", None, None),
        P("head", None, None),
        P("head"),
    )
    out_specs = P(("seq", "head"), None)
    return jax.shard_map(body, mesh=mesh, in_specs=in_specs, out_specs=out_specs, check_vma=False)
```

```python
import math

import jax
import jax.numpy as jnp
from jax import lax
from jax.experimental import pallas as pl
from jax.sharding import PartitionSpec as P

WINDOW = 64
BLOCK = 512
SPAN = 256


def passed_along(value, axis, steps):
    count = lax.axis_size(axis)
    first, last = (max(0, -steps), min(count, count - steps))
    return lax.ppermute(value, axis, [(source, source + steps) for source in range(first, last)])


def angle_tables(positions, half):
    frequency = [500000.0 ** (-float(order) / half) for order in range(half)]
    coarse = jnp.asarray([4096.0 * value % (2.0 * math.pi) for value in frequency], jnp.float32)
    medium = jnp.asarray([64.0 * value % (2.0 * math.pi) for value in frequency], jnp.float32)
    finest = jnp.asarray(frequency, jnp.float32)
    upper = (positions // 4096).astype(jnp.float32)[:, None] * coarse[None, :]
    middle = (positions // 64 % 64).astype(jnp.float32)[:, None] * medium[None, :]
    lower = (positions % 64).astype(jnp.float32)[:, None] * finest[None, :]
    cos_high = jnp.cos(upper) * jnp.cos(middle) - jnp.sin(upper) * jnp.sin(middle)
    sin_high = jnp.sin(upper) * jnp.cos(middle) + jnp.cos(upper) * jnp.sin(middle)
    cosine = cos_high * jnp.cos(lower) - sin_high * jnp.sin(lower)
    sine = sin_high * jnp.cos(lower) + cos_high * jnp.sin(lower)
    return (cosine, sine)


def span_tables(offsets, half):
    frequency = [500000.0 ** (-float(order) / half) for order in range(half)]
    coarse = jnp.asarray([4096.0 * value % (2.0 * math.pi) for value in frequency], jnp.float32)
    medium = jnp.asarray([64.0 * value % (2.0 * math.pi) for value in frequency], jnp.float32)
    finest = jnp.asarray(frequency, jnp.float32)
    quarters = SPAN // 64
    upper = (offsets // 4096).astype(jnp.float32)[:, None] * coarse[None, :]
    middle_index = (offsets[:, None] // 64 + jnp.arange(quarters, dtype=jnp.int32)[None, :]) % 64
    middle = middle_index.astype(jnp.float32)[:, :, None] * medium[None, None, :]
    lower = jnp.arange(64, dtype=jnp.float32)[:, None] * finest[None, :]
    cos_upper = jnp.cos(upper)[:, None, :]
    sin_upper = jnp.sin(upper)[:, None, :]
    cos_high = cos_upper * jnp.cos(middle) - sin_upper * jnp.sin(middle)
    sin_high = sin_upper * jnp.cos(middle) + cos_upper * jnp.sin(middle)
    cos_high = cos_high[:, :, None, :]
    sin_high = sin_high[:, :, None, :]
    cos_lower = jnp.cos(lower)[None, None]
    sin_lower = jnp.sin(lower)[None, None]
    cosine = cos_high * cos_lower - sin_high * sin_lower
    sine = sin_high * cos_lower + cos_high * sin_lower
    return (cosine.reshape(-1, half), sine.reshape(-1, half))


def rotate(rows, cosine, sine):
    half = rows.shape[-1] // 2
    first = rows[..., :half]
    second = rows[..., half:]
    cos_rows = cosine[:, None, :]
    sin_rows = sine[:, None, :]
    return jnp.concatenate(
        [first * cos_rows - second * sin_rows, second * cos_rows + first * sin_rows], axis=-1
    )


def two_softmax(logits):
    return jnp.concatenate(
        [jax.nn.softmax(logits, axis=-1), jax.nn.softmax(-logits, axis=-1)], axis=-1
    )


def split_parts(full_value):
    high_part = full_value.astype(jnp.bfloat16)
    rest_part = (full_value - high_part.astype(jnp.float32)).astype(jnp.bfloat16)
    return (high_part, rest_part)


def key_features(ext_keys2, key_map_t, ext_values2, mask, lag):
    rows, dim = ext_keys2.shape
    heads, feat, _ = key_map_t.shape

    def kernel(k_ref, m_ref, v_ref, mask_ref, phi_ref, st_ref, nm_ref):
        keys = k_ref[...]
        live = mask_ref[...] > 0.0
        values = v_ref[0:lag, :]
        for head in range(heads):
            logits = lax.dot_general(
                m_ref[head], keys, (((1,), (1,)), ((), ())), preferred_element_type=jnp.float32
            )
            for place, sign in enumerate((1.0, -1.0)):
                shifted = sign * logits
                expo = jnp.exp(shifted - jnp.max(shifted, axis=0, keepdims=True))
                soft = expo / jnp.sum(expo, axis=0, keepdims=True)
                phi = jnp.where(live, soft, 0.0).astype(jnp.bfloat16)
                band = slice(place * feat, (place + 1) * feat)
                phi_ref[head, band, :] = phi
                lagged = phi[:, 0:lag]
                st_ref[head, band, :] = jnp.dot(lagged, values, preferred_element_type=jnp.float32)
                nm_ref[head, band, :] = jnp.sum(lagged.astype(jnp.float32), axis=1, keepdims=True)

    return pl.pallas_call(
        kernel,
        grid=(1,),
        in_specs=[
            pl.BlockSpec((rows, dim), lambda h: (0, 0)),
            pl.BlockSpec((heads, feat, dim), lambda h: (0, 0, 0)),
            pl.BlockSpec((rows, dim), lambda h: (0, 0)),
            pl.BlockSpec((1, rows), lambda h: (0, 0)),
        ],
        out_specs=[
            pl.BlockSpec((heads, 2 * feat, rows), lambda h: (0, 0, 0)),
            pl.BlockSpec((heads, 2 * feat, dim), lambda h: (0, 0, 0)),
            pl.BlockSpec((heads, 2 * feat, 1), lambda h: (0, 0, 0)),
        ],
        out_shape=[
            jax.ShapeDtypeStruct((heads, 2 * feat, rows), jnp.bfloat16),
            jax.ShapeDtypeStruct((heads, 2 * feat, dim), jnp.float32),
            jax.ShapeDtypeStruct((heads, 2 * feat, 1), jnp.float32),
        ],
    )(ext_keys2, key_map_t, ext_values2, mask)

def body(queries, keys, values, offsets, query_map, key_map, window_logit):
    tokens = queries.shape[0]
    heads = query_map.shape[0]
    head_dim = query_map.shape[1]
    feat = query_map.shape[2]
    kv_local = keys.shape[1] // head_dim
    group = heads // kv_local
    blocks = tokens // BLOCK
    extent = BLOCK + WINDOW
    cosine, sine = span_tables(offsets, head_dim // 2)
    rot_k = rotate(
        keys.reshape(tokens, kv_local, head_dim).astype(jnp.float32), cosine, sine
    ).astype(jnp.bfloat16)
    value_rows = values.reshape(tokens, kv_local, head_dim)
    tail_keys, tail_values = passed_along(
        (rot_k[tokens - WINDOW :], value_rows[tokens - WINDOW :]), "seq", 1
    )
    ext_keys = jnp.concatenate([tail_keys, rot_k], axis=0)
    ext_values = jnp.concatenate([tail_values, value_rows], axis=0)
    valid = (jnp.arange(tokens + WINDOW) >= WINDOW) | (lax.axis_index("seq") > 0)
    ext_rows = tokens + WINDOW
    phi_heads, state_heads, norm_heads = key_features(
        ext_keys.reshape(ext_rows, head_dim),
        jnp.transpose(key_map, (0, 2, 1)),
        ext_values.reshape(ext_rows, head_dim),
        valid.astype(jnp.float32)[None, :],
        tokens,
    )
    phi_key = phi_heads.reshape(kv_local, group, 2 * feat, ext_rows)
    block_states = state_heads.reshape(1, kv_local, group, 2 * feat, head_dim)
    block_norms = norm_heads.reshape(1, kv_local, group, 2 * feat)
    total_state = jnp.sum(block_states, axis=0)
    total_norm = jnp.sum(block_norms, axis=0)
    before_state = jnp.concatenate(
        [jnp.zeros_like(block_states), jnp.cumsum(block_states, axis=0)[:-1]], axis=0
    )
    before_norm = jnp.concatenate(
        [jnp.zeros_like(block_norms), jnp.cumsum(block_norms, axis=0)[:-1]], axis=0
    )
    state_shape = total_state.shape
    state_size = total_state.size
    packed = jnp.concatenate([total_state.reshape(-1), total_norm.reshape(-1)])
    count = lax.axis_size("seq")
    shifts = []
    steps = 1
    while steps < count:
        shifts.append(steps)
        steps *= 2
    half = len(shifts) // 2 + 1
    orders = (shifts, shifts[half:] + shifts[:half])
    middle = packed.size // 2
    pieces = []
    for order, piece in zip(orders, lax.optimization_barrier((packed[:middle], packed[middle:]))):
        inclusive = piece
        exclusive = jnp.zeros_like(piece)
        for place, shift in enumerate(order):
            received = passed_along(inclusive, "seq", shift)
            if not pieces and place == 0:
                first_received = received
            exclusive = exclusive + received
            if place + 1 < len(order):
                inclusive = inclusive + received
        pieces.append(exclusive)
    exclusive = jnp.concatenate(pieces)
    queries, first_received = lax.optimization_barrier((queries, first_received))
    rot_q = rotate(
        queries.reshape(tokens, heads, head_dim).astype(jnp.float32), cosine, sine
    ).astype(jnp.bfloat16)
    query_logits = jnp.einsum("nhd,hdf->nhf", rot_q, query_map, preferred_element_type=jnp.float32)
    phi_query = (
        two_softmax(query_logits).astype(jnp.bfloat16).reshape(tokens, kv_local, group, 2 * feat)
    )
    prior_state = exclusive[:state_size].reshape(state_shape)
    prior_norm = exclusive[state_size:].reshape(total_norm.shape)
    factor = jax.nn.sigmoid(window_logit).reshape(kv_local, group)
    rot_grouped = rot_q.reshape(tokens, kv_local, group, head_dim)
    row_index = jnp.arange(BLOCK)[:, None]
    col_index = jnp.arange(extent)[None, :]
    window_mask = (col_index > row_index) & (col_index <= row_index + WINDOW)
    linear_mask = col_index <= row_index
    live = valid[None, :]
    scores = jnp.einsum(
        "igkd,jgd->gkij", rot_grouped, ext_keys, preferred_element_type=jnp.float32
    ) / math.sqrt(head_dim)
    near_window = window_mask & live
    peak = jnp.max(jnp.where(near_window, scores, -jnp.inf), axis=-1, keepdims=True)
    weights = jnp.where(near_window, jnp.exp(scores - peak), 0.0)
    window_sum = jnp.sum(weights, axis=-1)
    affinity = jnp.einsum("igkf,gkfj->gkij", phi_query, phi_key, preferred_element_type=jnp.float32)
    affinity = jnp.where(linear_mask & live, affinity, 0.0)
    near_sum = jnp.sum(affinity, axis=-1)
    window_num = jnp.einsum(
        "gkij,jgd->igkd",
        weights.astype(jnp.bfloat16),
        ext_values,
        preferred_element_type=jnp.float32,
    )
    near_num = jnp.einsum(
        "gkij,jgd->igkd",
        affinity.astype(jnp.bfloat16),
        ext_values,
        preferred_element_type=jnp.float32,
    )
    state_now = prior_state + before_state[0]
    norm_now = prior_norm + before_norm[0]
    state_high, state_rest = split_parts(state_now)
    norm_high, norm_rest = split_parts(norm_now)
    far_num = jnp.einsum(
        "igkf,gkfd->igkd", phi_query, state_high, preferred_element_type=jnp.float32
    )
    far_num = far_num + jnp.einsum(
        "igkf,gkfd->igkd", phi_query, state_rest, preferred_element_type=jnp.float32
    )
    far_sum = jnp.einsum("igkf,gkf->igk", phi_query, norm_high, preferred_element_type=jnp.float32)
    far_sum = far_sum + jnp.einsum(
        "igkf,gkf->igk", phi_query, norm_rest, preferred_element_type=jnp.float32
    )
    head_factor = factor[None, :, :, None]
    numerator = head_factor * window_num + (1.0 - head_factor) * (near_num + far_num)
    denominator = factor[None] * jnp.transpose(window_sum, (2, 0, 1)) + (1.0 - factor[None]) * (
        jnp.transpose(near_sum, (2, 0, 1)) + far_sum
    )
    outputs = (numerator / denominator[..., None]).astype(jnp.bfloat16)
    result = outputs.reshape(tokens, heads * head_dim)
    return lax.all_to_all(result, "head", split_axis=0, concat_axis=1, tiled=True)


def solution(mesh):
    in_specs = (
        P("seq", "head"),
        P("seq", "head"),
        P("seq", "head"),
        P("seq"),
        P("head", None, None),
        P("head", None, None),
        P("head"),
    )
    out_specs = P(("seq", "head"), None)
    return jax.shard_map(body, mesh=mesh, in_specs=in_specs, out_specs=out_specs, check_vma=False)
```

```python
import math

import jax
import jax.numpy as jnp
from jax import lax
from jax.experimental import pallas as pl
from jax.sharding import PartitionSpec as P

WINDOW = 64
BLOCK = 512
SPAN = 256


def passed_along(value, axis, steps):
    count = lax.axis_size(axis)
    first, last = (max(0, -steps), min(count, count - steps))
    return lax.ppermute(value, axis, [(source, source + steps) for source in range(first, last)])


def angle_tables(positions, half):
    frequency = [500000.0 ** (-float(order) / half) for order in range(half)]
    coarse = jnp.asarray([4096.0 * value % (2.0 * math.pi) for value in frequency], jnp.float32)
    medium = jnp.asarray([64.0 * value % (2.0 * math.pi) for value in frequency], jnp.float32)
    finest = jnp.asarray(frequency, jnp.float32)
    upper = (positions // 4096).astype(jnp.float32)[:, None] * coarse[None, :]
    middle = (positions // 64 % 64).astype(jnp.float32)[:, None] * medium[None, :]
    lower = (positions % 64).astype(jnp.float32)[:, None] * finest[None, :]
    cos_high = jnp.cos(upper) * jnp.cos(middle) - jnp.sin(upper) * jnp.sin(middle)
    sin_high = jnp.sin(upper) * jnp.cos(middle) + jnp.cos(upper) * jnp.sin(middle)
    cosine = cos_high * jnp.cos(lower) - sin_high * jnp.sin(lower)
    sine = sin_high * jnp.cos(lower) + cos_high * jnp.sin(lower)
    return (cosine, sine)


def span_tables(offsets, half):
    frequency = [500000.0 ** (-float(order) / half) for order in range(half)]
    coarse = jnp.asarray([4096.0 * value % (2.0 * math.pi) for value in frequency], jnp.float32)
    medium = jnp.asarray([64.0 * value % (2.0 * math.pi) for value in frequency], jnp.float32)
    finest = jnp.asarray(frequency, jnp.float32)
    quarters = SPAN // 64
    upper = (offsets // 4096).astype(jnp.float32)[:, None] * coarse[None, :]
    middle_index = (offsets[:, None] // 64 + jnp.arange(quarters, dtype=jnp.int32)[None, :]) % 64
    middle = middle_index.astype(jnp.float32)[:, :, None] * medium[None, None, :]
    lower = jnp.arange(64, dtype=jnp.float32)[:, None] * finest[None, :]
    cos_upper = jnp.cos(upper)[:, None, :]
    sin_upper = jnp.sin(upper)[:, None, :]
    cos_high = cos_upper * jnp.cos(middle) - sin_upper * jnp.sin(middle)
    sin_high = sin_upper * jnp.cos(middle) + cos_upper * jnp.sin(middle)
    cos_high = cos_high[:, :, None, :]
    sin_high = sin_high[:, :, None, :]
    cos_lower = jnp.cos(lower)[None, None]
    sin_lower = jnp.sin(lower)[None, None]
    cosine = cos_high * cos_lower - sin_high * sin_lower
    sine = sin_high * cos_lower + cos_high * sin_lower
    return (cosine.reshape(-1, half), sine.reshape(-1, half))


def rotate(rows, cosine, sine):
    half = rows.shape[-1] // 2
    first = rows[..., :half]
    second = rows[..., half:]
    cos_rows = cosine[:, None, :]
    sin_rows = sine[:, None, :]
    return jnp.concatenate(
        [first * cos_rows - second * sin_rows, second * cos_rows + first * sin_rows], axis=-1
    )


def two_softmax(logits):
    return jnp.concatenate(
        [jax.nn.softmax(logits, axis=-1), jax.nn.softmax(-logits, axis=-1)], axis=-1
    )


def split_parts(full_value):
    high_part = full_value.astype(jnp.bfloat16)
    rest_part = (full_value - high_part.astype(jnp.float32)).astype(jnp.bfloat16)
    return (high_part, rest_part)


def key_features(ext_keys2, key_map_t, ext_values2, mask, lag):
    rows, dim = ext_keys2.shape
    heads, feat, _ = key_map_t.shape

    def kernel(k_ref, m_ref, v_ref, mask_ref, phi_ref, st_ref, nm_ref):
        keys = k_ref[...]
        live = mask_ref[...] > 0.0
        values = v_ref[0:lag, :]
        for head in range(heads):
            logits = lax.dot_general(
                m_ref[head], keys, (((1,), (1,)), ((), ())), preferred_element_type=jnp.float32
            )
            for place, sign in enumerate((1.0, -1.0)):
                shifted = sign * logits
                expo = jnp.exp(shifted - jnp.max(shifted, axis=0, keepdims=True))
                soft = expo / jnp.sum(expo, axis=0, keepdims=True)
                phi = jnp.where(live, soft, 0.0).astype(jnp.bfloat16)
                band = slice(place * feat, (place + 1) * feat)
                phi_ref[head, band, :] = phi
                lagged = phi[:, 0:lag]
                st_ref[head, band, :] = jnp.dot(lagged, values, preferred_element_type=jnp.float32)
                nm_ref[head, band, :] = jnp.sum(lagged.astype(jnp.float32), axis=1, keepdims=True)

    return pl.pallas_call(
        kernel,
        grid=(1,),
        in_specs=[
            pl.BlockSpec((rows, dim), lambda h: (0, 0)),
            pl.BlockSpec((heads, feat, dim), lambda h: (0, 0, 0)),
            pl.BlockSpec((rows, dim), lambda h: (0, 0)),
            pl.BlockSpec((1, rows), lambda h: (0, 0)),
        ],
        out_specs=[
            pl.BlockSpec((heads, 2 * feat, rows), lambda h: (0, 0, 0)),
            pl.BlockSpec((heads, 2 * feat, dim), lambda h: (0, 0, 0)),
            pl.BlockSpec((heads, 2 * feat, 1), lambda h: (0, 0, 0)),
        ],
        out_shape=[
            jax.ShapeDtypeStruct((heads, 2 * feat, rows), jnp.bfloat16),
            jax.ShapeDtypeStruct((heads, 2 * feat, dim), jnp.float32),
            jax.ShapeDtypeStruct((heads, 2 * feat, 1), jnp.float32),
        ],
    )(ext_keys2, key_map_t, ext_values2, mask)

def body(queries, keys, values, offsets, query_map, key_map, window_logit):
    tokens = queries.shape[0]
    heads = query_map.shape[0]
    head_dim = query_map.shape[1]
    feat = query_map.shape[2]
    kv_local = keys.shape[1] // head_dim
    group = heads // kv_local
    blocks = tokens // BLOCK
    extent = BLOCK + WINDOW
    cosine, sine = span_tables(offsets, head_dim // 2)
    rot_k = rotate(
        keys.reshape(tokens, kv_local, head_dim).astype(jnp.float32), cosine, sine
    ).astype(jnp.bfloat16)
    value_rows = values.reshape(tokens, kv_local, head_dim)
    tail_keys, tail_values = passed_along(
        (rot_k[tokens - WINDOW :], value_rows[tokens - WINDOW :]), "seq", 1
    )
    ext_keys = jnp.concatenate([tail_keys, rot_k], axis=0)
    ext_values = jnp.concatenate([tail_values, value_rows], axis=0)
    valid = (jnp.arange(tokens + WINDOW) >= WINDOW) | (lax.axis_index("seq") > 0)
    ext_rows = tokens + WINDOW
    phi_heads, state_heads, norm_heads = key_features(
        ext_keys.reshape(ext_rows, head_dim),
        jnp.transpose(key_map, (0, 2, 1)),
        ext_values.reshape(ext_rows, head_dim),
        valid.astype(jnp.float32)[None, :],
        tokens,
    )
    phi_key = phi_heads.reshape(kv_local, group, 2 * feat, ext_rows)
    block_states = state_heads.reshape(1, kv_local, group, 2 * feat, head_dim)
    block_norms = norm_heads.reshape(1, kv_local, group, 2 * feat)
    total_state = jnp.sum(block_states, axis=0)
    total_norm = jnp.sum(block_norms, axis=0)
    before_state = jnp.concatenate(
        [jnp.zeros_like(block_states), jnp.cumsum(block_states, axis=0)[:-1]], axis=0
    )
    before_norm = jnp.concatenate(
        [jnp.zeros_like(block_norms), jnp.cumsum(block_norms, axis=0)[:-1]], axis=0
    )
    state_shape = total_state.shape
    state_size = total_state.size
    packed = jnp.concatenate([total_state.reshape(-1), total_norm.reshape(-1)])
    count = lax.axis_size("seq")
    shifts = []
    steps = 1
    while steps < count:
        shifts.append(steps)
        steps *= 2
    half = len(shifts) // 2 + 1
    orders = (shifts, shifts[half:] + shifts[:half])
    middle = packed.size // 2
    pieces = []
    for order, piece in zip(orders, lax.optimization_barrier((packed[:middle], packed[middle:]))):
        inclusive = piece
        exclusive = jnp.zeros_like(piece)
        for place, shift in enumerate(order):
            received = passed_along(inclusive, "seq", shift)
            if not pieces and place == 0:
                first_received = received
            exclusive = exclusive + received
            if place + 1 < len(order):
                inclusive = inclusive + received
        pieces.append(exclusive)
    exclusive = jnp.concatenate(pieces)
    queries, first_received = lax.optimization_barrier((queries, first_received))
    rot_q = rotate(
        queries.reshape(tokens, heads, head_dim).astype(jnp.float32), cosine, sine
    ).astype(jnp.bfloat16)
    query_logits = jnp.einsum("nhd,hdf->nhf", rot_q, query_map, preferred_element_type=jnp.float32)
    phi_query = (
        two_softmax(query_logits).astype(jnp.bfloat16).reshape(tokens, kv_local, group, 2 * feat)
    )
    prior_state = exclusive[:state_size].reshape(state_shape)
    prior_norm = exclusive[state_size:].reshape(total_norm.shape)
    factor = jax.nn.sigmoid(window_logit).reshape(kv_local, group)
    rot_grouped = rot_q.reshape(tokens, kv_local, group, head_dim)
    row_index = jnp.arange(BLOCK)[:, None]
    col_index = jnp.arange(extent)[None, :]
    window_mask = (col_index > row_index) & (col_index <= row_index + WINDOW)
    linear_mask = col_index <= row_index
    live = valid[None, :]
    scores = jnp.einsum(
        "igkd,jgd->gkij", rot_grouped, ext_keys, preferred_element_type=jnp.float32
    ) / math.sqrt(head_dim)
    near_window = window_mask & live
    peak = jnp.max(jnp.where(near_window, scores, -jnp.inf), axis=-1, keepdims=True)
    weights = jnp.where(near_window, jnp.exp(scores - peak), 0.0)
    window_sum = jnp.sum(weights, axis=-1)
    affinity = jnp.einsum("igkf,gkfj->gkij", phi_query, phi_key, preferred_element_type=jnp.float32)
    affinity = jnp.where(linear_mask & live, affinity, 0.0)
    near_sum = jnp.sum(affinity, axis=-1)
    window_num = jnp.einsum(
        "gkij,jgd->igkd",
        weights.astype(jnp.bfloat16),
        ext_values,
        preferred_element_type=jnp.float32,
    )
    near_num = jnp.einsum(
        "gkij,jgd->igkd",
        affinity.astype(jnp.bfloat16),
        ext_values,
        preferred_element_type=jnp.float32,
    )
    state_now = prior_state + before_state[0]
    norm_now = prior_norm + before_norm[0]
    state_high, state_rest = split_parts(state_now)
    norm_high, norm_rest = split_parts(norm_now)
    far_num = jnp.einsum(
        "igkf,gkfd->igkd", phi_query, state_high, preferred_element_type=jnp.float32
    )
    far_num = far_num + jnp.einsum(
        "igkf,gkfd->igkd", phi_query, state_rest, preferred_element_type=jnp.float32
    )
    far_sum = jnp.einsum("igkf,gkf->igk", phi_query, norm_high, preferred_element_type=jnp.float32)
    far_sum = far_sum + jnp.einsum(
        "igkf,gkf->igk", phi_query, norm_rest, preferred_element_type=jnp.float32
    )
    head_factor = factor[None, :, :, None]
    numerator = head_factor * window_num + (1.0 - head_factor) * (near_num + far_num)
    denominator = factor[None] * jnp.transpose(window_sum, (2, 0, 1)) + (1.0 - factor[None]) * (
        jnp.transpose(near_sum, (2, 0, 1)) + far_sum
    )
    outputs = (numerator / denominator[..., None]).astype(jnp.bfloat16)
    result = outputs.reshape(tokens, heads * head_dim)
    outer = lax.axis_size("hy")
    pair = lax.axis_size("hc")
    staged = result.reshape(outer, pair, tokens // (outer * pair), heads * head_dim)
    staged = lax.all_to_all(staged, "hc", split_axis=1, concat_axis=1, tiled=True)
    staged = lax.all_to_all(staged, "hy", split_axis=0, concat_axis=0, tiled=True)
    staged = jnp.transpose(staged, (2, 0, 1, 3))
    return staged.reshape(staged.shape[0], -1)


def solution(mesh):
    head_count = mesh.shape["head"]
    pair = math.gcd(head_count, 2)
    split_mesh = jax.sharding.Mesh(
        mesh.devices.reshape(mesh.shape["seq"], head_count // pair, pair), ("seq", "hy", "hc")
    )
    cols = ("hy", "hc")
    in_specs = (
        P("seq", cols),
        P("seq", cols),
        P("seq", cols),
        P("seq"),
        P(cols, None, None),
        P(cols, None, None),
        P(cols),
    )
    out_specs = P(("seq", "hy", "hc"), None)
    return jax.shard_map(
        body, mesh=split_mesh, in_specs=in_specs, out_specs=out_specs, check_vma=False
    )
```

```python
import math

import jax
import jax.numpy as jnp
from jax import lax
from jax.experimental import pallas as pl
from jax.sharding import PartitionSpec as P

WINDOW = 64
BLOCK = 512
SPAN = 256


def passed_along(value, axis, steps):
    count = lax.axis_size(axis)
    first, last = (max(0, -steps), min(count, count - steps))
    return lax.ppermute(value, axis, [(source, source + steps) for source in range(first, last)])


def angle_tables(positions, half):
    frequency = [500000.0 ** (-float(order) / half) for order in range(half)]
    coarse = jnp.asarray([4096.0 * value % (2.0 * math.pi) for value in frequency], jnp.float32)
    medium = jnp.asarray([64.0 * value % (2.0 * math.pi) for value in frequency], jnp.float32)
    finest = jnp.asarray(frequency, jnp.float32)
    upper = (positions // 4096).astype(jnp.float32)[:, None] * coarse[None, :]
    middle = (positions // 64 % 64).astype(jnp.float32)[:, None] * medium[None, :]
    lower = (positions % 64).astype(jnp.float32)[:, None] * finest[None, :]
    cos_high = jnp.cos(upper) * jnp.cos(middle) - jnp.sin(upper) * jnp.sin(middle)
    sin_high = jnp.sin(upper) * jnp.cos(middle) + jnp.cos(upper) * jnp.sin(middle)
    cosine = cos_high * jnp.cos(lower) - sin_high * jnp.sin(lower)
    sine = sin_high * jnp.cos(lower) + cos_high * jnp.sin(lower)
    return (cosine, sine)


def span_tables(offsets, half):
    frequency = [500000.0 ** (-float(order) / half) for order in range(half)]
    coarse = jnp.asarray([4096.0 * value % (2.0 * math.pi) for value in frequency], jnp.float32)
    medium = jnp.asarray([64.0 * value % (2.0 * math.pi) for value in frequency], jnp.float32)
    finest = jnp.asarray(frequency, jnp.float32)
    quarters = SPAN // 64
    upper = (offsets // 4096).astype(jnp.float32)[:, None] * coarse[None, :]
    middle_index = (offsets[:, None] // 64 + jnp.arange(quarters, dtype=jnp.int32)[None, :]) % 64
    middle = middle_index.astype(jnp.float32)[:, :, None] * medium[None, None, :]
    lower = jnp.arange(64, dtype=jnp.float32)[:, None] * finest[None, :]
    cos_upper = jnp.cos(upper)[:, None, :]
    sin_upper = jnp.sin(upper)[:, None, :]
    cos_high = cos_upper * jnp.cos(middle) - sin_upper * jnp.sin(middle)
    sin_high = sin_upper * jnp.cos(middle) + cos_upper * jnp.sin(middle)
    cos_high = cos_high[:, :, None, :]
    sin_high = sin_high[:, :, None, :]
    cos_lower = jnp.cos(lower)[None, None]
    sin_lower = jnp.sin(lower)[None, None]
    cosine = cos_high * cos_lower - sin_high * sin_lower
    sine = sin_high * cos_lower + cos_high * sin_lower
    return (cosine.reshape(-1, half), sine.reshape(-1, half))


def rotate(rows, cosine, sine):
    half = rows.shape[-1] // 2
    first = rows[..., :half]
    second = rows[..., half:]
    cos_rows = cosine[:, None, :]
    sin_rows = sine[:, None, :]
    return jnp.concatenate(
        [first * cos_rows - second * sin_rows, second * cos_rows + first * sin_rows], axis=-1
    )


def two_softmax(logits):
    return jnp.concatenate(
        [jax.nn.softmax(logits, axis=-1), jax.nn.softmax(-logits, axis=-1)], axis=-1
    )


def split_parts(full_value):
    high_part = full_value.astype(jnp.bfloat16)
    rest_part = (full_value - high_part.astype(jnp.float32)).astype(jnp.bfloat16)
    return (high_part, rest_part)


def key_features(ext_keys2, key_map_t, ext_values2, mask, lag):
    rows, dim = ext_keys2.shape
    heads, feat, _ = key_map_t.shape

    def kernel(k_ref, m_ref, v_ref, mask_ref, phi_ref, st_ref, nm_ref):
        keys = k_ref[...]
        live = mask_ref[...] > 0.0
        values = v_ref[0:lag, :]
        for head in range(heads):
            logits = lax.dot_general(
                m_ref[head], keys, (((1,), (1,)), ((), ())), preferred_element_type=jnp.float32
            )
            for place, sign in enumerate((1.0, -1.0)):
                shifted = sign * logits
                expo = jnp.exp(shifted - jnp.max(shifted, axis=0, keepdims=True))
                soft = expo / jnp.sum(expo, axis=0, keepdims=True)
                phi = jnp.where(live, soft, 0.0).astype(jnp.bfloat16)
                band = slice(place * feat, (place + 1) * feat)
                phi_ref[head, band, :] = phi
                lagged = phi[:, 0:lag]
                st_ref[head, band, :] = jnp.dot(lagged, values, preferred_element_type=jnp.float32)
                nm_ref[head, band, :] = jnp.sum(lagged.astype(jnp.float32), axis=1, keepdims=True)

    return pl.pallas_call(
        kernel,
        grid=(1,),
        in_specs=[
            pl.BlockSpec((rows, dim), lambda h: (0, 0)),
            pl.BlockSpec((heads, feat, dim), lambda h: (0, 0, 0)),
            pl.BlockSpec((rows, dim), lambda h: (0, 0)),
            pl.BlockSpec((1, rows), lambda h: (0, 0)),
        ],
        out_specs=[
            pl.BlockSpec((heads, 2 * feat, rows), lambda h: (0, 0, 0)),
            pl.BlockSpec((heads, 2 * feat, dim), lambda h: (0, 0, 0)),
            pl.BlockSpec((heads, 2 * feat, 1), lambda h: (0, 0, 0)),
        ],
        out_shape=[
            jax.ShapeDtypeStruct((heads, 2 * feat, rows), jnp.bfloat16),
            jax.ShapeDtypeStruct((heads, 2 * feat, dim), jnp.float32),
            jax.ShapeDtypeStruct((heads, 2 * feat, 1), jnp.float32),
        ],
    )(ext_keys2, key_map_t, ext_values2, mask)

def body(queries, keys, values, offsets, query_map, key_map, window_logit):
    tokens = queries.shape[0]
    heads = query_map.shape[0]
    head_dim = query_map.shape[1]
    feat = query_map.shape[2]
    kv_local = keys.shape[1] // head_dim
    group = heads // kv_local
    blocks = tokens // BLOCK
    extent = BLOCK + WINDOW
    cosine, sine = span_tables(offsets, head_dim // 2)
    rot_k = rotate(
        keys.reshape(tokens, kv_local, head_dim).astype(jnp.float32), cosine, sine
    ).astype(jnp.bfloat16)
    value_rows = values.reshape(tokens, kv_local, head_dim)
    tail_both = passed_along(
        jnp.concatenate([rot_k[tokens - WINDOW :], value_rows[tokens - WINDOW :]], axis=-1),
        "seq",
        1,
    )
    tail_keys = tail_both[..., :head_dim]
    tail_values = tail_both[..., head_dim:]
    ext_keys = jnp.concatenate([tail_keys, rot_k], axis=0)
    ext_values = jnp.concatenate([tail_values, value_rows], axis=0)
    valid = (jnp.arange(tokens + WINDOW) >= WINDOW) | (lax.axis_index("seq") > 0)
    ext_rows = tokens + WINDOW
    phi_heads, state_heads, norm_heads = key_features(
        ext_keys.reshape(ext_rows, head_dim),
        jnp.transpose(key_map, (0, 2, 1)),
        ext_values.reshape(ext_rows, head_dim),
        valid.astype(jnp.float32)[None, :],
        tokens,
    )
    phi_key = phi_heads.reshape(kv_local, group, 2 * feat, ext_rows)
    block_states = state_heads.reshape(1, kv_local, group, 2 * feat, head_dim)
    block_norms = norm_heads.reshape(1, kv_local, group, 2 * feat)
    total_state = jnp.sum(block_states, axis=0)
    total_norm = jnp.sum(block_norms, axis=0)
    before_state = jnp.concatenate(
        [jnp.zeros_like(block_states), jnp.cumsum(block_states, axis=0)[:-1]], axis=0
    )
    before_norm = jnp.concatenate(
        [jnp.zeros_like(block_norms), jnp.cumsum(block_norms, axis=0)[:-1]], axis=0
    )
    state_shape = total_state.shape
    state_size = total_state.size
    packed = jnp.concatenate([total_state.reshape(-1), total_norm.reshape(-1)])
    count = lax.axis_size("seq")
    shifts = []
    steps = 1
    while steps < count:
        shifts.append(steps)
        steps *= 2
    half = len(shifts) // 2 + 1
    orders = (shifts, shifts[half:] + shifts[:half])
    middle = packed.size // 2
    pieces = []
    for order, piece in zip(orders, lax.optimization_barrier((packed[:middle], packed[middle:]))):
        inclusive = piece
        exclusive = jnp.zeros_like(piece)
        for place, shift in enumerate(order):
            received = passed_along(inclusive, "seq", shift)
            if not pieces and place == 0:
                first_received = received
            exclusive = exclusive + received
            if place + 1 < len(order):
                inclusive = inclusive + received
        pieces.append(exclusive)
    exclusive = jnp.concatenate(pieces)
    queries, first_received = lax.optimization_barrier((queries, first_received))
    rot_q = rotate(
        queries.reshape(tokens, heads, head_dim).astype(jnp.float32), cosine, sine
    ).astype(jnp.bfloat16)
    query_logits = jnp.einsum("nhd,hdf->nhf", rot_q, query_map, preferred_element_type=jnp.float32)
    phi_query = (
        two_softmax(query_logits).astype(jnp.bfloat16).reshape(tokens, kv_local, group, 2 * feat)
    )
    prior_state = exclusive[:state_size].reshape(state_shape)
    prior_norm = exclusive[state_size:].reshape(total_norm.shape)
    factor = jax.nn.sigmoid(window_logit).reshape(kv_local, group)
    rot_grouped = rot_q.reshape(tokens, kv_local, group, head_dim)
    row_index = jnp.arange(BLOCK)[:, None]
    col_index = jnp.arange(extent)[None, :]
    window_mask = (col_index > row_index) & (col_index <= row_index + WINDOW)
    linear_mask = col_index <= row_index
    live = valid[None, :]
    scores = jnp.einsum(
        "igkd,jgd->gkij", rot_grouped, ext_keys, preferred_element_type=jnp.float32
    ) / math.sqrt(head_dim)
    near_window = window_mask & live
    peak = jnp.max(jnp.where(near_window, scores, -jnp.inf), axis=-1, keepdims=True)
    weights = jnp.where(near_window, jnp.exp(scores - peak), 0.0)
    window_sum = jnp.sum(weights, axis=-1)
    affinity = jnp.einsum("igkf,gkfj->gkij", phi_query, phi_key, preferred_element_type=jnp.float32)
    affinity = jnp.where(linear_mask & live, affinity, 0.0)
    near_sum = jnp.sum(affinity, axis=-1)
    window_num = jnp.einsum(
        "gkij,jgd->igkd",
        weights.astype(jnp.bfloat16),
        ext_values,
        preferred_element_type=jnp.float32,
    )
    near_num = jnp.einsum(
        "gkij,jgd->igkd",
        affinity.astype(jnp.bfloat16),
        ext_values,
        preferred_element_type=jnp.float32,
    )
    state_now = prior_state + before_state[0]
    norm_now = prior_norm + before_norm[0]
    state_high, state_rest = split_parts(state_now)
    norm_high, norm_rest = split_parts(norm_now)
    far_num = jnp.einsum(
        "igkf,gkfd->igkd", phi_query, state_high, preferred_element_type=jnp.float32
    )
    far_num = far_num + jnp.einsum(
        "igkf,gkfd->igkd", phi_query, state_rest, preferred_element_type=jnp.float32
    )
    far_sum = jnp.einsum("igkf,gkf->igk", phi_query, norm_high, preferred_element_type=jnp.float32)
    far_sum = far_sum + jnp.einsum(
        "igkf,gkf->igk", phi_query, norm_rest, preferred_element_type=jnp.float32
    )
    head_factor = factor[None, :, :, None]
    numerator = head_factor * window_num + (1.0 - head_factor) * (near_num + far_num)
    denominator = factor[None] * jnp.transpose(window_sum, (2, 0, 1)) + (1.0 - factor[None]) * (
        jnp.transpose(near_sum, (2, 0, 1)) + far_sum
    )
    outputs = (numerator / denominator[..., None]).astype(jnp.bfloat16)
    result = outputs.reshape(tokens, heads * head_dim)
    return lax.all_to_all(result, "head", split_axis=0, concat_axis=1, tiled=True)


def solution(mesh):
    in_specs = (
        P("seq", "head"),
        P("seq", "head"),
        P("seq", "head"),
        P("seq"),
        P("head", None, None),
        P("head", None, None),
        P("head"),
    )
    out_specs = P(("seq", "head"), None)
    return jax.shard_map(body, mesh=mesh, in_specs=in_specs, out_specs=out_specs, check_vma=False)
```

```python
import math

import jax
import jax.numpy as jnp
from jax import lax
from jax.experimental import pallas as pl
from jax.sharding import PartitionSpec as P

WINDOW = 64
BLOCK = 512
SPAN = 256


def passed_along(value, axis, steps):
    count = lax.axis_size(axis)
    first, last = (max(0, -steps), min(count, count - steps))
    return lax.ppermute(value, axis, [(source, source + steps) for source in range(first, last)])


def angle_tables(positions, half):
    frequency = [500000.0 ** (-float(order) / half) for order in range(half)]
    coarse = jnp.asarray([4096.0 * value % (2.0 * math.pi) for value in frequency], jnp.float32)
    medium = jnp.asarray([64.0 * value % (2.0 * math.pi) for value in frequency], jnp.float32)
    finest = jnp.asarray(frequency, jnp.float32)
    upper = (positions // 4096).astype(jnp.float32)[:, None] * coarse[None, :]
    middle = (positions // 64 % 64).astype(jnp.float32)[:, None] * medium[None, :]
    lower = (positions % 64).astype(jnp.float32)[:, None] * finest[None, :]
    cos_high = jnp.cos(upper) * jnp.cos(middle) - jnp.sin(upper) * jnp.sin(middle)
    sin_high = jnp.sin(upper) * jnp.cos(middle) + jnp.cos(upper) * jnp.sin(middle)
    cosine = cos_high * jnp.cos(lower) - sin_high * jnp.sin(lower)
    sine = sin_high * jnp.cos(lower) + cos_high * jnp.sin(lower)
    return (cosine, sine)


def span_tables(offsets, half):
    frequency = [500000.0 ** (-float(order) / half) for order in range(half)]
    coarse = jnp.asarray([4096.0 * value % (2.0 * math.pi) for value in frequency], jnp.float32)
    medium = jnp.asarray([64.0 * value % (2.0 * math.pi) for value in frequency], jnp.float32)
    finest = jnp.asarray(frequency, jnp.float32)
    quarters = SPAN // 64
    upper = (offsets // 4096).astype(jnp.float32)[:, None] * coarse[None, :]
    middle_index = (offsets[:, None] // 64 + jnp.arange(quarters, dtype=jnp.int32)[None, :]) % 64
    middle = middle_index.astype(jnp.float32)[:, :, None] * medium[None, None, :]
    lower = jnp.arange(64, dtype=jnp.float32)[:, None] * finest[None, :]
    cos_upper = jnp.cos(upper)[:, None, :]
    sin_upper = jnp.sin(upper)[:, None, :]
    cos_high = cos_upper * jnp.cos(middle) - sin_upper * jnp.sin(middle)
    sin_high = sin_upper * jnp.cos(middle) + cos_upper * jnp.sin(middle)
    cos_high = cos_high[:, :, None, :]
    sin_high = sin_high[:, :, None, :]
    cos_lower = jnp.cos(lower)[None, None]
    sin_lower = jnp.sin(lower)[None, None]
    cosine = cos_high * cos_lower - sin_high * sin_lower
    sine = sin_high * cos_lower + cos_high * sin_lower
    return (cosine.reshape(-1, half), sine.reshape(-1, half))


def rotate(rows, cosine, sine):
    half = rows.shape[-1] // 2
    first = rows[..., :half]
    second = rows[..., half:]
    cos_rows = cosine[:, None, :]
    sin_rows = sine[:, None, :]
    return jnp.concatenate(
        [first * cos_rows - second * sin_rows, second * cos_rows + first * sin_rows], axis=-1
    )


def two_softmax(logits):
    return jnp.concatenate(
        [jax.nn.softmax(logits, axis=-1), jax.nn.softmax(-logits, axis=-1)], axis=-1
    )


def split_parts(full_value):
    high_part = full_value.astype(jnp.bfloat16)
    rest_part = (full_value - high_part.astype(jnp.float32)).astype(jnp.bfloat16)
    return (high_part, rest_part)


def key_features(ext_keys2, key_map_t, ext_values2, mask, lag):
    rows, dim = ext_keys2.shape
    heads, feat, _ = key_map_t.shape

    def kernel(k_ref, m_ref, v_ref, mask_ref, phi_ref, st_ref, nm_ref):
        keys = k_ref[...]
        live = mask_ref[...] > 0.0
        values = v_ref[0:lag, :]
        for head in range(heads):
            logits = lax.dot_general(
                m_ref[head], keys, (((1,), (1,)), ((), ())), preferred_element_type=jnp.float32
            )
            for place, sign in enumerate((1.0, -1.0)):
                shifted = sign * logits
                expo = jnp.exp(shifted - jnp.max(shifted, axis=0, keepdims=True))
                soft = expo / jnp.sum(expo, axis=0, keepdims=True)
                phi = jnp.where(live, soft, 0.0).astype(jnp.bfloat16)
                band = slice(place * feat, (place + 1) * feat)
                phi_ref[head, band, :] = phi
                lagged = phi[:, 0:lag]
                st_ref[head, band, :] = jnp.dot(lagged, values, preferred_element_type=jnp.float32)
                nm_ref[head, band, :] = jnp.sum(lagged.astype(jnp.float32), axis=1, keepdims=True)

    return pl.pallas_call(
        kernel,
        grid=(1,),
        in_specs=[
            pl.BlockSpec((rows, dim), lambda h: (0, 0)),
            pl.BlockSpec((heads, feat, dim), lambda h: (0, 0, 0)),
            pl.BlockSpec((rows, dim), lambda h: (0, 0)),
            pl.BlockSpec((1, rows), lambda h: (0, 0)),
        ],
        out_specs=[
            pl.BlockSpec((heads, 2 * feat, rows), lambda h: (0, 0, 0)),
            pl.BlockSpec((heads, 2 * feat, dim), lambda h: (0, 0, 0)),
            pl.BlockSpec((heads, 2 * feat, 1), lambda h: (0, 0, 0)),
        ],
        out_shape=[
            jax.ShapeDtypeStruct((heads, 2 * feat, rows), jnp.bfloat16),
            jax.ShapeDtypeStruct((heads, 2 * feat, dim), jnp.float32),
            jax.ShapeDtypeStruct((heads, 2 * feat, 1), jnp.float32),
        ],
    )(ext_keys2, key_map_t, ext_values2, mask)

def body(queries, keys, values, offsets, query_map, key_map, window_logit):
    tokens = queries.shape[0]
    heads = query_map.shape[0]
    head_dim = query_map.shape[1]
    feat = query_map.shape[2]
    kv_local = keys.shape[1] // head_dim
    group = heads // kv_local
    blocks = tokens // BLOCK
    extent = BLOCK + WINDOW
    cosine, sine = span_tables(offsets, head_dim // 2)
    rot_k = rotate(
        keys.reshape(tokens, kv_local, head_dim).astype(jnp.float32), cosine, sine
    ).astype(jnp.bfloat16)
    value_rows = values.reshape(tokens, kv_local, head_dim)
    tail_both = passed_along(
        jnp.concatenate([rot_k[tokens - WINDOW :], value_rows[tokens - WINDOW :]], axis=-1),
        "seq",
        1,
    )
    tail_keys = tail_both[..., :head_dim]
    tail_values = tail_both[..., head_dim:]
    ext_keys = jnp.concatenate([tail_keys, rot_k], axis=0)
    ext_values = jnp.concatenate([tail_values, value_rows], axis=0)
    valid = (jnp.arange(tokens + WINDOW) >= WINDOW) | (lax.axis_index("seq") > 0)
    ext_rows = tokens + WINDOW
    phi_heads, state_heads, norm_heads = key_features(
        ext_keys.reshape(ext_rows, head_dim),
        jnp.transpose(key_map, (0, 2, 1)),
        ext_values.reshape(ext_rows, head_dim),
        valid.astype(jnp.float32)[None, :],
        tokens,
    )
    phi_key = phi_heads.reshape(kv_local, group, 2 * feat, ext_rows)
    block_states = state_heads.reshape(1, kv_local, group, 2 * feat, head_dim)
    block_norms = norm_heads.reshape(1, kv_local, group, 2 * feat)
    total_state = jnp.sum(block_states, axis=0)
    total_norm = jnp.sum(block_norms, axis=0)
    before_state = jnp.concatenate(
        [jnp.zeros_like(block_states), jnp.cumsum(block_states, axis=0)[:-1]], axis=0
    )
    before_norm = jnp.concatenate(
        [jnp.zeros_like(block_norms), jnp.cumsum(block_norms, axis=0)[:-1]], axis=0
    )
    state_shape = total_state.shape
    state_size = total_state.size
    packed = jnp.concatenate([total_state.reshape(-1), total_norm.reshape(-1)])
    count = lax.axis_size("seq")
    shifts = []
    steps = 1
    while steps < count:
        shifts.append(steps)
        steps *= 2
    half = len(shifts) // 2 + 1
    orders = (shifts, shifts[half:] + shifts[:half])
    middle = packed.size // 2
    pieces = []
    for order, piece in zip(orders, lax.optimization_barrier((packed[:middle], packed[middle:]))):
        inclusive = piece
        exclusive = jnp.zeros_like(piece)
        for place, shift in enumerate(order):
            received = passed_along(inclusive, "seq", shift)
            if not pieces and place == 1:
                first_received = received
            exclusive = exclusive + received
            if place + 1 < len(order):
                inclusive = inclusive + received
        pieces.append(exclusive)
    exclusive = jnp.concatenate(pieces)
    queries, first_received = lax.optimization_barrier((queries, first_received))
    rot_q = rotate(
        queries.reshape(tokens, heads, head_dim).astype(jnp.float32), cosine, sine
    ).astype(jnp.bfloat16)
    query_logits = jnp.einsum("nhd,hdf->nhf", rot_q, query_map, preferred_element_type=jnp.float32)
    phi_query = (
        two_softmax(query_logits).astype(jnp.bfloat16).reshape(tokens, kv_local, group, 2 * feat)
    )
    prior_state = exclusive[:state_size].reshape(state_shape)
    prior_norm = exclusive[state_size:].reshape(total_norm.shape)
    factor = jax.nn.sigmoid(window_logit).reshape(kv_local, group)
    rot_grouped = rot_q.reshape(tokens, kv_local, group, head_dim)
    row_index = jnp.arange(BLOCK)[:, None]
    col_index = jnp.arange(extent)[None, :]
    window_mask = (col_index > row_index) & (col_index <= row_index + WINDOW)
    linear_mask = col_index <= row_index
    live = valid[None, :]
    scores = jnp.einsum(
        "igkd,jgd->gkij", rot_grouped, ext_keys, preferred_element_type=jnp.float32
    ) / math.sqrt(head_dim)
    near_window = window_mask & live
    peak = jnp.max(jnp.where(near_window, scores, -jnp.inf), axis=-1, keepdims=True)
    weights = jnp.where(near_window, jnp.exp(scores - peak), 0.0)
    window_sum = jnp.sum(weights, axis=-1)
    affinity = jnp.einsum("igkf,gkfj->gkij", phi_query, phi_key, preferred_element_type=jnp.float32)
    affinity = jnp.where(linear_mask & live, affinity, 0.0)
    near_sum = jnp.sum(affinity, axis=-1)
    window_num = jnp.einsum(
        "gkij,jgd->igkd",
        weights.astype(jnp.bfloat16),
        ext_values,
        preferred_element_type=jnp.float32,
    )
    near_num = jnp.einsum(
        "gkij,jgd->igkd",
        affinity.astype(jnp.bfloat16),
        ext_values,
        preferred_element_type=jnp.float32,
    )
    state_now = prior_state + before_state[0]
    norm_now = prior_norm + before_norm[0]
    state_high, state_rest = split_parts(state_now)
    norm_high, norm_rest = split_parts(norm_now)
    far_num = jnp.einsum(
        "igkf,gkfd->igkd", phi_query, state_high, preferred_element_type=jnp.float32
    )
    far_num = far_num + jnp.einsum(
        "igkf,gkfd->igkd", phi_query, state_rest, preferred_element_type=jnp.float32
    )
    far_sum = jnp.einsum("igkf,gkf->igk", phi_query, norm_high, preferred_element_type=jnp.float32)
    far_sum = far_sum + jnp.einsum(
        "igkf,gkf->igk", phi_query, norm_rest, preferred_element_type=jnp.float32
    )
    head_factor = factor[None, :, :, None]
    numerator = head_factor * window_num + (1.0 - head_factor) * (near_num + far_num)
    denominator = factor[None] * jnp.transpose(window_sum, (2, 0, 1)) + (1.0 - factor[None]) * (
        jnp.transpose(near_sum, (2, 0, 1)) + far_sum
    )
    outputs = (numerator / denominator[..., None]).astype(jnp.bfloat16)
    result = outputs.reshape(tokens, heads * head_dim)
    return lax.all_to_all(result, "head", split_axis=0, concat_axis=1, tiled=True)


def solution(mesh):
    in_specs = (
        P("seq", "head"),
        P("seq", "head"),
        P("seq", "head"),
        P("seq"),
        P("head", None, None),
        P("head", None, None),
        P("head"),
    )
    out_specs = P(("seq", "head"), None)
    return jax.shard_map(body, mesh=mesh, in_specs=in_specs, out_specs=out_specs, check_vma=False)
```

```python
import math

import jax
import jax.numpy as jnp
from jax import lax
from jax.experimental import pallas as pl
from jax.sharding import PartitionSpec as P

WINDOW = 64
BLOCK = 512
SPAN = 256


def passed_along(value, axis, steps):
    count = lax.axis_size(axis)
    first, last = (max(0, -steps), min(count, count - steps))
    return lax.ppermute(value, axis, [(source, source + steps) for source in range(first, last)])


def angle_tables(positions, half):
    frequency = [500000.0 ** (-float(order) / half) for order in range(half)]
    coarse = jnp.asarray([4096.0 * value % (2.0 * math.pi) for value in frequency], jnp.float32)
    medium = jnp.asarray([64.0 * value % (2.0 * math.pi) for value in frequency], jnp.float32)
    finest = jnp.asarray(frequency, jnp.float32)
    upper = (positions // 4096).astype(jnp.float32)[:, None] * coarse[None, :]
    middle = (positions // 64 % 64).astype(jnp.float32)[:, None] * medium[None, :]
    lower = (positions % 64).astype(jnp.float32)[:, None] * finest[None, :]
    cos_high = jnp.cos(upper) * jnp.cos(middle) - jnp.sin(upper) * jnp.sin(middle)
    sin_high = jnp.sin(upper) * jnp.cos(middle) + jnp.cos(upper) * jnp.sin(middle)
    cosine = cos_high * jnp.cos(lower) - sin_high * jnp.sin(lower)
    sine = sin_high * jnp.cos(lower) + cos_high * jnp.sin(lower)
    return (cosine, sine)


def span_tables(offsets, half):
    frequency = [500000.0 ** (-float(order) / half) for order in range(half)]
    coarse = jnp.asarray([4096.0 * value % (2.0 * math.pi) for value in frequency], jnp.float32)
    medium = jnp.asarray([64.0 * value % (2.0 * math.pi) for value in frequency], jnp.float32)
    finest = jnp.asarray(frequency, jnp.float32)
    quarters = SPAN // 64
    upper = (offsets // 4096).astype(jnp.float32)[:, None] * coarse[None, :]
    middle_index = (offsets[:, None] // 64 + jnp.arange(quarters, dtype=jnp.int32)[None, :]) % 64
    middle = middle_index.astype(jnp.float32)[:, :, None] * medium[None, None, :]
    lower = jnp.arange(64, dtype=jnp.float32)[:, None] * finest[None, :]
    cos_upper = jnp.cos(upper)[:, None, :]
    sin_upper = jnp.sin(upper)[:, None, :]
    cos_high = cos_upper * jnp.cos(middle) - sin_upper * jnp.sin(middle)
    sin_high = sin_upper * jnp.cos(middle) + cos_upper * jnp.sin(middle)
    cos_high = cos_high[:, :, None, :]
    sin_high = sin_high[:, :, None, :]
    cos_lower = jnp.cos(lower)[None, None]
    sin_lower = jnp.sin(lower)[None, None]
    cosine = cos_high * cos_lower - sin_high * sin_lower
    sine = sin_high * cos_lower + cos_high * sin_lower
    return (cosine.reshape(-1, half), sine.reshape(-1, half))


def rotate(rows, cosine, sine):
    half = rows.shape[-1] // 2
    first = rows[..., :half]
    second = rows[..., half:]
    cos_rows = cosine[:, None, :]
    sin_rows = sine[:, None, :]
    return jnp.concatenate(
        [first * cos_rows - second * sin_rows, second * cos_rows + first * sin_rows], axis=-1
    )


def two_softmax(logits):
    return jnp.concatenate(
        [jax.nn.softmax(logits, axis=-1), jax.nn.softmax(-logits, axis=-1)], axis=-1
    )


def split_parts(full_value):
    high_part = full_value.astype(jnp.bfloat16)
    rest_part = (full_value - high_part.astype(jnp.float32)).astype(jnp.bfloat16)
    return (high_part, rest_part)


def key_features(ext_keys2, key_map_t, ext_values2, mask, lag):
    rows, dim = ext_keys2.shape
    heads, feat, _ = key_map_t.shape

    def kernel(k_ref, m_ref, v_ref, mask_ref, phi_ref, st_ref, nm_ref):
        keys = k_ref[...]
        live = mask_ref[...] > 0.0
        values = v_ref[0:lag, :]
        for head in range(heads):
            logits = lax.dot_general(
                m_ref[head], keys, (((1,), (1,)), ((), ())), preferred_element_type=jnp.float32
            )
            for place, sign in enumerate((1.0, -1.0)):
                shifted = sign * logits
                expo = jnp.exp(shifted - jnp.max(shifted, axis=0, keepdims=True))
                soft = expo / jnp.sum(expo, axis=0, keepdims=True)
                phi = jnp.where(live, soft, 0.0).astype(jnp.bfloat16)
                band = slice(place * feat, (place + 1) * feat)
                phi_ref[head, band, :] = phi
                lagged = phi[:, 0:lag]
                st_ref[head, band, :] = jnp.dot(lagged, values, preferred_element_type=jnp.float32)
                nm_ref[head, band, :] = jnp.sum(lagged.astype(jnp.float32), axis=1, keepdims=True)

    return pl.pallas_call(
        kernel,
        grid=(1,),
        in_specs=[
            pl.BlockSpec((rows, dim), lambda h: (0, 0)),
            pl.BlockSpec((heads, feat, dim), lambda h: (0, 0, 0)),
            pl.BlockSpec((rows, dim), lambda h: (0, 0)),
            pl.BlockSpec((1, rows), lambda h: (0, 0)),
        ],
        out_specs=[
            pl.BlockSpec((heads, 2 * feat, rows), lambda h: (0, 0, 0)),
            pl.BlockSpec((heads, 2 * feat, dim), lambda h: (0, 0, 0)),
            pl.BlockSpec((heads, 2 * feat, 1), lambda h: (0, 0, 0)),
        ],
        out_shape=[
            jax.ShapeDtypeStruct((heads, 2 * feat, rows), jnp.bfloat16),
            jax.ShapeDtypeStruct((heads, 2 * feat, dim), jnp.float32),
            jax.ShapeDtypeStruct((heads, 2 * feat, 1), jnp.float32),
        ],
    )(ext_keys2, key_map_t, ext_values2, mask)

def body(queries, keys, values, offsets, query_map, key_map, window_logit):
    tokens = queries.shape[0]
    heads = query_map.shape[0]
    head_dim = query_map.shape[1]
    feat = query_map.shape[2]
    kv_local = keys.shape[1] // head_dim
    group = heads // kv_local
    blocks = tokens // BLOCK
    extent = BLOCK + WINDOW
    cosine, sine = span_tables(offsets, head_dim // 2)
    rot_k = rotate(
        keys.reshape(tokens, kv_local, head_dim).astype(jnp.float32), cosine, sine
    ).astype(jnp.bfloat16)
    value_rows = values.reshape(tokens, kv_local, head_dim)
    tail_keys, tail_values = passed_along(
        (rot_k[tokens - WINDOW :], value_rows[tokens - WINDOW :]), "seq", 1
    )
    ext_keys = jnp.concatenate([tail_keys, rot_k], axis=0)
    ext_values = jnp.concatenate([tail_values, value_rows], axis=0)
    valid = (jnp.arange(tokens + WINDOW) >= WINDOW) | (lax.axis_index("seq") > 0)
    ext_rows = tokens + WINDOW
    phi_heads, state_heads, norm_heads = key_features(
        ext_keys.reshape(ext_rows, head_dim),
        jnp.transpose(key_map, (0, 2, 1)),
        ext_values.reshape(ext_rows, head_dim),
        valid.astype(jnp.float32)[None, :],
        tokens,
    )
    phi_key = phi_heads.reshape(kv_local, group, 2 * feat, ext_rows)
    block_states = state_heads.reshape(1, kv_local, group, 2 * feat, head_dim)
    block_norms = norm_heads.reshape(1, kv_local, group, 2 * feat)
    total_state = jnp.sum(block_states, axis=0)
    total_norm = jnp.sum(block_norms, axis=0)
    before_state = jnp.concatenate(
        [jnp.zeros_like(block_states), jnp.cumsum(block_states, axis=0)[:-1]], axis=0
    )
    before_norm = jnp.concatenate(
        [jnp.zeros_like(block_norms), jnp.cumsum(block_norms, axis=0)[:-1]], axis=0
    )
    state_shape = total_state.shape
    state_size = total_state.size
    packed = jnp.concatenate([total_state.reshape(-1), total_norm.reshape(-1)])
    count = lax.axis_size("seq")
    shifts = []
    steps = 1
    while steps < count:
        shifts.append(steps)
        steps *= 2
    half = len(shifts) // 2 + 1
    orders = (shifts, shifts[half:] + shifts[:half])
    middle = packed.size // 2
    pieces = []
    for order, piece in zip(orders, (packed[:middle], packed[middle:])):
        inclusive = piece
        exclusive = jnp.zeros_like(piece)
        for place, shift in enumerate(order):
            received = passed_along(inclusive, "seq", shift)
            if not pieces and place == 0:
                first_received = received
            exclusive = exclusive + received
            if place + 1 < len(order):
                inclusive = inclusive + received
        pieces.append(exclusive)
    exclusive = jnp.concatenate(pieces)
    queries, first_received = lax.optimization_barrier((queries, first_received))
    rot_q = rotate(
        queries.reshape(tokens, heads, head_dim).astype(jnp.float32), cosine, sine
    ).astype(jnp.bfloat16)
    query_logits = jnp.einsum("nhd,hdf->nhf", rot_q, query_map, preferred_element_type=jnp.float32)
    phi_query = (
        two_softmax(query_logits).astype(jnp.bfloat16).reshape(tokens, kv_local, group, 2 * feat)
    )
    prior_state = exclusive[:state_size].reshape(state_shape)
    prior_norm = exclusive[state_size:].reshape(total_norm.shape)
    factor = jax.nn.sigmoid(window_logit).reshape(kv_local, group)
    rot_grouped = rot_q.reshape(tokens, kv_local, group, head_dim)
    row_index = jnp.arange(BLOCK)[:, None]
    col_index = jnp.arange(extent)[None, :]
    window_mask = (col_index > row_index) & (col_index <= row_index + WINDOW)
    linear_mask = col_index <= row_index
    live = valid[None, :]
    scores = jnp.einsum(
        "igkd,jgd->gkij", rot_grouped, ext_keys, preferred_element_type=jnp.float32
    ) / math.sqrt(head_dim)
    near_window = window_mask & live
    peak = jnp.max(jnp.where(near_window, scores, -jnp.inf), axis=-1, keepdims=True)
    weights = jnp.where(near_window, jnp.exp(scores - peak), 0.0)
    window_sum = jnp.sum(weights, axis=-1)
    affinity = jnp.einsum("igkf,gkfj->gkij", phi_query, phi_key, preferred_element_type=jnp.float32)
    affinity = jnp.where(linear_mask & live, affinity, 0.0)
    near_sum = jnp.sum(affinity, axis=-1)
    window_num = jnp.einsum(
        "gkij,jgd->igkd",
        weights.astype(jnp.bfloat16),
        ext_values,
        preferred_element_type=jnp.float32,
    )
    near_num = jnp.einsum(
        "gkij,jgd->igkd",
        affinity.astype(jnp.bfloat16),
        ext_values,
        preferred_element_type=jnp.float32,
    )
    head_factor = factor[None, :, :, None]
    local_num = head_factor * window_num + (1.0 - head_factor) * near_num
    local_den = factor[None] * jnp.transpose(window_sum, (2, 0, 1)) + (1.0 - factor[None]) * (
        jnp.transpose(near_sum, (2, 0, 1))
    )
    state_now = prior_state + before_state[0]
    norm_now = prior_norm + before_norm[0]
    state_high, state_rest = split_parts(state_now)
    norm_high, norm_rest = split_parts(norm_now)
    far_num = jnp.einsum(
        "igkf,gkfd->igkd", phi_query, state_high, preferred_element_type=jnp.float32
    )
    far_num = far_num + jnp.einsum(
        "igkf,gkfd->igkd", phi_query, state_rest, preferred_element_type=jnp.float32
    )
    far_sum = jnp.einsum("igkf,gkf->igk", phi_query, norm_high, preferred_element_type=jnp.float32)
    far_sum = far_sum + jnp.einsum(
        "igkf,gkf->igk", phi_query, norm_rest, preferred_element_type=jnp.float32
    )
    numerator = local_num + (1.0 - head_factor) * far_num
    denominator = local_den + (1.0 - factor[None]) * far_sum
    outputs = (numerator / denominator[..., None]).astype(jnp.bfloat16)
    result = outputs.reshape(tokens, heads * head_dim)
    return lax.all_to_all(result, "head", split_axis=0, concat_axis=1, tiled=True)


def solution(mesh):
    in_specs = (
        P("seq", "head"),
        P("seq", "head"),
        P("seq", "head"),
        P("seq"),
        P("head", None, None),
        P("head", None, None),
        P("head"),
    )
    out_specs = P(("seq", "head"), None)
    return jax.shard_map(body, mesh=mesh, in_specs=in_specs, out_specs=out_specs, check_vma=False)
```

```python
import math

import jax
import jax.numpy as jnp
from jax import lax
from jax.experimental import pallas as pl
from jax.sharding import PartitionSpec as P

WINDOW = 64
BLOCK = 512
SPAN = 256


def passed_along(value, axis, steps):
    count = lax.axis_size(axis)
    first, last = (max(0, -steps), min(count, count - steps))
    return lax.ppermute(value, axis, [(source, source + steps) for source in range(first, last)])


def angle_tables(positions, half):
    frequency = [500000.0 ** (-float(order) / half) for order in range(half)]
    coarse = jnp.asarray([4096.0 * value % (2.0 * math.pi) for value in frequency], jnp.float32)
    medium = jnp.asarray([64.0 * value % (2.0 * math.pi) for value in frequency], jnp.float32)
    finest = jnp.asarray(frequency, jnp.float32)
    upper = (positions // 4096).astype(jnp.float32)[:, None] * coarse[None, :]
    middle = (positions // 64 % 64).astype(jnp.float32)[:, None] * medium[None, :]
    lower = (positions % 64).astype(jnp.float32)[:, None] * finest[None, :]
    cos_high = jnp.cos(upper) * jnp.cos(middle) - jnp.sin(upper) * jnp.sin(middle)
    sin_high = jnp.sin(upper) * jnp.cos(middle) + jnp.cos(upper) * jnp.sin(middle)
    cosine = cos_high * jnp.cos(lower) - sin_high * jnp.sin(lower)
    sine = sin_high * jnp.cos(lower) + cos_high * jnp.sin(lower)
    return (cosine, sine)


def span_tables(offsets, half):
    frequency = [500000.0 ** (-float(order) / half) for order in range(half)]
    coarse = jnp.asarray([4096.0 * value % (2.0 * math.pi) for value in frequency], jnp.float32)
    medium = jnp.asarray([64.0 * value % (2.0 * math.pi) for value in frequency], jnp.float32)
    finest = jnp.asarray(frequency, jnp.float32)
    quarters = SPAN // 64
    upper = (offsets // 4096).astype(jnp.float32)[:, None] * coarse[None, :]
    middle_index = (offsets[:, None] // 64 + jnp.arange(quarters, dtype=jnp.int32)[None, :]) % 64
    middle = middle_index.astype(jnp.float32)[:, :, None] * medium[None, None, :]
    lower = jnp.arange(64, dtype=jnp.float32)[:, None] * finest[None, :]
    cos_upper = jnp.cos(upper)[:, None, :]
    sin_upper = jnp.sin(upper)[:, None, :]
    cos_high = cos_upper * jnp.cos(middle) - sin_upper * jnp.sin(middle)
    sin_high = sin_upper * jnp.cos(middle) + cos_upper * jnp.sin(middle)
    cos_high = cos_high[:, :, None, :]
    sin_high = sin_high[:, :, None, :]
    cos_lower = jnp.cos(lower)[None, None]
    sin_lower = jnp.sin(lower)[None, None]
    cosine = cos_high * cos_lower - sin_high * sin_lower
    sine = sin_high * cos_lower + cos_high * sin_lower
    return (cosine.reshape(-1, half), sine.reshape(-1, half))


def rotate(rows, cosine, sine):
    half = rows.shape[-1] // 2
    first = rows[..., :half]
    second = rows[..., half:]
    cos_rows = cosine[:, None, :]
    sin_rows = sine[:, None, :]
    return jnp.concatenate(
        [first * cos_rows - second * sin_rows, second * cos_rows + first * sin_rows], axis=-1
    )


def two_softmax(logits):
    return jnp.concatenate(
        [jax.nn.softmax(logits, axis=-1), jax.nn.softmax(-logits, axis=-1)], axis=-1
    )


def split_parts(full_value):
    high_part = full_value.astype(jnp.bfloat16)
    rest_part = (full_value - high_part.astype(jnp.float32)).astype(jnp.bfloat16)
    return (high_part, rest_part)


def key_features(ext_keys2, key_map_t, ext_values2, mask, lag):
    rows, dim = ext_keys2.shape
    heads, feat, _ = key_map_t.shape

    def kernel(k_ref, m_ref, v_ref, mask_ref, phi_ref, st_ref, nm_ref):
        keys = k_ref[...]
        live = mask_ref[...] > 0.0
        values = v_ref[0:lag, :]
        for head in range(heads):
            logits = lax.dot_general(
                m_ref[head], keys, (((1,), (1,)), ((), ())), preferred_element_type=jnp.float32
            )
            for place, sign in enumerate((1.0, -1.0)):
                shifted = sign * logits
                expo = jnp.exp(shifted - jnp.max(shifted, axis=0, keepdims=True))
                soft = expo / jnp.sum(expo, axis=0, keepdims=True)
                phi = jnp.where(live, soft, 0.0).astype(jnp.bfloat16)
                band = slice(place * feat, (place + 1) * feat)
                phi_ref[head, band, :] = phi
                lagged = phi[:, 0:lag]
                st_ref[head, band, :] = jnp.dot(lagged, values, preferred_element_type=jnp.float32)
                nm_ref[head, band, :] = jnp.sum(lagged.astype(jnp.float32), axis=1, keepdims=True)

    return pl.pallas_call(
        kernel,
        grid=(1,),
        in_specs=[
            pl.BlockSpec((rows, dim), lambda h: (0, 0)),
            pl.BlockSpec((heads, feat, dim), lambda h: (0, 0, 0)),
            pl.BlockSpec((rows, dim), lambda h: (0, 0)),
            pl.BlockSpec((1, rows), lambda h: (0, 0)),
        ],
        out_specs=[
            pl.BlockSpec((heads, 2 * feat, rows), lambda h: (0, 0, 0)),
            pl.BlockSpec((heads, 2 * feat, dim), lambda h: (0, 0, 0)),
            pl.BlockSpec((heads, 2 * feat, 1), lambda h: (0, 0, 0)),
        ],
        out_shape=[
            jax.ShapeDtypeStruct((heads, 2 * feat, rows), jnp.bfloat16),
            jax.ShapeDtypeStruct((heads, 2 * feat, dim), jnp.float32),
            jax.ShapeDtypeStruct((heads, 2 * feat, 1), jnp.float32),
        ],
    )(ext_keys2, key_map_t, ext_values2, mask)

def body(queries, keys, values, offsets, query_map, key_map, window_logit):
    tokens = queries.shape[0]
    heads = query_map.shape[0]
    head_dim = query_map.shape[1]
    feat = query_map.shape[2]
    kv_local = keys.shape[1] // head_dim
    group = heads // kv_local
    blocks = tokens // BLOCK
    extent = BLOCK + WINDOW
    cosine, sine = span_tables(offsets, head_dim // 2)
    rot_k = rotate(
        keys.reshape(tokens, kv_local, head_dim).astype(jnp.float32), cosine, sine
    ).astype(jnp.bfloat16)
    value_rows = values.reshape(tokens, kv_local, head_dim)
    tail_keys, tail_values = passed_along(
        (rot_k[tokens - WINDOW :], value_rows[tokens - WINDOW :]), "seq", 1
    )
    ext_keys = jnp.concatenate([tail_keys, rot_k], axis=0)
    ext_values = jnp.concatenate([tail_values, value_rows], axis=0)
    valid = (jnp.arange(tokens + WINDOW) >= WINDOW) | (lax.axis_index("seq") > 0)
    ext_rows = tokens + WINDOW
    phi_heads, state_heads, norm_heads = key_features(
        ext_keys.reshape(ext_rows, head_dim),
        jnp.transpose(key_map, (0, 2, 1)),
        ext_values.reshape(ext_rows, head_dim),
        valid.astype(jnp.float32)[None, :],
        tokens,
    )
    phi_key = phi_heads.reshape(kv_local, group, 2 * feat, ext_rows)
    block_states = state_heads.reshape(1, kv_local, group, 2 * feat, head_dim)
    block_norms = norm_heads.reshape(1, kv_local, group, 2 * feat)
    total_state = jnp.sum(block_states, axis=0)
    total_norm = jnp.sum(block_norms, axis=0)
    before_state = jnp.concatenate(
        [jnp.zeros_like(block_states), jnp.cumsum(block_states, axis=0)[:-1]], axis=0
    )
    before_norm = jnp.concatenate(
        [jnp.zeros_like(block_norms), jnp.cumsum(block_norms, axis=0)[:-1]], axis=0
    )
    state_shape = total_state.shape
    state_size = total_state.size
    packed = jnp.concatenate([total_state.reshape(-1), total_norm.reshape(-1)])
    count = lax.axis_size("seq")
    shifts = []
    steps = 1
    while steps < count:
        shifts.append(steps)
        steps *= 2
    half = len(shifts) // 2 + 1
    orders = (shifts, shifts[half:] + shifts[:half])
    middle = packed.size // 2
    pieces = []
    for order, piece in zip(orders, (packed[:middle], packed[middle:])):
        inclusive = piece
        exclusive = jnp.zeros_like(piece)
        for place, shift in enumerate(order):
            received = passed_along(inclusive, "seq", shift)
            if not pieces and place == 0:
                first_received = received
            exclusive = exclusive + received
            if place + 1 < len(order):
                inclusive = inclusive + received
        pieces.append(exclusive)
    exclusive = jnp.concatenate(pieces)
    queries, first_received = lax.optimization_barrier((queries, first_received))
    rot_q = rotate(
        queries.reshape(tokens, heads, head_dim).astype(jnp.float32), cosine, sine
    ).astype(jnp.bfloat16)
    query_logits = jnp.einsum("nhd,hdf->nhf", rot_q, query_map, preferred_element_type=jnp.float32)
    phi_query = (
        two_softmax(query_logits).astype(jnp.bfloat16).reshape(tokens, kv_local, group, 2 * feat)
    )
    prior_state = exclusive[:state_size].reshape(state_shape)
    prior_norm = exclusive[state_size:].reshape(total_norm.shape)
    factor = jax.nn.sigmoid(window_logit).reshape(kv_local, group)
    rot_grouped = rot_q.reshape(tokens, kv_local, group, head_dim)
    row_index = jnp.arange(BLOCK)[:, None]
    col_index = jnp.arange(extent)[None, :]
    window_mask = (col_index > row_index) & (col_index <= row_index + WINDOW)
    linear_mask = col_index <= row_index
    live = valid[None, :]
    scores = jnp.einsum(
        "igkd,jgd->gkij", rot_grouped, ext_keys, preferred_element_type=jnp.float32
    ) / math.sqrt(head_dim)
    near_window = window_mask & live
    peak = jnp.max(jnp.where(near_window, scores, -jnp.inf), axis=-1, keepdims=True)
    weights = jnp.where(near_window, jnp.exp(scores - peak), 0.0)
    window_sum = jnp.sum(weights, axis=-1)
    affinity = jnp.einsum("igkf,gkfj->gkij", phi_query, phi_key, preferred_element_type=jnp.float32)
    affinity = jnp.where(linear_mask & live, affinity, 0.0)
    near_sum = jnp.sum(affinity, axis=-1)
    window_num = jnp.einsum(
        "gkij,jgd->igkd",
        weights.astype(jnp.bfloat16),
        ext_values,
        preferred_element_type=jnp.float32,
    )
    near_num = jnp.einsum(
        "gkij,jgd->igkd",
        affinity.astype(jnp.bfloat16),
        ext_values,
        preferred_element_type=jnp.float32,
    )
    head_factor = factor[None, :, :, None]
    local_num = head_factor * window_num + (1.0 - head_factor) * near_num
    local_den = factor[None] * jnp.transpose(window_sum, (2, 0, 1)) + (1.0 - factor[None]) * (
        jnp.transpose(near_sum, (2, 0, 1))
    )
    local_num, local_den = lax.optimization_barrier((local_num, local_den))
    state_now = prior_state + before_state[0]
    norm_now = prior_norm + before_norm[0]
    state_high, state_rest = split_parts(state_now)
    norm_high, norm_rest = split_parts(norm_now)
    far_num = jnp.einsum(
        "igkf,gkfd->igkd", phi_query, state_high, preferred_element_type=jnp.float32
    )
    far_num = far_num + jnp.einsum(
        "igkf,gkfd->igkd", phi_query, state_rest, preferred_element_type=jnp.float32
    )
    far_sum = jnp.einsum("igkf,gkf->igk", phi_query, norm_high, preferred_element_type=jnp.float32)
    far_sum = far_sum + jnp.einsum(
        "igkf,gkf->igk", phi_query, norm_rest, preferred_element_type=jnp.float32
    )
    numerator = local_num + (1.0 - head_factor) * far_num
    denominator = local_den + (1.0 - factor[None]) * far_sum
    outputs = (numerator / denominator[..., None]).astype(jnp.bfloat16)
    result = outputs.reshape(tokens, heads * head_dim)
    return lax.all_to_all(result, "head", split_axis=0, concat_axis=1, tiled=True)


def solution(mesh):
    in_specs = (
        P("seq", "head"),
        P("seq", "head"),
        P("seq", "head"),
        P("seq"),
        P("head", None, None),
        P("head", None, None),
        P("head"),
    )
    out_specs = P(("seq", "head"), None)
    return jax.shard_map(body, mesh=mesh, in_specs=in_specs, out_specs=out_specs, check_vma=False)
```

```python
import math

import jax
import jax.numpy as jnp
from jax import lax
from jax.experimental import pallas as pl
from jax.sharding import PartitionSpec as P

WINDOW = 64
BLOCK = 512
SPAN = 256


def passed_along(value, axis, steps):
    count = lax.axis_size(axis)
    first, last = (max(0, -steps), min(count, count - steps))
    return lax.ppermute(value, axis, [(source, source + steps) for source in range(first, last)])


def angle_tables(positions, half):
    frequency = [500000.0 ** (-float(order) / half) for order in range(half)]
    coarse = jnp.asarray([4096.0 * value % (2.0 * math.pi) for value in frequency], jnp.float32)
    medium = jnp.asarray([64.0 * value % (2.0 * math.pi) for value in frequency], jnp.float32)
    finest = jnp.asarray(frequency, jnp.float32)
    upper = (positions // 4096).astype(jnp.float32)[:, None] * coarse[None, :]
    middle = (positions // 64 % 64).astype(jnp.float32)[:, None] * medium[None, :]
    lower = (positions % 64).astype(jnp.float32)[:, None] * finest[None, :]
    cos_high = jnp.cos(upper) * jnp.cos(middle) - jnp.sin(upper) * jnp.sin(middle)
    sin_high = jnp.sin(upper) * jnp.cos(middle) + jnp.cos(upper) * jnp.sin(middle)
    cosine = cos_high * jnp.cos(lower) - sin_high * jnp.sin(lower)
    sine = sin_high * jnp.cos(lower) + cos_high * jnp.sin(lower)
    return (cosine, sine)


def span_tables(offsets, half):
    frequency = [500000.0 ** (-float(order) / half) for order in range(half)]
    coarse = jnp.asarray([4096.0 * value % (2.0 * math.pi) for value in frequency], jnp.float32)
    medium = jnp.asarray([64.0 * value % (2.0 * math.pi) for value in frequency], jnp.float32)
    finest = jnp.asarray(frequency, jnp.float32)
    quarters = SPAN // 64
    upper = (offsets // 4096).astype(jnp.float32)[:, None] * coarse[None, :]
    middle_index = (offsets[:, None] // 64 + jnp.arange(quarters, dtype=jnp.int32)[None, :]) % 64
    middle = middle_index.astype(jnp.float32)[:, :, None] * medium[None, None, :]
    lower = jnp.arange(64, dtype=jnp.float32)[:, None] * finest[None, :]
    cos_upper = jnp.cos(upper)[:, None, :]
    sin_upper = jnp.sin(upper)[:, None, :]
    cos_high = cos_upper * jnp.cos(middle) - sin_upper * jnp.sin(middle)
    sin_high = sin_upper * jnp.cos(middle) + cos_upper * jnp.sin(middle)
    cos_high = cos_high[:, :, None, :]
    sin_high = sin_high[:, :, None, :]
    cos_lower = jnp.cos(lower)[None, None]
    sin_lower = jnp.sin(lower)[None, None]
    cosine = cos_high * cos_lower - sin_high * sin_lower
    sine = sin_high * cos_lower + cos_high * sin_lower
    return (cosine.reshape(-1, half), sine.reshape(-1, half))


def rotate(rows, cosine, sine):
    half = rows.shape[-1] // 2
    first = rows[..., :half]
    second = rows[..., half:]
    cos_rows = cosine[:, None, :]
    sin_rows = sine[:, None, :]
    return jnp.concatenate(
        [first * cos_rows - second * sin_rows, second * cos_rows + first * sin_rows], axis=-1
    )


def two_softmax(logits):
    return jnp.concatenate(
        [jax.nn.softmax(logits, axis=-1), jax.nn.softmax(-logits, axis=-1)], axis=-1
    )


def split_parts(full_value):
    high_part = full_value.astype(jnp.bfloat16)
    rest_part = (full_value - high_part.astype(jnp.float32)).astype(jnp.bfloat16)
    return (high_part, rest_part)


def key_features(ext_keys2, key_map_t, ext_values2, mask, lag):
    rows, dim = ext_keys2.shape
    heads, feat, _ = key_map_t.shape

    def kernel(k_ref, m_ref, v_ref, mask_ref, phi_ref, st_ref, nm_ref):
        keys = k_ref[...]
        live = mask_ref[...] > 0.0
        values = v_ref[0:lag, :]
        for head in range(heads):
            logits = lax.dot_general(
                m_ref[head], keys, (((1,), (1,)), ((), ())), preferred_element_type=jnp.float32
            )
            for place, sign in enumerate((1.0, -1.0)):
                shifted = sign * logits
                expo = jnp.exp(shifted - jnp.max(shifted, axis=0, keepdims=True))
                soft = expo / jnp.sum(expo, axis=0, keepdims=True)
                phi = jnp.where(live, soft, 0.0).astype(jnp.bfloat16)
                band = slice(place * feat, (place + 1) * feat)
                phi_ref[head, band, :] = phi
                lagged = phi[:, 0:lag]
                st_ref[head, band, :] = jnp.dot(lagged, values, preferred_element_type=jnp.float32)
                nm_ref[head, band, :] = jnp.sum(lagged.astype(jnp.float32), axis=1, keepdims=True)

    return pl.pallas_call(
        kernel,
        grid=(1,),
        in_specs=[
            pl.BlockSpec((rows, dim), lambda h: (0, 0)),
            pl.BlockSpec((heads, feat, dim), lambda h: (0, 0, 0)),
            pl.BlockSpec((rows, dim), lambda h: (0, 0)),
            pl.BlockSpec((1, rows), lambda h: (0, 0)),
        ],
        out_specs=[
            pl.BlockSpec((heads, 2 * feat, rows), lambda h: (0, 0, 0)),
            pl.BlockSpec((heads, 2 * feat, dim), lambda h: (0, 0, 0)),
            pl.BlockSpec((heads, 2 * feat, 1), lambda h: (0, 0, 0)),
        ],
        out_shape=[
            jax.ShapeDtypeStruct((heads, 2 * feat, rows), jnp.bfloat16),
            jax.ShapeDtypeStruct((heads, 2 * feat, dim), jnp.float32),
            jax.ShapeDtypeStruct((heads, 2 * feat, 1), jnp.float32),
        ],
    )(ext_keys2, key_map_t, ext_values2, mask)

def body(queries, keys, values, offsets, query_map, key_map, window_logit):
    tokens = queries.shape[0]
    heads = query_map.shape[0]
    head_dim = query_map.shape[1]
    feat = query_map.shape[2]
    kv_local = keys.shape[1] // head_dim
    group = heads // kv_local
    blocks = tokens // BLOCK
    extent = BLOCK + WINDOW
    cosine, sine = span_tables(offsets, head_dim // 2)
    rot_k = rotate(
        keys.reshape(tokens, kv_local, head_dim).astype(jnp.float32), cosine, sine
    ).astype(jnp.bfloat16)
    value_rows = values.reshape(tokens, kv_local, head_dim)
    tail_keys, tail_values = passed_along(
        (rot_k[tokens - WINDOW :], value_rows[tokens - WINDOW :]), "seq", 1
    )
    ext_keys = jnp.concatenate([tail_keys, rot_k], axis=0)
    ext_values = jnp.concatenate([tail_values, value_rows], axis=0)
    valid = (jnp.arange(tokens + WINDOW) >= WINDOW) | (lax.axis_index("seq") > 0)
    ext_rows = tokens + WINDOW
    phi_heads, state_heads, norm_heads = key_features(
        ext_keys.reshape(ext_rows, head_dim),
        jnp.transpose(key_map, (0, 2, 1)),
        ext_values.reshape(ext_rows, head_dim),
        valid.astype(jnp.float32)[None, :],
        tokens,
    )
    phi_key = phi_heads.reshape(kv_local, group, 2 * feat, ext_rows)
    block_states = state_heads.reshape(1, kv_local, group, 2 * feat, head_dim)
    block_norms = norm_heads.reshape(1, kv_local, group, 2 * feat)
    total_state = jnp.sum(block_states, axis=0)
    total_norm = jnp.sum(block_norms, axis=0)
    before_state = jnp.concatenate(
        [jnp.zeros_like(block_states), jnp.cumsum(block_states, axis=0)[:-1]], axis=0
    )
    before_norm = jnp.concatenate(
        [jnp.zeros_like(block_norms), jnp.cumsum(block_norms, axis=0)[:-1]], axis=0
    )
    state_shape = total_state.shape
    state_size = total_state.size
    packed = jnp.concatenate([total_state.reshape(-1), total_norm.reshape(-1)])
    count = lax.axis_size("seq")
    shifts = []
    steps = 1
    while steps < count:
        shifts.append(steps)
        steps *= 2
    half = len(shifts) // 2 + 1
    orders = (shifts, shifts[half:] + shifts[:half][::-1])
    middle = packed.size // 2
    pieces = []
    for order, piece in zip(orders, (packed[:middle], packed[middle:])):
        inclusive = piece
        exclusive = jnp.zeros_like(piece)
        for place, shift in enumerate(order):
            received = passed_along(inclusive, "seq", shift)
            if not pieces and place == 0:
                first_received = received
            exclusive = exclusive + received
            if place + 1 < len(order):
                inclusive = inclusive + received
        pieces.append(exclusive)
    exclusive = jnp.concatenate(pieces)
    queries, first_received = lax.optimization_barrier((queries, first_received))
    rot_q = rotate(
        queries.reshape(tokens, heads, head_dim).astype(jnp.float32), cosine, sine
    ).astype(jnp.bfloat16)
    query_logits = jnp.einsum("nhd,hdf->nhf", rot_q, query_map, preferred_element_type=jnp.float32)
    phi_query = (
        two_softmax(query_logits).astype(jnp.bfloat16).reshape(tokens, kv_local, group, 2 * feat)
    )
    prior_state = exclusive[:state_size].reshape(state_shape)
    prior_norm = exclusive[state_size:].reshape(total_norm.shape)
    factor = jax.nn.sigmoid(window_logit).reshape(kv_local, group)
    rot_grouped = rot_q.reshape(tokens, kv_local, group, head_dim)
    row_index = jnp.arange(BLOCK)[:, None]
    col_index = jnp.arange(extent)[None, :]
    window_mask = (col_index > row_index) & (col_index <= row_index + WINDOW)
    linear_mask = col_index <= row_index
    live = valid[None, :]
    scores = jnp.einsum(
        "igkd,jgd->gkij", rot_grouped, ext_keys, preferred_element_type=jnp.float32
    ) / math.sqrt(head_dim)
    near_window = window_mask & live
    peak = jnp.max(jnp.where(near_window, scores, -jnp.inf), axis=-1, keepdims=True)
    weights = jnp.where(near_window, jnp.exp(scores - peak), 0.0)
    window_sum = jnp.sum(weights, axis=-1)
    affinity = jnp.einsum("igkf,gkfj->gkij", phi_query, phi_key, preferred_element_type=jnp.float32)
    affinity = jnp.where(linear_mask & live, affinity, 0.0)
    near_sum = jnp.sum(affinity, axis=-1)
    window_num = jnp.einsum(
        "gkij,jgd->igkd",
        weights.astype(jnp.bfloat16),
        ext_values,
        preferred_element_type=jnp.float32,
    )
    near_num = jnp.einsum(
        "gkij,jgd->igkd",
        affinity.astype(jnp.bfloat16),
        ext_values,
        preferred_element_type=jnp.float32,
    )
    head_factor = factor[None, :, :, None]
    local_num = head_factor * window_num + (1.0 - head_factor) * near_num
    local_den = factor[None] * jnp.transpose(window_sum, (2, 0, 1)) + (1.0 - factor[None]) * (
        jnp.transpose(near_sum, (2, 0, 1))
    )
    local_num, local_den = lax.optimization_barrier((local_num, local_den))
    state_now = prior_state + before_state[0]
    norm_now = prior_norm + before_norm[0]
    state_high, state_rest = split_parts(state_now)
    norm_high, norm_rest = split_parts(norm_now)
    far_num = jnp.einsum(
        "igkf,gkfd->igkd", phi_query, state_high, preferred_element_type=jnp.float32
    )
    far_num = far_num + jnp.einsum(
        "igkf,gkfd->igkd", phi_query, state_rest, preferred_element_type=jnp.float32
    )
    far_sum = jnp.einsum("igkf,gkf->igk", phi_query, norm_high, preferred_element_type=jnp.float32)
    far_sum = far_sum + jnp.einsum(
        "igkf,gkf->igk", phi_query, norm_rest, preferred_element_type=jnp.float32
    )
    numerator = local_num + (1.0 - head_factor) * far_num
    denominator = local_den + (1.0 - factor[None]) * far_sum
    outputs = (numerator / denominator[..., None]).astype(jnp.bfloat16)
    result = outputs.reshape(tokens, heads * head_dim)
    return lax.all_to_all(result, "head", split_axis=0, concat_axis=1, tiled=True)


def solution(mesh):
    in_specs = (
        P("seq", "head"),
        P("seq", "head"),
        P("seq", "head"),
        P("seq"),
        P("head", None, None),
        P("head", None, None),
        P("head"),
    )
    out_specs = P(("seq", "head"), None)
    return jax.shard_map(body, mesh=mesh, in_specs=in_specs, out_specs=out_specs, check_vma=False)
```

```python
import math

import jax
import jax.numpy as jnp
from jax import lax
from jax.experimental import pallas as pl
from jax.sharding import PartitionSpec as P

WINDOW = 64
BLOCK = 512
SPAN = 256


def passed_along(value, axis, steps):
    count = lax.axis_size(axis)
    first, last = (max(0, -steps), min(count, count - steps))
    return lax.ppermute(value, axis, [(source, source + steps) for source in range(first, last)])


def angle_tables(positions, half):
    frequency = [500000.0 ** (-float(order) / half) for order in range(half)]
    coarse = jnp.asarray([4096.0 * value % (2.0 * math.pi) for value in frequency], jnp.float32)
    medium = jnp.asarray([64.0 * value % (2.0 * math.pi) for value in frequency], jnp.float32)
    finest = jnp.asarray(frequency, jnp.float32)
    upper = (positions // 4096).astype(jnp.float32)[:, None] * coarse[None, :]
    middle = (positions // 64 % 64).astype(jnp.float32)[:, None] * medium[None, :]
    lower = (positions % 64).astype(jnp.float32)[:, None] * finest[None, :]
    cos_high = jnp.cos(upper) * jnp.cos(middle) - jnp.sin(upper) * jnp.sin(middle)
    sin_high = jnp.sin(upper) * jnp.cos(middle) + jnp.cos(upper) * jnp.sin(middle)
    cosine = cos_high * jnp.cos(lower) - sin_high * jnp.sin(lower)
    sine = sin_high * jnp.cos(lower) + cos_high * jnp.sin(lower)
    return (cosine, sine)


def span_tables(offsets, half):
    frequency = [500000.0 ** (-float(order) / half) for order in range(half)]
    coarse = jnp.asarray([4096.0 * value % (2.0 * math.pi) for value in frequency], jnp.float32)
    medium = jnp.asarray([64.0 * value % (2.0 * math.pi) for value in frequency], jnp.float32)
    finest = jnp.asarray(frequency, jnp.float32)
    quarters = SPAN // 64
    upper = (offsets // 4096).astype(jnp.float32)[:, None] * coarse[None, :]
    middle_index = (offsets[:, None] // 64 + jnp.arange(quarters, dtype=jnp.int32)[None, :]) % 64
    middle = middle_index.astype(jnp.float32)[:, :, None] * medium[None, None, :]
    lower = jnp.arange(64, dtype=jnp.float32)[:, None] * finest[None, :]
    cos_upper = jnp.cos(upper)[:, None, :]
    sin_upper = jnp.sin(upper)[:, None, :]
    cos_high = cos_upper * jnp.cos(middle) - sin_upper * jnp.sin(middle)
    sin_high = sin_upper * jnp.cos(middle) + cos_upper * jnp.sin(middle)
    cos_high = cos_high[:, :, None, :]
    sin_high = sin_high[:, :, None, :]
    cos_lower = jnp.cos(lower)[None, None]
    sin_lower = jnp.sin(lower)[None, None]
    cosine = cos_high * cos_lower - sin_high * sin_lower
    sine = sin_high * cos_lower + cos_high * sin_lower
    return (cosine.reshape(-1, half), sine.reshape(-1, half))


def rotate(rows, cosine, sine):
    half = rows.shape[-1] // 2
    first = rows[..., :half]
    second = rows[..., half:]
    cos_rows = cosine[:, None, :]
    sin_rows = sine[:, None, :]
    return jnp.concatenate(
        [first * cos_rows - second * sin_rows, second * cos_rows + first * sin_rows], axis=-1
    )


def two_softmax(logits):
    return jnp.concatenate(
        [jax.nn.softmax(logits, axis=-1), jax.nn.softmax(-logits, axis=-1)], axis=-1
    )


def split_parts(full_value):
    high_part = full_value.astype(jnp.bfloat16)
    rest_part = (full_value - high_part.astype(jnp.float32)).astype(jnp.bfloat16)
    return (high_part, rest_part)


def key_features(ext_keys2, key_map_t, ext_values2, mask, lag):
    rows, dim = ext_keys2.shape
    heads, feat, _ = key_map_t.shape

    def kernel(k_ref, m_ref, v_ref, mask_ref, phi_ref, st_ref, nm_ref):
        keys = k_ref[...]
        live = mask_ref[...] > 0.0
        values = v_ref[0:lag, :]
        for head in range(heads):
            logits = lax.dot_general(
                m_ref[head], keys, (((1,), (1,)), ((), ())), preferred_element_type=jnp.float32
            )
            for place, sign in enumerate((1.0, -1.0)):
                shifted = sign * logits
                expo = jnp.exp(shifted - jnp.max(shifted, axis=0, keepdims=True))
                soft = expo / jnp.sum(expo, axis=0, keepdims=True)
                phi = jnp.where(live, soft, 0.0).astype(jnp.bfloat16)
                band = slice(place * feat, (place + 1) * feat)
                phi_ref[head, band, :] = phi
                lagged = phi[:, 0:lag]
                st_ref[head, band, :] = jnp.dot(lagged, values, preferred_element_type=jnp.float32)
                nm_ref[head, band, :] = jnp.sum(lagged.astype(jnp.float32), axis=1, keepdims=True)

    return pl.pallas_call(
        kernel,
        grid=(1,),
        in_specs=[
            pl.BlockSpec((rows, dim), lambda h: (0, 0)),
            pl.BlockSpec((heads, feat, dim), lambda h: (0, 0, 0)),
            pl.BlockSpec((rows, dim), lambda h: (0, 0)),
            pl.BlockSpec((1, rows), lambda h: (0, 0)),
        ],
        out_specs=[
            pl.BlockSpec((heads, 2 * feat, rows), lambda h: (0, 0, 0)),
            pl.BlockSpec((heads, 2 * feat, dim), lambda h: (0, 0, 0)),
            pl.BlockSpec((heads, 2 * feat, 1), lambda h: (0, 0, 0)),
        ],
        out_shape=[
            jax.ShapeDtypeStruct((heads, 2 * feat, rows), jnp.bfloat16),
            jax.ShapeDtypeStruct((heads, 2 * feat, dim), jnp.float32),
            jax.ShapeDtypeStruct((heads, 2 * feat, 1), jnp.float32),
        ],
    )(ext_keys2, key_map_t, ext_values2, mask)

def body(queries, keys, values, offsets, query_map, key_map, window_logit):
    tokens = queries.shape[0]
    heads = query_map.shape[0]
    head_dim = query_map.shape[1]
    feat = query_map.shape[2]
    kv_local = keys.shape[1] // head_dim
    group = heads // kv_local
    blocks = tokens // BLOCK
    extent = BLOCK + WINDOW
    cosine, sine = span_tables(offsets, head_dim // 2)
    rot_k = rotate(
        keys.reshape(tokens, kv_local, head_dim).astype(jnp.float32), cosine, sine
    ).astype(jnp.bfloat16)
    value_rows = values.reshape(tokens, kv_local, head_dim)
    tail_keys, tail_values = passed_along(
        (rot_k[tokens - WINDOW :], value_rows[tokens - WINDOW :]), "seq", 1
    )
    ext_keys = jnp.concatenate([tail_keys, rot_k], axis=0)
    ext_values = jnp.concatenate([tail_values, value_rows], axis=0)
    valid = (jnp.arange(tokens + WINDOW) >= WINDOW) | (lax.axis_index("seq") > 0)
    ext_rows = tokens + WINDOW
    phi_heads, state_heads, norm_heads = key_features(
        ext_keys.reshape(ext_rows, head_dim),
        jnp.transpose(key_map, (0, 2, 1)),
        ext_values.reshape(ext_rows, head_dim),
        valid.astype(jnp.float32)[None, :],
        tokens,
    )
    phi_key = phi_heads.reshape(kv_local, group, 2 * feat, ext_rows)
    block_states = state_heads.reshape(1, kv_local, group, 2 * feat, head_dim)
    block_norms = norm_heads.reshape(1, kv_local, group, 2 * feat)
    total_state = jnp.sum(block_states, axis=0)
    total_norm = jnp.sum(block_norms, axis=0)
    before_state = jnp.concatenate(
        [jnp.zeros_like(block_states), jnp.cumsum(block_states, axis=0)[:-1]], axis=0
    )
    before_norm = jnp.concatenate(
        [jnp.zeros_like(block_norms), jnp.cumsum(block_norms, axis=0)[:-1]], axis=0
    )
    state_shape = total_state.shape
    state_size = total_state.size
    packed = jnp.concatenate([total_state.reshape(-1), total_norm.reshape(-1)])
    count = lax.axis_size("seq")
    shifts = []
    steps = 1
    while steps < count:
        shifts.append(steps)
        steps *= 2
    half = len(shifts) // 2 + 1
    orders = (shifts[:half] + shifts[half:][::-1], shifts[half:] + shifts[:half][::-1])
    middle = packed.size // 2
    pieces = []
    for order, piece in zip(orders, (packed[:middle], packed[middle:])):
        inclusive = piece
        exclusive = jnp.zeros_like(piece)
        for place, shift in enumerate(order):
            received = passed_along(inclusive, "seq", shift)
            if not pieces and place == 0:
                first_received = received
            exclusive = exclusive + received
            if place + 1 < len(order):
                inclusive = inclusive + received
        pieces.append(exclusive)
    exclusive = jnp.concatenate(pieces)
    queries, first_received = lax.optimization_barrier((queries, first_received))
    rot_q = rotate(
        queries.reshape(tokens, heads, head_dim).astype(jnp.float32), cosine, sine
    ).astype(jnp.bfloat16)
    query_logits = jnp.einsum("nhd,hdf->nhf", rot_q, query_map, preferred_element_type=jnp.float32)
    phi_query = (
        two_softmax(query_logits).astype(jnp.bfloat16).reshape(tokens, kv_local, group, 2 * feat)
    )
    prior_state = exclusive[:state_size].reshape(state_shape)
    prior_norm = exclusive[state_size:].reshape(total_norm.shape)
    factor = jax.nn.sigmoid(window_logit).reshape(kv_local, group)
    rot_grouped = rot_q.reshape(tokens, kv_local, group, head_dim)
    row_index = jnp.arange(BLOCK)[:, None]
    col_index = jnp.arange(extent)[None, :]
    window_mask = (col_index > row_index) & (col_index <= row_index + WINDOW)
    linear_mask = col_index <= row_index
    live = valid[None, :]
    scores = jnp.einsum(
        "igkd,jgd->gkij", rot_grouped, ext_keys, preferred_element_type=jnp.float32
    ) / math.sqrt(head_dim)
    near_window = window_mask & live
    peak = jnp.max(jnp.where(near_window, scores, -jnp.inf), axis=-1, keepdims=True)
    weights = jnp.where(near_window, jnp.exp(scores - peak), 0.0)
    window_sum = jnp.sum(weights, axis=-1)
    affinity = jnp.einsum("igkf,gkfj->gkij", phi_query, phi_key, preferred_element_type=jnp.float32)
    affinity = jnp.where(linear_mask & live, affinity, 0.0)
    near_sum = jnp.sum(affinity, axis=-1)
    window_num = jnp.einsum(
        "gkij,jgd->igkd",
        weights.astype(jnp.bfloat16),
        ext_values,
        preferred_element_type=jnp.float32,
    )
    near_num = jnp.einsum(
        "gkij,jgd->igkd",
        affinity.astype(jnp.bfloat16),
        ext_values,
        preferred_element_type=jnp.float32,
    )
    head_factor = factor[None, :, :, None]
    local_num = head_factor * window_num + (1.0 - head_factor) * near_num
    local_den = factor[None] * jnp.transpose(window_sum, (2, 0, 1)) + (1.0 - factor[None]) * (
        jnp.transpose(near_sum, (2, 0, 1))
    )
    local_num, local_den = lax.optimization_barrier((local_num, local_den))
    state_now = prior_state + before_state[0]
    norm_now = prior_norm + before_norm[0]
    state_high, state_rest = split_parts(state_now)
    norm_high, norm_rest = split_parts(norm_now)
    far_num = jnp.einsum(
        "igkf,gkfd->igkd", phi_query, state_high, preferred_element_type=jnp.float32
    )
    far_num = far_num + jnp.einsum(
        "igkf,gkfd->igkd", phi_query, state_rest, preferred_element_type=jnp.float32
    )
    far_sum = jnp.einsum("igkf,gkf->igk", phi_query, norm_high, preferred_element_type=jnp.float32)
    far_sum = far_sum + jnp.einsum(
        "igkf,gkf->igk", phi_query, norm_rest, preferred_element_type=jnp.float32
    )
    numerator = local_num + (1.0 - head_factor) * far_num
    denominator = local_den + (1.0 - factor[None]) * far_sum
    outputs = (numerator / denominator[..., None]).astype(jnp.bfloat16)
    result = outputs.reshape(tokens, heads * head_dim)
    return lax.all_to_all(result, "head", split_axis=0, concat_axis=1, tiled=True)


def solution(mesh):
    in_specs = (
        P("seq", "head"),
        P("seq", "head"),
        P("seq", "head"),
        P("seq"),
        P("head", None, None),
        P("head", None, None),
        P("head"),
    )
    out_specs = P(("seq", "head"), None)
    return jax.shard_map(body, mesh=mesh, in_specs=in_specs, out_specs=out_specs, check_vma=False)
```

```python
import math

import jax
import jax.numpy as jnp
from jax import lax
from jax.experimental import pallas as pl
from jax.sharding import PartitionSpec as P

WINDOW = 64
BLOCK = 512
SPAN = 256


def passed_along(value, axis, steps):
    count = lax.axis_size(axis)
    first, last = (max(0, -steps), min(count, count - steps))
    return lax.ppermute(value, axis, [(source, source + steps) for source in range(first, last)])


def angle_tables(positions, half):
    frequency = [500000.0 ** (-float(order) / half) for order in range(half)]
    coarse = jnp.asarray([4096.0 * value % (2.0 * math.pi) for value in frequency], jnp.float32)
    medium = jnp.asarray([64.0 * value % (2.0 * math.pi) for value in frequency], jnp.float32)
    finest = jnp.asarray(frequency, jnp.float32)
    upper = (positions // 4096).astype(jnp.float32)[:, None] * coarse[None, :]
    middle = (positions // 64 % 64).astype(jnp.float32)[:, None] * medium[None, :]
    lower = (positions % 64).astype(jnp.float32)[:, None] * finest[None, :]
    cos_high = jnp.cos(upper) * jnp.cos(middle) - jnp.sin(upper) * jnp.sin(middle)
    sin_high = jnp.sin(upper) * jnp.cos(middle) + jnp.cos(upper) * jnp.sin(middle)
    cosine = cos_high * jnp.cos(lower) - sin_high * jnp.sin(lower)
    sine = sin_high * jnp.cos(lower) + cos_high * jnp.sin(lower)
    return (cosine, sine)


def span_tables(offsets, half):
    frequency = [500000.0 ** (-float(order) / half) for order in range(half)]
    coarse = jnp.asarray([4096.0 * value % (2.0 * math.pi) for value in frequency], jnp.float32)
    medium = jnp.asarray([64.0 * value % (2.0 * math.pi) for value in frequency], jnp.float32)
    finest = jnp.asarray(frequency, jnp.float32)
    quarters = SPAN // 64
    upper = (offsets // 4096).astype(jnp.float32)[:, None] * coarse[None, :]
    middle_index = (offsets[:, None] // 64 + jnp.arange(quarters, dtype=jnp.int32)[None, :]) % 64
    middle = middle_index.astype(jnp.float32)[:, :, None] * medium[None, None, :]
    lower = jnp.arange(64, dtype=jnp.float32)[:, None] * finest[None, :]
    cos_upper = jnp.cos(upper)[:, None, :]
    sin_upper = jnp.sin(upper)[:, None, :]
    cos_high = cos_upper * jnp.cos(middle) - sin_upper * jnp.sin(middle)
    sin_high = sin_upper * jnp.cos(middle) + cos_upper * jnp.sin(middle)
    cos_high = cos_high[:, :, None, :]
    sin_high = sin_high[:, :, None, :]
    cos_lower = jnp.cos(lower)[None, None]
    sin_lower = jnp.sin(lower)[None, None]
    cosine = cos_high * cos_lower - sin_high * sin_lower
    sine = sin_high * cos_lower + cos_high * sin_lower
    return (cosine.reshape(-1, half), sine.reshape(-1, half))


def rotate(rows, cosine, sine):
    half = rows.shape[-1] // 2
    first = rows[..., :half]
    second = rows[..., half:]
    cos_rows = cosine[:, None, :]
    sin_rows = sine[:, None, :]
    return jnp.concatenate(
        [first * cos_rows - second * sin_rows, second * cos_rows + first * sin_rows], axis=-1
    )


def two_softmax(logits):
    return jnp.concatenate(
        [jax.nn.softmax(logits, axis=-1), jax.nn.softmax(-logits, axis=-1)], axis=-1
    )


def split_parts(full_value):
    high_part = full_value.astype(jnp.bfloat16)
    rest_part = (full_value - high_part.astype(jnp.float32)).astype(jnp.bfloat16)
    return (high_part, rest_part)


def key_features(ext_keys2, key_map_t, ext_values2, mask, lag):
    rows, dim = ext_keys2.shape
    heads, feat, _ = key_map_t.shape

    def kernel(k_ref, m_ref, v_ref, mask_ref, phi_ref, st_ref, nm_ref):
        keys = k_ref[...]
        live = mask_ref[...] > 0.0
        values = v_ref[0:lag, :]
        for head in range(heads):
            logits = lax.dot_general(
                m_ref[head], keys, (((1,), (1,)), ((), ())), preferred_element_type=jnp.float32
            )
            for place, sign in enumerate((1.0, -1.0)):
                shifted = sign * logits
                expo = jnp.exp(shifted - jnp.max(shifted, axis=0, keepdims=True))
                soft = expo / jnp.sum(expo, axis=0, keepdims=True)
                phi = jnp.where(live, soft, 0.0).astype(jnp.bfloat16)
                band = slice(place * feat, (place + 1) * feat)
                phi_ref[head, band, :] = phi
                lagged = phi[:, 0:lag]
                st_ref[head, band, :] = jnp.dot(lagged, values, preferred_element_type=jnp.float32)
                nm_ref[head, band, :] = jnp.sum(lagged.astype(jnp.float32), axis=1, keepdims=True)

    return pl.pallas_call(
        kernel,
        grid=(1,),
        in_specs=[
            pl.BlockSpec((rows, dim), lambda h: (0, 0)),
            pl.BlockSpec((heads, feat, dim), lambda h: (0, 0, 0)),
            pl.BlockSpec((rows, dim), lambda h: (0, 0)),
            pl.BlockSpec((1, rows), lambda h: (0, 0)),
        ],
        out_specs=[
            pl.BlockSpec((heads, 2 * feat, rows), lambda h: (0, 0, 0)),
            pl.BlockSpec((heads, 2 * feat, dim), lambda h: (0, 0, 0)),
            pl.BlockSpec((heads, 2 * feat, 1), lambda h: (0, 0, 0)),
        ],
        out_shape=[
            jax.ShapeDtypeStruct((heads, 2 * feat, rows), jnp.bfloat16),
            jax.ShapeDtypeStruct((heads, 2 * feat, dim), jnp.float32),
            jax.ShapeDtypeStruct((heads, 2 * feat, 1), jnp.float32),
        ],
    )(ext_keys2, key_map_t, ext_values2, mask)

def body(queries, keys, values, offsets, query_map, key_map, window_logit):
    tokens = queries.shape[0]
    heads = query_map.shape[0]
    head_dim = query_map.shape[1]
    feat = query_map.shape[2]
    kv_local = keys.shape[1] // head_dim
    group = heads // kv_local
    blocks = tokens // BLOCK
    extent = BLOCK + WINDOW
    cosine, sine = span_tables(offsets, head_dim // 2)
    rot_k = rotate(
        keys.reshape(tokens, kv_local, head_dim).astype(jnp.float32), cosine, sine
    ).astype(jnp.bfloat16)
    value_rows = values.reshape(tokens, kv_local, head_dim)
    tail_keys, tail_values = passed_along(
        (rot_k[tokens - WINDOW :], value_rows[tokens - WINDOW :]), "seq", 1
    )
    ext_keys = jnp.concatenate([tail_keys, rot_k], axis=0)
    ext_values = jnp.concatenate([tail_values, value_rows], axis=0)
    valid = (jnp.arange(tokens + WINDOW) >= WINDOW) | (lax.axis_index("seq") > 0)
    ext_rows = tokens + WINDOW
    phi_heads, state_heads, norm_heads = key_features(
        ext_keys.reshape(ext_rows, head_dim),
        jnp.transpose(key_map, (0, 2, 1)),
        ext_values.reshape(ext_rows, head_dim),
        valid.astype(jnp.float32)[None, :],
        tokens,
    )
    phi_key = phi_heads.reshape(kv_local, group, 2 * feat, ext_rows)
    block_states = state_heads.reshape(1, kv_local, group, 2 * feat, head_dim)
    block_norms = norm_heads.reshape(1, kv_local, group, 2 * feat)
    total_state = jnp.sum(block_states, axis=0)
    total_norm = jnp.sum(block_norms, axis=0)
    before_state = jnp.concatenate(
        [jnp.zeros_like(block_states), jnp.cumsum(block_states, axis=0)[:-1]], axis=0
    )
    before_norm = jnp.concatenate(
        [jnp.zeros_like(block_norms), jnp.cumsum(block_norms, axis=0)[:-1]], axis=0
    )
    state_shape = total_state.shape
    state_size = total_state.size
    packed = jnp.concatenate([total_state.reshape(-1), total_norm.reshape(-1)])
    count = lax.axis_size("seq")
    shifts = []
    steps = 1
    while steps < count:
        shifts.append(steps)
        steps *= 2
    half = len(shifts) // 2 + 1
    orders = (shifts, shifts[::-1])
    middle = packed.size // 2
    pieces = []
    for order, piece in zip(orders, (packed[:middle], packed[middle:])):
        inclusive = piece
        exclusive = jnp.zeros_like(piece)
        for place, shift in enumerate(order):
            received = passed_along(inclusive, "seq", shift)
            if not pieces and place == 0:
                first_received = received
            exclusive = exclusive + received
            if place + 1 < len(order):
                inclusive = inclusive + received
        pieces.append(exclusive)
    exclusive = jnp.concatenate(pieces)
    queries, first_received = lax.optimization_barrier((queries, first_received))
    rot_q = rotate(
        queries.reshape(tokens, heads, head_dim).astype(jnp.float32), cosine, sine
    ).astype(jnp.bfloat16)
    query_logits = jnp.einsum("nhd,hdf->nhf", rot_q, query_map, preferred_element_type=jnp.float32)
    phi_query = (
        two_softmax(query_logits).astype(jnp.bfloat16).reshape(tokens, kv_local, group, 2 * feat)
    )
    prior_state = exclusive[:state_size].reshape(state_shape)
    prior_norm = exclusive[state_size:].reshape(total_norm.shape)
    factor = jax.nn.sigmoid(window_logit).reshape(kv_local, group)
    rot_grouped = rot_q.reshape(tokens, kv_local, group, head_dim)
    row_index = jnp.arange(BLOCK)[:, None]
    col_index = jnp.arange(extent)[None, :]
    window_mask = (col_index > row_index) & (col_index <= row_index + WINDOW)
    linear_mask = col_index <= row_index
    live = valid[None, :]
    scores = jnp.einsum(
        "igkd,jgd->gkij", rot_grouped, ext_keys, preferred_element_type=jnp.float32
    ) / math.sqrt(head_dim)
    near_window = window_mask & live
    peak = jnp.max(jnp.where(near_window, scores, -jnp.inf), axis=-1, keepdims=True)
    weights = jnp.where(near_window, jnp.exp(scores - peak), 0.0)
    window_sum = jnp.sum(weights, axis=-1)
    affinity = jnp.einsum("igkf,gkfj->gkij", phi_query, phi_key, preferred_element_type=jnp.float32)
    affinity = jnp.where(linear_mask & live, affinity, 0.0)
    near_sum = jnp.sum(affinity, axis=-1)
    window_num = jnp.einsum(
        "gkij,jgd->igkd",
        weights.astype(jnp.bfloat16),
        ext_values,
        preferred_element_type=jnp.float32,
    )
    near_num = jnp.einsum(
        "gkij,jgd->igkd",
        affinity.astype(jnp.bfloat16),
        ext_values,
        preferred_element_type=jnp.float32,
    )
    head_factor = factor[None, :, :, None]
    local_num = head_factor * window_num + (1.0 - head_factor) * near_num
    local_den = factor[None] * jnp.transpose(window_sum, (2, 0, 1)) + (1.0 - factor[None]) * (
        jnp.transpose(near_sum, (2, 0, 1))
    )
    local_num, local_den = lax.optimization_barrier((local_num, local_den))
    state_now = prior_state + before_state[0]
    norm_now = prior_norm + before_norm[0]
    state_high, state_rest = split_parts(state_now)
    norm_high, norm_rest = split_parts(norm_now)
    far_num = jnp.einsum(
        "igkf,gkfd->igkd", phi_query, state_high, preferred_element_type=jnp.float32
    )
    far_num = far_num + jnp.einsum(
        "igkf,gkfd->igkd", phi_query, state_rest, preferred_element_type=jnp.float32
    )
    far_sum = jnp.einsum("igkf,gkf->igk", phi_query, norm_high, preferred_element_type=jnp.float32)
    far_sum = far_sum + jnp.einsum(
        "igkf,gkf->igk", phi_query, norm_rest, preferred_element_type=jnp.float32
    )
    numerator = local_num + (1.0 - head_factor) * far_num
    denominator = local_den + (1.0 - factor[None]) * far_sum
    outputs = (numerator / denominator[..., None]).astype(jnp.bfloat16)
    result = outputs.reshape(tokens, heads * head_dim)
    return lax.all_to_all(result, "head", split_axis=0, concat_axis=1, tiled=True)


def solution(mesh):
    in_specs = (
        P("seq", "head"),
        P("seq", "head"),
        P("seq", "head"),
        P("seq"),
        P("head", None, None),
        P("head", None, None),
        P("head"),
    )
    out_specs = P(("seq", "head"), None)
    return jax.shard_map(body, mesh=mesh, in_specs=in_specs, out_specs=out_specs, check_vma=False)
```
